512 devices in a mesh: seq: 64 (over z, y), tp: 4 (over x), dp: 2 (over core).
Axes of the slice: x: 4, y: 4, z: 16, core: 2. Of those that a mesh axis runs over, the one named last changes fastest.
Arguments:
- inputs: bfloat16 [16384, 1280], P(('dp', 'seq'), 'tp'), parts along dimension 0, may hold values from -6 to 6
- out_grads: bfloat16 [16384, 1280], P(('dp', 'seq'), 'tp'), parts along dimension 0, may hold values from -6 to 6
- norm_gain: float32 [1280], replicated, may hold values from 0.1 to 1.9
- w_query: bfloat16 [640, 1280], P('tp'), may hold values from -0.15625 to 0.15625
- w_key: bfloat16 [640, 1280], P('tp'), may hold values from -0.15625 to 0.15625
- w_value: bfloat16 [640, 1280], P('tp'), may hold values from -0.15625 to 0.15625
- w_output: bfloat16 [640, 1280], P('tp'), may hold values from -0.25 to 0.25
- query_scale: float32 [80], replicated, may hold values from -4 to 4
- offsets: int32 [64], replicated, may hold values from 0 to 63, each once
Outputs:
- input_grads: bfloat16 [16384, 1280], P(('dp', 'seq'), 'tp'), parts along dimension 0
The draws below stay inside these ranges and needn't reach their ends.
There are 2 independent parts, one for each index of `dp`. The reference program is written for one: setup_inputs(seed, part) draws one part's arguments, and reference() takes and returns one part's arrays. A program takes and returns all parts, laid end to end along the dimension named above; an argument that names none is the same for every part. Nothing has to cross between parts.
Inputs may be any that keep to these rules, and one draw needn't show every extreme that they name: `offsets`: each number appears exactly once.
All inputs are finite; a program needn't handle non-finite values.
Results may differ from the reference program's by a relative error of at most 0.007.
The reference program's roundings to bfloat16 on the way (of `normed`, `head_grads`, `query_grad` and `score_grad`) count: a program that leaves them out, or rounds other values in their place, can miss the bound.
Values may be sent and summed in bfloat16 or wider, within the bound.
No kernel may reach another device: no remote copies, remote signals or barrier semaphores. Data moves between devices by JAX's collectives and lax.ppermute only.
A program may use at most 64 MiB of HBM per device.

```python
import math
import jax
import jax.numpy as jnp
from jax import lax

D = 1280
HEADS = 8
HEAD = 80
PIECE = 128
LENGTH = 8192
SHARDS = 64


def draw_query_scale(key, part):
    return jnp.clip(jax.random.normal(key, (HEAD,), jnp.float32), -4.0, 4.0)


def shard_levels(rng, dims, pieces, low, high):
    def one(position, parts):
        steps = jax.random.uniform(jax.random.fold_in(jax.random.fold_in(rng, 6), position), (parts,), jnp.float32, low / len(pieces), high / len(pieces))
        return jnp.repeat(jnp.exp(steps), dims[position] // parts).reshape((-1,) + (1,) * (len(dims) - position - 1))

    factor_of = one(*pieces[0])
    for cut in pieces[1:]:
        factor_of = factor_of * one(*cut)
    return factor_of


def scatter_about(own_key, extent, scale, bound, pieces=(), kind=jnp.bfloat16):
    gain = shard_levels(own_key, extent, pieces, -0.22, 0.18) if pieces else 1.0
    array = jax.random.normal(own_key, extent, jnp.float32) * scale * gain
    return jnp.minimum(jnp.maximum(array, -bound), bound).astype(kind)


def setup_inputs(seed: int = 0, part: int = 0) -> dict:
    seeds = jax.random.split(jax.random.key(seed), 10)
    part_keys = jax.random.split(jax.random.fold_in(seeds[9], part), 10)
    inputs = scatter_about(part_keys[0], (LENGTH, D), 1.0, 6.0, ((0, 64), (1, 4)))
    out_grads = scatter_about(part_keys[1], (LENGTH, D), 1.0, 6.0, ((0, 64), (1, 4)))
    norm_gain = jnp.clip(1.0 + 0.18 * jax.random.normal(seeds[2], (D,), jnp.float32), 0.1, 1.9)
    w_query = scatter_about(seeds[3], (HEADS * HEAD, D), D ** -0.5, 0.15625, ((0, 4),))
    w_key = scatter_about(seeds[4], (HEADS * HEAD, D), D ** -0.5, 0.15625, ((0, 4),))
    w_value = scatter_about(seeds[5], (HEADS * HEAD, D), D ** -0.5, 0.15625, ((0, 4),))
    w_output = scatter_about(seeds[6], (HEADS * HEAD, D), (HEADS * HEAD) ** -0.5, 0.25, ((0, 4),))
    query_scale = draw_query_scale(jax.random.fold_in(seeds[9], 71), part)
    offsets = jax.random.permutation(seeds[8], SHARDS).astype(jnp.int32)
    return {"inputs": inputs, "out_grads": out_grads, "norm_gain": norm_gain, "w_query": w_query, "w_key": w_key, "w_value": w_value, "w_output": w_output, "query_scale": query_scale, "offsets": offsets}


scale_base = 1.4426950408889634
masked_score = -1e+30
norm_eps = 1e-06

def positions_of(offsets, first_row, piece_rows, block_len):
    row_index = first_row + lax.iota(jnp.int32, piece_rows)
    shard_ids = row_index // block_len
    one_hot = (shard_ids[:, None] == lax.iota(jnp.int32, offsets.shape[0])[None, :]).astype(jnp.int32)
    return lax.optimization_barrier(jnp.sum(one_hot * offsets.astype(jnp.int32)[None, :], axis=1)) * block_len + row_index % block_len

def column_scale(query_scale, head_count):
    head_width = query_scale.shape[0]
    factor = scale_base / math.sqrt(head_width) * jax.nn.softplus(query_scale.astype(jnp.float32))
    return jnp.tile(factor, head_count)

def split_heads(values, head_count):
    return values.reshape(values.shape[0], head_count, values.shape[1] // head_count)

def rounded(values):
    return lax.optimization_barrier(values.astype(jnp.bfloat16)).astype(jnp.float32)

def reference(inputs, out_grads, norm_gain, w_query, w_key, w_value, w_output, query_scale, offsets):
    all_rows, full_width = inputs.shape
    head_count = HEADS
    contract = (((1,), (1,)), ((), ()))
    widened = inputs.astype(jnp.float32)
    inverse = lax.rsqrt(lax.optimization_barrier(jnp.mean(widened * widened, axis=1, keepdims=True)) + norm_eps)
    gain_full = norm_gain.astype(jnp.float32)
    normed = (widened * inverse * gain_full[None, :]).astype(jnp.bfloat16)
    factor = column_scale(query_scale, head_count)
    queries = (lax.dot_general(normed, w_query, contract, preferred_element_type=jnp.float32) * factor[None, :]).astype(jnp.bfloat16)
    key_rows = lax.dot_general(normed, w_key, contract, preferred_element_type=jnp.float32).astype(jnp.bfloat16)
    values = lax.dot_general(normed, w_value, contract, preferred_element_type=jnp.float32).astype(jnp.bfloat16)
    head_grads = lax.dot_general(out_grads, w_output, contract, preferred_element_type=jnp.float32).astype(jnp.bfloat16)
    positions = positions_of(offsets, 0, all_rows, PIECE)
    block_rows = math.gcd(all_rows, 512)
    block_count = all_rows // block_rows
    query_heads = split_heads(queries.astype(jnp.float32), head_count)
    key_heads = split_heads(key_rows.astype(jnp.float32), head_count)
    value_heads = split_heads(values.astype(jnp.float32), head_count)
    grad_heads = split_heads(head_grads.astype(jnp.float32), head_count)

    def query_block(number):
        first_row = number * block_rows
        query_part = lax.dynamic_slice_in_dim(query_heads, first_row, block_rows, 0)
        grad_part = lax.dynamic_slice_in_dim(grad_heads, first_row, block_rows, 0)
        query_place = lax.dynamic_slice_in_dim(positions, first_row, block_rows, 0)
        raw_scores = jnp.einsum('qhd,khd->hqk', query_part, key_heads)
        visible = positions[None, None, :] <= query_place[None, :, None]
        masked = jnp.where(visible, raw_scores, masked_score)
        row_peak = lax.optimization_barrier(jnp.max(masked, axis=2))
        summed = lax.optimization_barrier(jnp.sum(jnp.where(visible, jnp.exp(masked - row_peak[:, :, None]), 0.0), axis=2))
        log_total = row_peak + jnp.log(summed)
        attend = jnp.exp(jnp.where(visible, raw_scores - log_total[:, :, None], masked_score))
        grad_probs = jnp.einsum('qhd,khd->hqk', grad_part, value_heads)
        weighted = attend * grad_probs
        row_delta = lax.optimization_barrier(jnp.sum(weighted, axis=2))
        first_sum = jnp.einsum('hqk,khd->hqd', rounded(weighted), key_heads)
        second_sum = jnp.einsum('hqk,khd->hqd', rounded(attend), key_heads)
        query_grad = first_sum - row_delta[:, :, None] * second_sum
        return (log_total, row_delta, query_grad)
    log_blocks, delta_blocks, query_blocks = lax.map(query_block, jnp.arange(block_count, dtype=jnp.int32))
    log_total = jnp.transpose(log_blocks, (1, 0, 2)).reshape(head_count, all_rows)
    row_delta = jnp.transpose(delta_blocks, (1, 0, 2)).reshape(head_count, all_rows)
    query_grad = jnp.transpose(query_blocks, (0, 2, 1, 3)).reshape(all_rows, head_count * HEAD)

    def key_block(number):
        first_row = number * block_rows
        key_part = lax.dynamic_slice_in_dim(key_heads, first_row, block_rows, 0)
        value_part = lax.dynamic_slice_in_dim(value_heads, first_row, block_rows, 0)
        key_place = lax.dynamic_slice_in_dim(positions, first_row, block_rows, 0)
        raw_scores = jnp.einsum('qhd,khd->hqk', query_heads, key_part)
        visible = key_place[None, None, :] <= positions[None, :, None]
        attend = jnp.exp(jnp.where(visible, raw_scores - log_total[:, :, None], masked_score))
        grad_probs = jnp.einsum('qhd,khd->hqk', grad_heads, value_part)
        score_grad = rounded(attend * (grad_probs - row_delta[:, :, None]))
        key_grad = jnp.einsum('hqk,qhd->khd', score_grad, query_heads)
        value_grad = jnp.einsum('hqk,qhd->khd', rounded(attend), grad_heads)
        return (key_grad, value_grad)
    key_blocks, value_blocks = lax.map(key_block, jnp.arange(block_count, dtype=jnp.int32))
    key_grad = key_blocks.reshape(all_rows, head_count * HEAD).astype(jnp.bfloat16)
    value_grad = value_blocks.reshape(all_rows, head_count * HEAD).astype(jnp.bfloat16)
    query_done = (query_grad * factor[None, :]).astype(jnp.bfloat16)
    back_sum = jnp.dot(query_done, w_query, preferred_element_type=jnp.float32)
    back_sum = back_sum + jnp.dot(key_grad, w_key, preferred_element_type=jnp.float32)
    back_sum = back_sum + jnp.dot(value_grad, w_value, preferred_element_type=jnp.float32)
    scaled = back_sum * gain_full[None, :]
    row_dot = lax.optimization_barrier(jnp.sum(widened * scaled, axis=1, keepdims=True))
    branch = inverse * scaled - widened * inverse * inverse * inverse * row_dot / full_width
    return (out_grads.astype(jnp.float32) + branch).astype(jnp.bfloat16)
```

```python
import math

import jax
import jax.numpy as jnp
import numpy as np
from jax import lax
from jax.sharding import Mesh
from jax.sharding import PartitionSpec as P

PIECE = 128

scale_base = 1.4426950408889634
masked_score = -1e30
norm_eps = 1e-06


def column_scale(query_scale, head_count):
    head_width = query_scale.shape[0]
    factor = scale_base / math.sqrt(head_width) * jax.nn.softplus(query_scale)
    return jnp.tile(factor, head_count)


def block_positions(offsets, rows):
    return (offsets[:, None] * PIECE + lax.iota(jnp.int32, PIECE)[None, :]).reshape(rows)


def per_device(
    inputs, out_grads, norm_gain, w_query, w_key, w_value, w_output, query_scale, offsets
):
    row_count, width_here = inputs.shape
    head_width = query_scale.shape[0]
    heads_here = w_query.shape[0] // head_width
    cols = heads_here * head_width
    tp_size = lax.axis_size("tp")
    y_size = lax.axis_size("y")
    shards = offsets.shape[0]
    all_rows = shards * row_count
    contract = (((1,), (1,)), ((), ()))

    with jax.named_scope("gather_features"):
        both = jnp.concatenate([inputs, out_grads], axis=1)
        gathered = lax.all_gather(both, "tp", axis=1, tiled=True)
        gathered = gathered.reshape(row_count, tp_size, 2, width_here)
        full_inputs = gathered[:, :, 0, :].reshape(row_count, tp_size * width_here)
        full_grads = gathered[:, :, 1, :].reshape(row_count, tp_size * width_here)
    full_width = full_inputs.shape[1]

    with jax.named_scope("projections"):
        widened = full_inputs.astype(jnp.float32)
        inverse = lax.rsqrt(jnp.mean(widened * widened, axis=1, keepdims=True) + norm_eps)
        normed = (widened * inverse * norm_gain[None, :]).astype(jnp.bfloat16)
        factor = column_scale(query_scale, heads_here)
        queries = (
            lax.dot_general(normed, w_query, contract, preferred_element_type=jnp.float32)
            * factor[None, :]
        ).astype(jnp.bfloat16)
        keys = lax.dot_general(normed, w_key, contract, preferred_element_type=jnp.float32).astype(
            jnp.bfloat16
        )
        values = lax.dot_general(
            normed, w_value, contract, preferred_element_type=jnp.float32
        ).astype(jnp.bfloat16)
        head_grads = lax.dot_general(
            full_grads, w_output, contract, preferred_element_type=jnp.float32
        ).astype(jnp.bfloat16)

    with jax.named_scope("gather_sequence"):
        packed = jnp.concatenate([keys, values, queries, head_grads], axis=1)
        packed = lax.all_gather(packed, "y", axis=0, tiled=True)
        packed = lax.all_gather(packed, "z", axis=0, tiled=True)
        key_all = packed[:, 0 * cols : 1 * cols].reshape(all_rows, heads_here, head_width)
        value_all = packed[:, 1 * cols : 2 * cols].reshape(all_rows, heads_here, head_width)
        query_all = packed[:, 2 * cols : 3 * cols].reshape(all_rows, heads_here, head_width)
        grad_all = packed[:, 3 * cols : 4 * cols].reshape(all_rows, heads_here, head_width)

    seq_index = lax.axis_index("z") * y_size + lax.axis_index("y")
    positions = block_positions(offsets, all_rows)
    own_positions = offsets[seq_index] * PIECE + lax.iota(jnp.int32, row_count)

    query_heads = queries.reshape(row_count, heads_here, head_width)
    grad_heads = head_grads.reshape(row_count, heads_here, head_width)
    key_heads = keys.reshape(row_count, heads_here, head_width)
    value_heads = values.reshape(row_count, heads_here, head_width)

    with jax.named_scope("query_pass"):
        scores = jnp.einsum(
            "qhd,khd->hqk", query_heads, key_all, preferred_element_type=jnp.float32
        )
        visible = positions[None, None, :] <= own_positions[None, :, None]
        masked = jnp.where(visible, scores, masked_score)
        row_peak = jnp.max(masked, axis=2)
        summed = jnp.sum(jnp.where(visible, jnp.exp(masked - row_peak[:, :, None]), 0.0), axis=2)
        log_total = row_peak + jnp.log(summed)
        attend = jnp.exp(jnp.where(visible, scores - log_total[:, :, None], masked_score))
        grad_probs = jnp.einsum(
            "qhd,khd->hqk", grad_heads, value_all, preferred_element_type=jnp.float32
        )
        weighted = attend * grad_probs
        row_delta = jnp.sum(weighted, axis=2)
        first_sum = jnp.einsum(
            "hqk,khd->hqd",
            weighted.astype(jnp.bfloat16),
            key_all,
            preferred_element_type=jnp.float32,
        )
        second_sum = jnp.einsum(
            "hqk,khd->hqd", attend.astype(jnp.bfloat16), key_all, preferred_element_type=jnp.float32
        )
        query_grad = first_sum - row_delta[:, :, None] * second_sum
        query_grad = jnp.transpose(query_grad, (1, 0, 2)).reshape(row_count, cols)
        query_done = (query_grad * factor[None, :]).astype(jnp.bfloat16)

    with jax.named_scope("gather_row_stats"):
        stats = jnp.stack([log_total, row_delta], axis=0)
        sent = jnp.broadcast_to(stats[None], (shards,) + stats.shape)
        stats_all = lax.all_to_all(sent, ("z", "y"), 0, 0, tiled=False)
        log_all = jnp.transpose(stats_all[:, 0], (1, 0, 2)).reshape(heads_here, all_rows)
        delta_all = jnp.transpose(stats_all[:, 1], (1, 0, 2)).reshape(heads_here, all_rows)

    with jax.named_scope("key_pass"):
        scores_t = jnp.einsum(
            "khd,qhd->hkq", key_heads, query_all, preferred_element_type=jnp.float32
        )
        visible_t = own_positions[None, :, None] <= positions[None, None, :]
        attend_t = jnp.exp(
            jnp.where(visible_t, scores_t - log_all[:, None, :], masked_score)
        )
        grad_probs_t = jnp.einsum(
            "khd,qhd->hkq", value_heads, grad_all, preferred_element_type=jnp.float32
        )
        score_grad = (attend_t * (grad_probs_t - delta_all[:, None, :])).astype(jnp.bfloat16)
        key_grad = jnp.einsum(
            "hkq,qhd->khd", score_grad, query_all, preferred_element_type=jnp.float32
        )
        value_grad = jnp.einsum(
            "hkq,qhd->khd", attend_t.astype(jnp.bfloat16), grad_all, preferred_element_type=jnp.float32
        )
        key_done = key_grad.reshape(row_count, cols).astype(jnp.bfloat16)
        value_done = value_grad.reshape(row_count, cols).astype(jnp.bfloat16)

    with jax.named_scope("back_projection"):
        back_sum = jnp.dot(query_done, w_query, preferred_element_type=jnp.float32)
        back_sum = back_sum + jnp.dot(key_done, w_key, preferred_element_type=jnp.float32)
        back_sum = back_sum + jnp.dot(value_done, w_value, preferred_element_type=jnp.float32)
        scaled = back_sum * norm_gain[None, :]
        row_part = jnp.sum(widened * scaled, axis=1)
        chunks = scaled.reshape(row_count, tp_size, width_here).transpose(1, 0, 2)
        extra = jnp.zeros((tp_size, 1, width_here), jnp.float32)
        extra = extra.at[:, 0, :row_count].set(jnp.broadcast_to(row_part, (tp_size, row_count)))
        payload = jnp.concatenate([chunks, extra], axis=1)
        received = lax.all_to_all(payload, "tp", 0, 0, tiled=False)
        total = jnp.sum(received, axis=0)
        scaled_own = total[:row_count]
        row_dot = total[row_count, :row_count][:, None]

    with jax.named_scope("input_grads"):
        start_col = lax.axis_index("tp") * width_here
        own_inputs = inputs.astype(jnp.float32)
        branch = (
            inverse * scaled_own
            - own_inputs * inverse * inverse * inverse * row_dot / full_width
        )
        result = out_grads.astype(jnp.float32) + branch
    return result.astype(jnp.bfloat16)


def solution(mesh):
    seq_size = mesh.shape["seq"]
    devices = mesh.devices
    y_size = 4 if seq_size % 4 == 0 else 1
    split = Mesh(
        devices.reshape((seq_size // y_size, y_size) + devices.shape[1:]),
        ("z", "y", "tp", "dp"),
    )
    rows = P(("dp", "z", "y"), "tp")
    return jax.shard_map(
        per_device,
        mesh=split,
        in_specs=(
            rows,
            rows,
            P(),
            P("tp", None),
            P("tp", None),
            P("tp", None),
            P("tp", None),
            P(),
            P(),
        ),
        out_specs=rows,
        check_vma=False,
    )
```

```python
import math

import jax
import jax.numpy as jnp
import numpy as np
from jax import lax
from jax.sharding import Mesh
from jax.sharding import PartitionSpec as P

PIECE = 128

scale_base = 1.4426950408889634
masked_score = -1e30
norm_eps = 1e-06


def column_scale(query_scale, head_count):
    head_width = query_scale.shape[0]
    factor = scale_base / math.sqrt(head_width) * jax.nn.softplus(query_scale)
    return jnp.tile(factor, head_count)


def block_positions(offsets, rows):
    return (offsets[:, None] * PIECE + lax.iota(jnp.int32, PIECE)[None, :]).reshape(rows)


def ring_steps(size):
    return size // 2, (size - 1) // 2


def two_rings(first, first_axis, first_size, second, second_axis, second_size):
    results = []
    state = []
    for data, axis, size in ((first, first_axis, first_size), (second, second_axis, second_size)):
        forward, backward = ring_steps(size)
        pieces = [None] * size
        pieces[0] = data
        results.append(pieces)
        state.append([data, data, axis, size, forward, backward])
    for step in range(max(max(s[4], s[5]) for s in state)):
        for pieces, entry in zip(results, state):
            ahead, behind, axis, size, forward, backward = entry
            if step < forward:
                ahead = lax.ppermute(ahead, axis, [(i, (i + 1) % size) for i in range(size)])
                pieces[size - 1 - step] = ahead
            if step < backward:
                behind = lax.ppermute(behind, axis, [(i, (i - 1) % size) for i in range(size)])
                pieces[1 + step] = behind
            entry[0], entry[1] = ahead, behind
    return results


def per_device(
    inputs, out_grads, norm_gain, w_query, w_key, w_value, w_output, query_scale, offsets
):
    row_count, width_here = inputs.shape
    head_width = query_scale.shape[0]
    heads_here = w_query.shape[0] // head_width
    cols = heads_here * head_width
    tp_size = lax.axis_size("tp")
    y_size = lax.axis_size("y")
    shards = offsets.shape[0]
    all_rows = shards * row_count
    contract = (((1,), (1,)), ((), ()))

    with jax.named_scope("gather_features"):
        both = jnp.concatenate([inputs, out_grads], axis=1)
        gathered = lax.all_gather(both, "tp", axis=1, tiled=True)
        gathered = gathered.reshape(row_count, tp_size, 2, width_here)
        full_inputs = gathered[:, :, 0, :].reshape(row_count, tp_size * width_here)
        full_grads = gathered[:, :, 1, :].reshape(row_count, tp_size * width_here)
    full_width = full_inputs.shape[1]

    with jax.named_scope("projections"):
        widened = full_inputs.astype(jnp.float32)
        inverse = lax.rsqrt(jnp.mean(widened * widened, axis=1, keepdims=True) + norm_eps)
        normed = (widened * inverse * norm_gain[None, :]).astype(jnp.bfloat16)
        factor = column_scale(query_scale, heads_here)
        queries = (
            lax.dot_general(normed, w_query, contract, preferred_element_type=jnp.float32)
            * factor[None, :]
        ).astype(jnp.bfloat16)
        keys = lax.dot_general(normed, w_key, contract, preferred_element_type=jnp.float32).astype(
            jnp.bfloat16
        )
        values = lax.dot_general(
            normed, w_value, contract, preferred_element_type=jnp.float32
        ).astype(jnp.bfloat16)
        head_grads = lax.dot_general(
            full_grads, w_output, contract, preferred_element_type=jnp.float32
        ).astype(jnp.bfloat16)

    z_size = lax.axis_size("z")
    z_index = lax.axis_index("z")
    y_index = lax.axis_index("y")

    with jax.named_scope("gather_sequence"):
        kv = jnp.concatenate([keys, values], axis=1)
        qg = jnp.concatenate([queries, head_grads], axis=1)
        kv_y, qg_z = two_rings(kv, "y", y_size, qg, "z", z_size)
        kv_y = jnp.concatenate(kv_y, axis=0)
        qg_z = jnp.concatenate(qg_z, axis=0)
        kv_all, qg_all = two_rings(kv_y, "z", z_size, qg_z, "y", y_size)
        kv_all = jnp.concatenate(kv_all, axis=0)
        qg_all = jnp.concatenate(qg_all, axis=0)
        key_all = kv_all[:, :cols].reshape(all_rows, heads_here, head_width)
        value_all = kv_all[:, cols:].reshape(all_rows, heads_here, head_width)
        query_all = qg_all[:, :cols].reshape(all_rows, heads_here, head_width)
        grad_all = qg_all[:, cols:].reshape(all_rows, heads_here, head_width)

    rel_z = lax.iota(jnp.int32, z_size)
    rel_y = lax.iota(jnp.int32, y_size)
    abs_z = (z_index + rel_z) % z_size
    abs_y = (y_index + rel_y) % y_size
    kv_source = (abs_z[:, None] * y_size + abs_y[None, :]).reshape(shards)
    qg_source = (abs_z[None, :] * y_size + abs_y[:, None]).reshape(shards)
    key_positions = block_positions(offsets[kv_source], all_rows)
    query_positions = block_positions(offsets[qg_source], all_rows)
    seq_index = z_index * y_size + y_index
    own_positions = offsets[seq_index] * PIECE + lax.iota(jnp.int32, row_count)

    query_heads = queries.reshape(row_count, heads_here, head_width)
    grad_heads = head_grads.reshape(row_count, heads_here, head_width)
    key_heads = keys.reshape(row_count, heads_here, head_width)
    value_heads = values.reshape(row_count, heads_here, head_width)

    with jax.named_scope("query_pass"):
        scores = jnp.einsum(
            "qhd,khd->hqk", query_heads, key_all, preferred_element_type=jnp.float32
        )
        visible = key_positions[None, None, :] <= own_positions[None, :, None]
        masked = jnp.where(visible, scores, masked_score)
        row_peak = jnp.max(masked, axis=2)
        summed = jnp.sum(jnp.where(visible, jnp.exp(masked - row_peak[:, :, None]), 0.0), axis=2)
        log_total = row_peak + jnp.log(summed)
        attend = jnp.exp(jnp.where(visible, scores - log_total[:, :, None], masked_score))
        grad_probs = jnp.einsum(
            "qhd,khd->hqk", grad_heads, value_all, preferred_element_type=jnp.float32
        )
        weighted = attend * grad_probs
        row_delta = jnp.sum(weighted, axis=2)
        first_sum = jnp.einsum(
            "hqk,khd->hqd",
            weighted.astype(jnp.bfloat16),
            key_all,
            preferred_element_type=jnp.float32,
        )
        second_sum = jnp.einsum(
            "hqk,khd->hqd", attend.astype(jnp.bfloat16), key_all, preferred_element_type=jnp.float32
        )
        query_grad = first_sum - row_delta[:, :, None] * second_sum
        query_grad = jnp.transpose(query_grad, (1, 0, 2)).reshape(row_count, cols)
        query_done = (query_grad * factor[None, :]).astype(jnp.bfloat16)

    with jax.named_scope("gather_row_stats"):
        stats = jnp.stack([log_total, row_delta], axis=0)
        sent = jnp.broadcast_to(stats[None], (shards,) + stats.shape)
        stats_all = lax.all_to_all(sent, ("z", "y"), 0, 0, tiled=False)
        stats_all = stats_all[qg_source]
        log_all = jnp.transpose(stats_all[:, 0], (1, 0, 2)).reshape(heads_here, all_rows)
        delta_all = jnp.transpose(stats_all[:, 1], (1, 0, 2)).reshape(heads_here, all_rows)

    with jax.named_scope("key_pass"):
        scores_t = jnp.einsum(
            "khd,qhd->hkq", key_heads, query_all, preferred_element_type=jnp.float32
        )
        visible_t = own_positions[None, :, None] <= query_positions[None, None, :]
        attend_t = jnp.exp(
            jnp.where(visible_t, scores_t - log_all[:, None, :], masked_score)
        )
        grad_probs_t = jnp.einsum(
            "khd,qhd->hkq", value_heads, grad_all, preferred_element_type=jnp.float32
        )
        score_grad = (attend_t * (grad_probs_t - delta_all[:, None, :])).astype(jnp.bfloat16)
        key_grad = jnp.einsum(
            "hkq,qhd->khd", score_grad, query_all, preferred_element_type=jnp.float32
        )
        value_grad = jnp.einsum(
            "hkq,qhd->khd", attend_t.astype(jnp.bfloat16), grad_all, preferred_element_type=jnp.float32
        )
        key_done = key_grad.reshape(row_count, cols).astype(jnp.bfloat16)
        value_done = value_grad.reshape(row_count, cols).astype(jnp.bfloat16)

    with jax.named_scope("back_projection"):
        back_sum = jnp.dot(query_done, w_query, preferred_element_type=jnp.float32)
        back_sum = back_sum + jnp.dot(key_done, w_key, preferred_element_type=jnp.float32)
        back_sum = back_sum + jnp.dot(value_done, w_value, preferred_element_type=jnp.float32)
        scaled = back_sum * norm_gain[None, :]
        row_part = jnp.sum(widened * scaled, axis=1)
        chunks = scaled.reshape(row_count, tp_size, width_here).transpose(1, 0, 2)
        extra = jnp.zeros((tp_size, 1, width_here), jnp.float32)
        extra = extra.at[:, 0, :row_count].set(jnp.broadcast_to(row_part, (tp_size, row_count)))
        payload = jnp.concatenate([chunks, extra], axis=1)
        received = lax.all_to_all(payload, "tp", 0, 0, tiled=False)
        total = jnp.sum(received, axis=0)
        scaled_own = total[:row_count]
        row_dot = total[row_count, :row_count][:, None]

    with jax.named_scope("input_grads"):
        start_col = lax.axis_index("tp") * width_here
        own_inputs = inputs.astype(jnp.float32)
        branch = (
            inverse * scaled_own
            - own_inputs * inverse * inverse * inverse * row_dot / full_width
        )
        result = out_grads.astype(jnp.float32) + branch
    return result.astype(jnp.bfloat16)


def solution(mesh):
    seq_size = mesh.shape["seq"]
    devices = mesh.devices
    y_size = 4 if seq_size % 4 == 0 else 1
    split = Mesh(
        devices.reshape((seq_size // y_size, y_size) + devices.shape[1:]),
        ("z", "y", "tp", "dp"),
    )
    rows = P(("dp", "z", "y"), "tp")
    return jax.shard_map(
        per_device,
        mesh=split,
        in_specs=(
            rows,
            rows,
            P(),
            P("tp", None),
            P("tp", None),
            P("tp", None),
            P("tp", None),
            P(),
            P(),
        ),
        out_specs=rows,
        check_vma=False,
    )
```

```python
import math

import jax
import jax.numpy as jnp
import numpy as np
from jax import lax
from jax.sharding import Mesh
from jax.sharding import PartitionSpec as P

PIECE = 128

scale_base = 1.4426950408889634
masked_score = -1e30
norm_eps = 1e-06


def column_scale(query_scale, head_count):
    head_width = query_scale.shape[0]
    factor = scale_base / math.sqrt(head_width) * jax.nn.softplus(query_scale)
    return jnp.tile(factor, head_count)


def block_positions(offsets, rows):
    return (offsets[:, None] * PIECE + lax.iota(jnp.int32, PIECE)[None, :]).reshape(rows)


def ring_steps(size):
    return size // 2, (size - 1) // 2


def ring_gather(data, axis, size):
    forward, backward = ring_steps(size)
    pieces = [None] * size
    pieces[0] = data
    ahead = behind = data
    for step in range(max(forward, backward)):
        if step < forward:
            ahead = lax.ppermute(ahead, axis, [(i, (i + 1) % size) for i in range(size)])
            pieces[size - 1 - step] = ahead
        if step < backward:
            behind = lax.ppermute(behind, axis, [(i, (i - 1) % size) for i in range(size)])
            pieces[1 + step] = behind
    return pieces


def per_device(
    inputs, out_grads, norm_gain, w_query, w_key, w_value, w_output, query_scale, offsets
):
    row_count, width_here = inputs.shape
    head_width = query_scale.shape[0]
    heads_here = w_query.shape[0] // head_width
    cols = heads_here * head_width
    tp_size = lax.axis_size("tp")
    y_size = lax.axis_size("y")
    shards = offsets.shape[0]
    all_rows = shards * row_count
    contract = (((1,), (1,)), ((), ()))

    with jax.named_scope("gather_features"):
        both = jnp.concatenate([inputs, out_grads], axis=1)
        gathered = lax.all_gather(both, "tp", axis=1, tiled=True)
        gathered = gathered.reshape(row_count, tp_size, 2, width_here)
        full_inputs = gathered[:, :, 0, :].reshape(row_count, tp_size * width_here)
        full_grads = gathered[:, :, 1, :].reshape(row_count, tp_size * width_here)
    full_width = full_inputs.shape[1]

    with jax.named_scope("projections"):
        widened = full_inputs.astype(jnp.float32)
        inverse = lax.rsqrt(jnp.mean(widened * widened, axis=1, keepdims=True) + norm_eps)
        normed = (widened * inverse * norm_gain[None, :]).astype(jnp.bfloat16)
        factor = column_scale(query_scale, heads_here)
        queries = (
            lax.dot_general(normed, w_query, contract, preferred_element_type=jnp.float32)
            * factor[None, :]
        ).astype(jnp.bfloat16)
        keys = lax.dot_general(normed, w_key, contract, preferred_element_type=jnp.float32).astype(
            jnp.bfloat16
        )
        values = lax.dot_general(
            normed, w_value, contract, preferred_element_type=jnp.float32
        ).astype(jnp.bfloat16)
        head_grads = lax.dot_general(
            full_grads, w_output, contract, preferred_element_type=jnp.float32
        ).astype(jnp.bfloat16)

    z_size = lax.axis_size("z")
    z_index = lax.axis_index("z")
    y_index = lax.axis_index("y")

    with jax.named_scope("gather_sequence"):
        kv = jnp.concatenate([keys, values], axis=1)
        qg = jnp.concatenate([queries, head_grads], axis=1)
        kv_all = lax.all_gather(kv, "y", axis=0, tiled=True)
        kv_all = lax.all_gather(kv_all, "z", axis=0, tiled=True)
        qg_z = jnp.concatenate(ring_gather(qg, "z", z_size), axis=0)
        qg_all = jnp.concatenate(ring_gather(qg_z, "y", y_size), axis=0)
        key_all = kv_all[:, :cols].reshape(all_rows, heads_here, head_width)
        value_all = kv_all[:, cols:].reshape(all_rows, heads_here, head_width)
        query_all = qg_all[:, :cols].reshape(all_rows, heads_here, head_width)
        grad_all = qg_all[:, cols:].reshape(all_rows, heads_here, head_width)

    rel_z = lax.iota(jnp.int32, z_size)
    rel_y = lax.iota(jnp.int32, y_size)
    abs_z = (z_index + rel_z) % z_size
    abs_y = (y_index + rel_y) % y_size
    qg_source = (abs_z[None, :] * y_size + abs_y[:, None]).reshape(shards)
    key_positions = block_positions(offsets, all_rows)
    query_positions = block_positions(offsets[qg_source], all_rows)
    seq_index = z_index * y_size + y_index
    own_positions = offsets[seq_index] * PIECE + lax.iota(jnp.int32, row_count)

    query_heads = queries.reshape(row_count, heads_here, head_width)
    grad_heads = head_grads.reshape(row_count, heads_here, head_width)
    key_heads = keys.reshape(row_count, heads_here, head_width)
    value_heads = values.reshape(row_count, heads_here, head_width)

    with jax.named_scope("query_pass"):
        scores = jnp.einsum(
            "qhd,khd->hqk", query_heads, key_all, preferred_element_type=jnp.float32
        )
        visible = key_positions[None, None, :] <= own_positions[None, :, None]
        masked = jnp.where(visible, scores, masked_score)
        row_peak = jnp.max(masked, axis=2)
        summed = jnp.sum(jnp.where(visible, jnp.exp(masked - row_peak[:, :, None]), 0.0), axis=2)
        log_total = row_peak + jnp.log(summed)
        attend = jnp.exp(jnp.where(visible, scores - log_total[:, :, None], masked_score))
        grad_probs = jnp.einsum(
            "qhd,khd->hqk", grad_heads, value_all, preferred_element_type=jnp.float32
        )
        weighted = attend * grad_probs
        row_delta = jnp.sum(weighted, axis=2)
        first_sum = jnp.einsum(
            "hqk,khd->hqd",
            weighted.astype(jnp.bfloat16),
            key_all,
            preferred_element_type=jnp.float32,
        )
        second_sum = jnp.einsum(
            "hqk,khd->hqd", attend.astype(jnp.bfloat16), key_all, preferred_element_type=jnp.float32
        )
        query_grad = first_sum - row_delta[:, :, None] * second_sum
        query_grad = jnp.transpose(query_grad, (1, 0, 2)).reshape(row_count, cols)
        query_done = (query_grad * factor[None, :]).astype(jnp.bfloat16)

    with jax.named_scope("gather_row_stats"):
        stats = jnp.stack([log_total, row_delta], axis=0)
        sent = jnp.broadcast_to(stats[None], (shards,) + stats.shape)
        stats_all = lax.all_to_all(sent, ("z", "y"), 0, 0, tiled=False)
        stats_all = stats_all[qg_source]
        log_all = jnp.transpose(stats_all[:, 0], (1, 0, 2)).reshape(heads_here, all_rows)
        delta_all = jnp.transpose(stats_all[:, 1], (1, 0, 2)).reshape(heads_here, all_rows)

    with jax.named_scope("key_pass"):
        scores_t = jnp.einsum(
            "khd,qhd->hkq", key_heads, query_all, preferred_element_type=jnp.float32
        )
        visible_t = own_positions[None, :, None] <= query_positions[None, None, :]
        attend_t = jnp.exp(
            jnp.where(visible_t, scores_t - log_all[:, None, :], masked_score)
        )
        grad_probs_t = jnp.einsum(
            "khd,qhd->hkq", value_heads, grad_all, preferred_element_type=jnp.float32
        )
        score_grad = (attend_t * (grad_probs_t - delta_all[:, None, :])).astype(jnp.bfloat16)
        key_grad = jnp.einsum(
            "hkq,qhd->khd", score_grad, query_all, preferred_element_type=jnp.float32
        )
        value_grad = jnp.einsum(
            "hkq,qhd->khd", attend_t.astype(jnp.bfloat16), grad_all, preferred_element_type=jnp.float32
        )
        key_done = key_grad.reshape(row_count, cols).astype(jnp.bfloat16)
        value_done = value_grad.reshape(row_count, cols).astype(jnp.bfloat16)

    with jax.named_scope("back_projection"):
        back_sum = jnp.dot(query_done, w_query, preferred_element_type=jnp.float32)
        back_sum = back_sum + jnp.dot(key_done, w_key, preferred_element_type=jnp.float32)
        back_sum = back_sum + jnp.dot(value_done, w_value, preferred_element_type=jnp.float32)
        scaled = back_sum * norm_gain[None, :]
        row_part = jnp.sum(widened * scaled, axis=1)
        chunks = scaled.reshape(row_count, tp_size, width_here).transpose(1, 0, 2)
        extra = jnp.zeros((tp_size, 1, width_here), jnp.float32)
        extra = extra.at[:, 0, :row_count].set(jnp.broadcast_to(row_part, (tp_size, row_count)))
        payload = jnp.concatenate([chunks, extra], axis=1)
        received = lax.all_to_all(payload, "tp", 0, 0, tiled=False)
        total = jnp.sum(received, axis=0)
        scaled_own = total[:row_count]
        row_dot = total[row_count, :row_count][:, None]

    with jax.named_scope("input_grads"):
        start_col = lax.axis_index("tp") * width_here
        own_inputs = inputs.astype(jnp.float32)
        branch = (
            inverse * scaled_own
            - own_inputs * inverse * inverse * inverse * row_dot / full_width
        )
        result = out_grads.astype(jnp.float32) + branch
    return result.astype(jnp.bfloat16)


def solution(mesh):
    seq_size = mesh.shape["seq"]
    devices = mesh.devices
    y_size = 4 if seq_size % 4 == 0 else 1
    split = Mesh(
        devices.reshape((seq_size // y_size, y_size) + devices.shape[1:]),
        ("z", "y", "tp", "dp"),
    )
    rows = P(("dp", "z", "y"), "tp")
    return jax.shard_map(
        per_device,
        mesh=split,
        in_specs=(
            rows,
            rows,
            P(),
            P("tp", None),
            P("tp", None),
            P("tp", None),
            P("tp", None),
            P(),
            P(),
        ),
        out_specs=rows,
        check_vma=False,
    )
```

```python
import math

import jax
import jax.numpy as jnp
import numpy as np
from jax import lax
from jax.sharding import Mesh
from jax.sharding import PartitionSpec as P

PIECE = 128

scale_base = 1.4426950408889634
masked_score = -1e30
norm_eps = 1e-06


def column_scale(query_scale, head_count):
    head_width = query_scale.shape[0]
    factor = scale_base / math.sqrt(head_width) * jax.nn.softplus(query_scale)
    return jnp.tile(factor, head_count)


def block_positions(offsets, rows):
    return (offsets[:, None] * PIECE + lax.iota(jnp.int32, PIECE)[None, :]).reshape(rows)


def ring_steps(size):
    return size // 2, (size - 1) // 2


def ring_gather(data, axis, size, split_far=False):
    forward, backward = ring_steps(size)
    if split_far and size % 2 == 0 and size > 2:
        backward = forward
    half = data.shape[0] // 2
    pieces = [None] * size
    pieces[0] = data
    ahead = behind = data
    far_parts = [None, None]
    for step in range(max(forward, backward)):
        last = split_far and size % 2 == 0 and size > 2 and step == forward - 1
        if step < forward:
            sent = ahead[:half] if last else ahead
            ahead = lax.ppermute(sent, axis, [(i, (i + 1) % size) for i in range(size)])
            if last:
                far_parts[0] = ahead
            else:
                pieces[size - 1 - step] = ahead
        if step < backward:
            sent = behind[half:] if last else behind
            behind = lax.ppermute(sent, axis, [(i, (i - 1) % size) for i in range(size)])
            if last:
                far_parts[1] = behind
            else:
                pieces[1 + step] = behind
    if far_parts[0] is not None:
        pieces[size // 2] = jnp.concatenate(far_parts, axis=0)
    return pieces


def per_device(
    inputs, out_grads, norm_gain, w_query, w_key, w_value, w_output, query_scale, offsets
):
    row_count, width_here = inputs.shape
    head_width = query_scale.shape[0]
    heads_here = w_query.shape[0] // head_width
    cols = heads_here * head_width
    tp_size = lax.axis_size("tp")
    y_size = lax.axis_size("y")
    shards = offsets.shape[0]
    all_rows = shards * row_count
    contract = (((1,), (1,)), ((), ()))

    with jax.named_scope("gather_features"):
        both = jnp.concatenate([inputs, out_grads], axis=1)
        gathered = lax.all_gather(both, "tp", axis=1, tiled=True)
        gathered = gathered.reshape(row_count, tp_size, 2, width_here)
        full_inputs = gathered[:, :, 0, :].reshape(row_count, tp_size * width_here)
        full_grads = gathered[:, :, 1, :].reshape(row_count, tp_size * width_here)
    full_width = full_inputs.shape[1]

    with jax.named_scope("projections"):
        widened = full_inputs.astype(jnp.float32)
        inverse = lax.rsqrt(jnp.mean(widened * widened, axis=1, keepdims=True) + norm_eps)
        normed = (widened * inverse * norm_gain[None, :]).astype(jnp.bfloat16)
        factor = column_scale(query_scale, heads_here)
        queries = (
            lax.dot_general(normed, w_query, contract, preferred_element_type=jnp.float32)
            * factor[None, :]
        ).astype(jnp.bfloat16)
        keys = lax.dot_general(normed, w_key, contract, preferred_element_type=jnp.float32).astype(
            jnp.bfloat16
        )
        values = lax.dot_general(
            normed, w_value, contract, preferred_element_type=jnp.float32
        ).astype(jnp.bfloat16)
        head_grads = lax.dot_general(
            full_grads, w_output, contract, preferred_element_type=jnp.float32
        ).astype(jnp.bfloat16)

    z_size = lax.axis_size("z")
    z_index = lax.axis_index("z")
    y_index = lax.axis_index("y")

    with jax.named_scope("gather_sequence"):
        kv = jnp.concatenate([keys, values], axis=1)
        qg = jnp.concatenate([queries, head_grads], axis=1)
        kv_all = lax.all_gather(kv, "y", axis=0, tiled=True)
        kv_all = lax.all_gather(kv_all, "z", axis=0, tiled=True)
        qg_z = jnp.concatenate(ring_gather(qg, "z", z_size), axis=0)
        qg_z, kv_all = lax.optimization_barrier((qg_z, kv_all))
        qg_all = jnp.concatenate(ring_gather(qg_z, "y", y_size, True), axis=0)
        key_all = kv_all[:, :cols].reshape(all_rows, heads_here, head_width)
        value_all = kv_all[:, cols:].reshape(all_rows, heads_here, head_width)
        query_all = qg_all[:, :cols].reshape(all_rows, heads_here, head_width)
        grad_all = qg_all[:, cols:].reshape(all_rows, heads_here, head_width)

    rel_z = lax.iota(jnp.int32, z_size)
    rel_y = lax.iota(jnp.int32, y_size)
    abs_z = (z_index + rel_z) % z_size
    abs_y = (y_index + rel_y) % y_size
    qg_source = (abs_z[None, :] * y_size + abs_y[:, None]).reshape(shards)
    key_positions = block_positions(offsets, all_rows)
    query_positions = block_positions(offsets[qg_source], all_rows)
    seq_index = z_index * y_size + y_index
    own_positions = offsets[seq_index] * PIECE + lax.iota(jnp.int32, row_count)

    query_heads = queries.reshape(row_count, heads_here, head_width)
    grad_heads = head_grads.reshape(row_count, heads_here, head_width)
    key_heads = keys.reshape(row_count, heads_here, head_width)
    value_heads = values.reshape(row_count, heads_here, head_width)

    with jax.named_scope("query_pass"):
        scores = jnp.einsum(
            "qhd,khd->hqk", query_heads, key_all, preferred_element_type=jnp.float32
        )
        visible = key_positions[None, None, :] <= own_positions[None, :, None]
        masked = jnp.where(visible, scores, masked_score)
        row_peak = jnp.max(masked, axis=2)
        summed = jnp.sum(jnp.where(visible, jnp.exp(masked - row_peak[:, :, None]), 0.0), axis=2)
        log_total = row_peak + jnp.log(summed)
        attend = jnp.exp(jnp.where(visible, scores - log_total[:, :, None], masked_score))
        grad_probs = jnp.einsum(
            "qhd,khd->hqk", grad_heads, value_all, preferred_element_type=jnp.float32
        )
        weighted = attend * grad_probs
        row_delta = jnp.sum(weighted, axis=2)
        first_sum = jnp.einsum(
            "hqk,khd->hqd",
            weighted.astype(jnp.bfloat16),
            key_all,
            preferred_element_type=jnp.float32,
        )
        second_sum = jnp.einsum(
            "hqk,khd->hqd", attend.astype(jnp.bfloat16), key_all, preferred_element_type=jnp.float32
        )
        query_grad = first_sum - row_delta[:, :, None] * second_sum
        query_grad = jnp.transpose(query_grad, (1, 0, 2)).reshape(row_count, cols)
        query_done = (query_grad * factor[None, :]).astype(jnp.bfloat16)

    with jax.named_scope("gather_row_stats"):
        stats = jnp.stack([log_total, row_delta], axis=0)
        sent = jnp.broadcast_to(stats[None], (shards,) + stats.shape)
        stats_all = lax.all_to_all(sent, ("z", "y"), 0, 0, tiled=False)
        stats_all = stats_all[qg_source]
        log_all = jnp.transpose(stats_all[:, 0], (1, 0, 2)).reshape(heads_here, all_rows)
        delta_all = jnp.transpose(stats_all[:, 1], (1, 0, 2)).reshape(heads_here, all_rows)

    with jax.named_scope("key_pass"):
        scores_t = jnp.einsum(
            "khd,qhd->hkq", key_heads, query_all, preferred_element_type=jnp.float32
        )
        visible_t = own_positions[None, :, None] <= query_positions[None, None, :]
        attend_t = jnp.exp(
            jnp.where(visible_t, scores_t - log_all[:, None, :], masked_score)
        )
        grad_probs_t = jnp.einsum(
            "khd,qhd->hkq", value_heads, grad_all, preferred_element_type=jnp.float32
        )
        score_grad = (attend_t * (grad_probs_t - delta_all[:, None, :])).astype(jnp.bfloat16)
        key_grad = jnp.einsum(
            "hkq,qhd->khd", score_grad, query_all, preferred_element_type=jnp.float32
        )
        value_grad = jnp.einsum(
            "hkq,qhd->khd", attend_t.astype(jnp.bfloat16), grad_all, preferred_element_type=jnp.float32
        )
        key_done = key_grad.reshape(row_count, cols).astype(jnp.bfloat16)
        value_done = value_grad.reshape(row_count, cols).astype(jnp.bfloat16)

    with jax.named_scope("back_projection"):
        back_sum = jnp.dot(query_done, w_query, preferred_element_type=jnp.float32)
        back_sum = back_sum + jnp.dot(key_done, w_key, preferred_element_type=jnp.float32)
        back_sum = back_sum + jnp.dot(value_done, w_value, preferred_element_type=jnp.float32)
        scaled = back_sum * norm_gain[None, :]
        row_part = jnp.sum(widened * scaled, axis=1)
        chunks = scaled.reshape(row_count, tp_size, width_here).transpose(1, 0, 2)
        extra = jnp.zeros((tp_size, 1, width_here), jnp.float32)
        extra = extra.at[:, 0, :row_count].set(jnp.broadcast_to(row_part, (tp_size, row_count)))
        payload = jnp.concatenate([chunks, extra], axis=1)
        received = lax.all_to_all(payload, "tp", 0, 0, tiled=False)
        total = jnp.sum(received, axis=0)
        scaled_own = total[:row_count]
        row_dot = total[row_count, :row_count][:, None]

    with jax.named_scope("input_grads"):
        start_col = lax.axis_index("tp") * width_here
        own_inputs = inputs.astype(jnp.float32)
        branch = (
            inverse * scaled_own
            - own_inputs * inverse * inverse * inverse * row_dot / full_width
        )
        result = out_grads.astype(jnp.float32) + branch
    return result.astype(jnp.bfloat16)


def solution(mesh):
    seq_size = mesh.shape["seq"]
    devices = mesh.devices
    y_size = 4 if seq_size % 4 == 0 else 1
    split = Mesh(
        devices.reshape((seq_size // y_size, y_size) + devices.shape[1:]),
        ("z", "y", "tp", "dp"),
    )
    rows = P(("dp", "z", "y"), "tp")
    return jax.shard_map(
        per_device,
        mesh=split,
        in_specs=(
            rows,
            rows,
            P(),
            P("tp", None),
            P("tp", None),
            P("tp", None),
            P("tp", None),
            P(),
            P(),
        ),
        out_specs=rows,
        check_vma=False,
    )
```

```python
import math

import jax
import jax.numpy as jnp
import numpy as np
from jax import lax
from jax.sharding import Mesh
from jax.sharding import PartitionSpec as P

PIECE = 128

scale_base = 1.4426950408889634
masked_score = -1e30
norm_eps = 1e-06


def column_scale(query_scale, head_count):
    head_width = query_scale.shape[0]
    factor = scale_base / math.sqrt(head_width) * jax.nn.softplus(query_scale)
    return jnp.tile(factor, head_count)


def block_positions(offsets, rows):
    return (offsets[:, None] * PIECE + lax.iota(jnp.int32, PIECE)[None, :]).reshape(rows)


def ring_steps(size):
    return size // 2, (size - 1) // 2


def shift(data, axis, size, step):
    return lax.ppermute(data, axis, [(i, (i + step) % size) for i in range(size)])


def ring_gather(data, axis, size):
    forward, backward = ring_steps(size)
    pieces = [None] * size
    pieces[0] = data
    ahead = behind = data
    for step in range(max(forward, backward)):
        if step < forward:
            ahead = shift(ahead, axis, size, 1)
            pieces[size - 1 - step] = ahead
        if step < backward:
            behind = shift(behind, axis, size, -1)
            pieces[1 + step] = behind
    return pieces


def ring4_first(data, axis):
    return shift(data, axis, 4, 1), shift(data, axis, 4, -1)


def ring4_last(data, ahead, behind, axis):
    half = data.shape[0] // 2
    far = jnp.concatenate(
        [shift(ahead[:half], axis, 4, 1), shift(behind[half:], axis, 4, -1)], axis=0
    )
    return [data, behind, far, ahead]


def per_device(
    inputs, out_grads, norm_gain, w_query, w_key, w_value, w_output, query_scale, offsets
):
    row_count, width_here = inputs.shape
    head_width = query_scale.shape[0]
    heads_here = w_query.shape[0] // head_width
    cols = heads_here * head_width
    tp_size = lax.axis_size("tp")
    y_size = lax.axis_size("y")
    shards = offsets.shape[0]
    all_rows = shards * row_count
    contract = (((1,), (1,)), ((), ()))

    with jax.named_scope("gather_features"):
        both = jnp.concatenate([inputs, out_grads], axis=1)
        gathered = lax.all_gather(both, "tp", axis=1, tiled=True)
        gathered = gathered.reshape(row_count, tp_size, 2, width_here)
        full_inputs = gathered[:, :, 0, :].reshape(row_count, tp_size * width_here)
        full_grads = gathered[:, :, 1, :].reshape(row_count, tp_size * width_here)
    full_width = full_inputs.shape[1]

    with jax.named_scope("projections"):
        widened = full_inputs.astype(jnp.float32)
        inverse = lax.rsqrt(jnp.mean(widened * widened, axis=1, keepdims=True) + norm_eps)
        normed = (widened * inverse * norm_gain[None, :]).astype(jnp.bfloat16)
        factor = column_scale(query_scale, heads_here)
        queries = (
            lax.dot_general(normed, w_query, contract, preferred_element_type=jnp.float32)
            * factor[None, :]
        ).astype(jnp.bfloat16)
        keys = lax.dot_general(normed, w_key, contract, preferred_element_type=jnp.float32).astype(
            jnp.bfloat16
        )
        values = lax.dot_general(
            normed, w_value, contract, preferred_element_type=jnp.float32
        ).astype(jnp.bfloat16)
        head_grads = lax.dot_general(
            full_grads, w_output, contract, preferred_element_type=jnp.float32
        ).astype(jnp.bfloat16)

    z_size = lax.axis_size("z")
    z_index = lax.axis_index("z")
    y_index = lax.axis_index("y")

    with jax.named_scope("gather_sequence"):
        kv = jnp.concatenate([keys, values], axis=1)
        qg = jnp.concatenate([queries, head_grads], axis=1)
        kv_all = lax.all_gather(kv, "y", axis=0, tiled=True)
        kv_all = lax.all_gather(kv_all, "z", axis=0, tiled=True)
        qg_z = jnp.concatenate(ring_gather(qg, "z", z_size), axis=0)
        qg_z, kv_all = lax.optimization_barrier((qg_z, kv_all))
        qg_ahead, qg_behind = ring4_first(qg_z, "y")
        key_all = kv_all[:, :cols].reshape(all_rows, heads_here, head_width)
        value_all = kv_all[:, cols:].reshape(all_rows, heads_here, head_width)

    rel_z = lax.iota(jnp.int32, z_size)
    rel_y = lax.iota(jnp.int32, y_size)
    abs_z = (z_index + rel_z) % z_size
    abs_y = (y_index + rel_y) % y_size
    qg_source = (abs_z[None, :] * y_size + abs_y[:, None]).reshape(shards)
    key_positions = block_positions(offsets, all_rows)
    query_positions = block_positions(offsets[qg_source], all_rows)
    seq_index = z_index * y_size + y_index
    own_positions = offsets[seq_index] * PIECE + lax.iota(jnp.int32, row_count)

    query_heads = queries.reshape(row_count, heads_here, head_width)
    grad_heads = head_grads.reshape(row_count, heads_here, head_width)
    key_heads = keys.reshape(row_count, heads_here, head_width)
    value_heads = values.reshape(row_count, heads_here, head_width)

    with jax.named_scope("query_pass"):
        scores = jnp.einsum(
            "qhd,khd->hqk", query_heads, key_all, preferred_element_type=jnp.float32
        )
        visible = key_positions[None, None, :] <= own_positions[None, :, None]
        masked = jnp.where(visible, scores, masked_score)
        row_peak = jnp.max(masked, axis=2)
        summed = jnp.sum(jnp.where(visible, jnp.exp(masked - row_peak[:, :, None]), 0.0), axis=2)
        log_total = row_peak + jnp.log(summed)
        attend = jnp.exp(jnp.where(visible, scores - log_total[:, :, None], masked_score))
        grad_probs = jnp.einsum(
            "qhd,khd->hqk", grad_heads, value_all, preferred_element_type=jnp.float32
        )
        weighted = attend * grad_probs
        row_delta = jnp.sum(weighted, axis=2)
        first_sum = jnp.einsum(
            "hqk,khd->hqd",
            weighted.astype(jnp.bfloat16),
            key_all,
            preferred_element_type=jnp.float32,
        )
        second_sum = jnp.einsum(
            "hqk,khd->hqd", attend.astype(jnp.bfloat16), key_all, preferred_element_type=jnp.float32
        )
        query_grad = first_sum - row_delta[:, :, None] * second_sum
        query_grad = jnp.transpose(query_grad, (1, 0, 2)).reshape(row_count, cols)
        query_done = (query_grad * factor[None, :]).astype(jnp.bfloat16)

    with jax.named_scope("gather_row_stats"):
        stats = jnp.stack([log_total, row_delta], axis=0)
        stats, qg_ahead, qg_behind = lax.optimization_barrier((stats, qg_ahead, qg_behind))
        qg_all = jnp.concatenate(ring4_last(qg_z, qg_ahead, qg_behind, "y"), axis=0)
        query_all = qg_all[:, :cols].reshape(all_rows, heads_here, head_width)
        grad_all = qg_all[:, cols:].reshape(all_rows, heads_here, head_width)
        sent = jnp.broadcast_to(stats[None], (shards,) + stats.shape)
        stats_all = lax.all_to_all(sent, ("z", "y"), 0, 0, tiled=False)
        stats_all = stats_all[qg_source]
        log_all = jnp.transpose(stats_all[:, 0], (1, 0, 2)).reshape(heads_here, all_rows)
        delta_all = jnp.transpose(stats_all[:, 1], (1, 0, 2)).reshape(heads_here, all_rows)

    with jax.named_scope("key_pass"):
        scores_t = jnp.einsum(
            "khd,qhd->hkq", key_heads, query_all, preferred_element_type=jnp.float32
        )
        visible_t = own_positions[None, :, None] <= query_positions[None, None, :]
        attend_t = jnp.exp(
            jnp.where(visible_t, scores_t - log_all[:, None, :], masked_score)
        )
        grad_probs_t = jnp.einsum(
            "khd,qhd->hkq", value_heads, grad_all, preferred_element_type=jnp.float32
        )
        score_grad = (attend_t * (grad_probs_t - delta_all[:, None, :])).astype(jnp.bfloat16)
        key_grad = jnp.einsum(
            "hkq,qhd->khd", score_grad, query_all, preferred_element_type=jnp.float32
        )
        value_grad = jnp.einsum(
            "hkq,qhd->khd", attend_t.astype(jnp.bfloat16), grad_all, preferred_element_type=jnp.float32
        )
        key_done = key_grad.reshape(row_count, cols).astype(jnp.bfloat16)
        value_done = value_grad.reshape(row_count, cols).astype(jnp.bfloat16)

    with jax.named_scope("back_projection"):
        back_sum = jnp.dot(query_done, w_query, preferred_element_type=jnp.float32)
        back_sum = back_sum + jnp.dot(key_done, w_key, preferred_element_type=jnp.float32)
        back_sum = back_sum + jnp.dot(value_done, w_value, preferred_element_type=jnp.float32)
        scaled = back_sum * norm_gain[None, :]
        row_part = jnp.sum(widened * scaled, axis=1)
        chunks = scaled.reshape(row_count, tp_size, width_here).transpose(1, 0, 2)
        extra = jnp.zeros((tp_size, 1, width_here), jnp.float32)
        extra = extra.at[:, 0, :row_count].set(jnp.broadcast_to(row_part, (tp_size, row_count)))
        payload = jnp.concatenate([chunks, extra], axis=1)
        received = lax.all_to_all(payload, "tp", 0, 0, tiled=False)
        total = jnp.sum(received, axis=0)
        scaled_own = total[:row_count]
        row_dot = total[row_count, :row_count][:, None]

    with jax.named_scope("input_grads"):
        start_col = lax.axis_index("tp") * width_here
        own_inputs = inputs.astype(jnp.float32)
        branch = (
            inverse * scaled_own
            - own_inputs * inverse * inverse * inverse * row_dot / full_width
        )
        result = out_grads.astype(jnp.float32) + branch
    return result.astype(jnp.bfloat16)


def solution(mesh):
    seq_size = mesh.shape["seq"]
    devices = mesh.devices
    y_size = 4 if seq_size % 4 == 0 else 1
    split = Mesh(
        devices.reshape((seq_size // y_size, y_size) + devices.shape[1:]),
        ("z", "y", "tp", "dp"),
    )
    rows = P(("dp", "z", "y"), "tp")
    return jax.shard_map(
        per_device,
        mesh=split,
        in_specs=(
            rows,
            rows,
            P(),
            P("tp", None),
            P("tp", None),
            P("tp", None),
            P("tp", None),
            P(),
            P(),
        ),
        out_specs=rows,
        check_vma=False,
    )
```

```python
import math

import jax
import jax.numpy as jnp
import numpy as np
from jax import lax
from jax.sharding import Mesh
from jax.sharding import PartitionSpec as P

PIECE = 128

scale_base = 1.4426950408889634
masked_score = -1e30
norm_eps = 1e-06


def column_scale(query_scale, head_count):
    head_width = query_scale.shape[0]
    factor = scale_base / math.sqrt(head_width) * jax.nn.softplus(query_scale)
    return jnp.tile(factor, head_count)


def block_positions(offsets, rows):
    return (offsets[:, None] * PIECE + lax.iota(jnp.int32, PIECE)[None, :]).reshape(rows)


def ring_steps(size):
    return size // 2, (size - 1) // 2


def shift(data, axis, size, step):
    return lax.ppermute(data, axis, [(i, (i + step) % size) for i in range(size)])


def ring_gather(data, axis, size):
    forward, backward = ring_steps(size)
    pieces = [None] * size
    pieces[0] = data
    ahead = behind = data
    for step in range(max(forward, backward)):
        if step < forward:
            ahead = shift(ahead, axis, size, 1)
            pieces[size - 1 - step] = ahead
        if step < backward:
            behind = shift(behind, axis, size, -1)
            pieces[1 + step] = behind
    return pieces


def ring4_first(data, axis):
    return shift(data, axis, 4, 1), shift(data, axis, 4, -1)


def ring4_last(data, ahead, behind, axis):
    half = data.shape[0] // 2
    far = jnp.concatenate(
        [shift(ahead[:half], axis, 4, 1), shift(behind[half:], axis, 4, -1)], axis=0
    )
    return [data, behind, far, ahead]


def per_device(
    inputs, out_grads, norm_gain, w_query, w_key, w_value, w_output, query_scale, offsets
):
    row_count, width_here = inputs.shape
    head_width = query_scale.shape[0]
    heads_here = w_query.shape[0] // head_width
    cols = heads_here * head_width
    tp_size = lax.axis_size("tp")
    y_size = lax.axis_size("y")
    shards = offsets.shape[0]
    all_rows = shards * row_count
    contract = (((1,), (1,)), ((), ()))

    with jax.named_scope("gather_features"):
        both = jnp.concatenate([inputs, out_grads], axis=1)
        gathered = lax.all_gather(both, "tp", axis=1, tiled=True)
        gathered = gathered.reshape(row_count, tp_size, 2, width_here)
        full_inputs = gathered[:, :, 0, :].reshape(row_count, tp_size * width_here)
        full_grads = gathered[:, :, 1, :].reshape(row_count, tp_size * width_here)
    full_width = full_inputs.shape[1]

    with jax.named_scope("projections"):
        widened = full_inputs.astype(jnp.float32)
        inverse = lax.rsqrt(jnp.mean(widened * widened, axis=1, keepdims=True) + norm_eps)
        normed = (widened * inverse * norm_gain[None, :]).astype(jnp.bfloat16)
        factor = column_scale(query_scale, heads_here)
        queries = (
            lax.dot_general(normed, w_query, contract, preferred_element_type=jnp.float32)
            * factor[None, :]
        ).astype(jnp.bfloat16)
        keys = lax.dot_general(normed, w_key, contract, preferred_element_type=jnp.float32).astype(
            jnp.bfloat16
        )
        values = lax.dot_general(
            normed, w_value, contract, preferred_element_type=jnp.float32
        ).astype(jnp.bfloat16)
        head_grads = lax.dot_general(
            full_grads, w_output, contract, preferred_element_type=jnp.float32
        ).astype(jnp.bfloat16)

    z_size = lax.axis_size("z")
    z_index = lax.axis_index("z")
    y_index = lax.axis_index("y")

    with jax.named_scope("gather_sequence"):
        kv = jnp.concatenate([keys, values], axis=1)
        qg = jnp.concatenate([queries, head_grads], axis=1)
        kv_all = lax.all_gather(kv, "y", axis=0, tiled=True)
        kv_all = lax.all_gather(kv_all, "z", axis=0, tiled=True)
        qg_z = jnp.concatenate(ring_gather(qg, "z", z_size), axis=0)
        qg_z, kv_all = lax.optimization_barrier((qg_z, kv_all))
        qg_ahead, qg_behind = ring4_first(qg_z, "y")
        key_all = kv_all[:, :cols].reshape(all_rows, heads_here, head_width)
        value_all = kv_all[:, cols:].reshape(all_rows, heads_here, head_width)

    rel_z = lax.iota(jnp.int32, z_size)
    rel_y = lax.iota(jnp.int32, y_size)
    abs_z = (z_index + rel_z) % z_size
    abs_y = (y_index + rel_y) % y_size
    qg_source = (abs_z[None, :] * y_size + abs_y[:, None]).reshape(shards)
    key_positions = block_positions(offsets, all_rows)
    seq_index = z_index * y_size + y_index
    own_positions = offsets[seq_index] * PIECE + lax.iota(jnp.int32, row_count)

    query_heads = queries.reshape(row_count, heads_here, head_width)
    grad_heads = head_grads.reshape(row_count, heads_here, head_width)
    key_heads = keys.reshape(row_count, heads_here, head_width)
    value_heads = values.reshape(row_count, heads_here, head_width)

    with jax.named_scope("query_pass"):
        scores = jnp.einsum(
            "qhd,khd->hqk", query_heads, key_all, preferred_element_type=jnp.float32
        )
        visible = key_positions[None, None, :] <= own_positions[None, :, None]
        masked = jnp.where(visible, scores, masked_score)
        row_peak = jnp.max(masked, axis=2)
        summed = jnp.sum(jnp.where(visible, jnp.exp(masked - row_peak[:, :, None]), 0.0), axis=2)
        log_total = row_peak + jnp.log(summed)
        attend = jnp.exp(jnp.where(visible, scores - log_total[:, :, None], masked_score))
        grad_probs = jnp.einsum(
            "qhd,khd->hqk", grad_heads, value_all, preferred_element_type=jnp.float32
        )
        weighted = attend * grad_probs
        row_delta = jnp.sum(weighted, axis=2)
        first_sum = jnp.einsum(
            "hqk,khd->hqd",
            weighted.astype(jnp.bfloat16),
            key_all,
            preferred_element_type=jnp.float32,
        )
        second_sum = jnp.einsum(
            "hqk,khd->hqd", attend.astype(jnp.bfloat16), key_all, preferred_element_type=jnp.float32
        )
        query_grad = first_sum - row_delta[:, :, None] * second_sum
        query_grad = jnp.transpose(query_grad, (1, 0, 2)).reshape(row_count, cols)
        query_done = (query_grad * factor[None, :]).astype(jnp.bfloat16)

    with jax.named_scope("gather_row_stats"):
        stats = jnp.stack([log_total, row_delta], axis=0)
        stats, qg_ahead, qg_behind = lax.optimization_barrier((stats, qg_ahead, qg_behind))
        qg_pieces = ring4_last(qg_z, qg_ahead, qg_behind, "y")
        sent = jnp.broadcast_to(stats[None], (shards,) + stats.shape)
        stats_all = lax.all_to_all(sent, ("z", "y"), 0, 0, tiled=False)

    with jax.named_scope("key_pass"):
        piece_rows = qg_pieces[0].shape[0]
        key_grad = jnp.zeros((row_count, heads_here, head_width), jnp.float32)
        value_grad = jnp.zeros((row_count, heads_here, head_width), jnp.float32)
        for ry, piece in enumerate(qg_pieces):
            source = qg_source[ry * z_size : (ry + 1) * z_size]
            query_part = piece[:, :cols].reshape(piece_rows, heads_here, head_width)
            grad_part = piece[:, cols:].reshape(piece_rows, heads_here, head_width)
            place = block_positions(offsets[source], piece_rows)
            part_stats = stats_all[source]
            log_part = jnp.transpose(part_stats[:, 0], (1, 0, 2)).reshape(heads_here, piece_rows)
            delta_part = jnp.transpose(part_stats[:, 1], (1, 0, 2)).reshape(
                heads_here, piece_rows
            )
            scores_t = jnp.einsum(
                "khd,qhd->hkq", key_heads, query_part, preferred_element_type=jnp.float32
            )
            visible_t = own_positions[None, :, None] <= place[None, None, :]
            attend_t = jnp.exp(
                jnp.where(visible_t, scores_t - log_part[:, None, :], masked_score)
            )
            grad_probs_t = jnp.einsum(
                "khd,qhd->hkq", value_heads, grad_part, preferred_element_type=jnp.float32
            )
            score_grad = (attend_t * (grad_probs_t - delta_part[:, None, :])).astype(
                jnp.bfloat16
            )
            key_grad = key_grad + jnp.einsum(
                "hkq,qhd->khd", score_grad, query_part, preferred_element_type=jnp.float32
            )
            value_grad = value_grad + jnp.einsum(
                "hkq,qhd->khd",
                attend_t.astype(jnp.bfloat16),
                grad_part,
                preferred_element_type=jnp.float32,
            )
        key_done = key_grad.reshape(row_count, cols).astype(jnp.bfloat16)
        value_done = value_grad.reshape(row_count, cols).astype(jnp.bfloat16)

    with jax.named_scope("back_projection"):
        back_sum = jnp.dot(query_done, w_query, preferred_element_type=jnp.float32)
        back_sum = back_sum + jnp.dot(key_done, w_key, preferred_element_type=jnp.float32)
        back_sum = back_sum + jnp.dot(value_done, w_value, preferred_element_type=jnp.float32)
        scaled = back_sum * norm_gain[None, :]
        row_part = jnp.sum(widened * scaled, axis=1)
        chunks = scaled.reshape(row_count, tp_size, width_here).transpose(1, 0, 2)
        extra = jnp.zeros((tp_size, 1, width_here), jnp.float32)
        extra = extra.at[:, 0, :row_count].set(jnp.broadcast_to(row_part, (tp_size, row_count)))
        payload = jnp.concatenate([chunks, extra], axis=1)
        received = lax.all_to_all(payload, "tp", 0, 0, tiled=False)
        total = jnp.sum(received, axis=0)
        scaled_own = total[:row_count]
        row_dot = total[row_count, :row_count][:, None]

    with jax.named_scope("input_grads"):
        start_col = lax.axis_index("tp") * width_here
        own_inputs = inputs.astype(jnp.float32)
        branch = (
            inverse * scaled_own
            - own_inputs * inverse * inverse * inverse * row_dot / full_width
        )
        result = out_grads.astype(jnp.float32) + branch
    return result.astype(jnp.bfloat16)


def solution(mesh):
    seq_size = mesh.shape["seq"]
    devices = mesh.devices
    y_size = 4 if seq_size % 4 == 0 else 1
    split = Mesh(
        devices.reshape((seq_size // y_size, y_size) + devices.shape[1:]),
        ("z", "y", "tp", "dp"),
    )
    rows = P(("dp", "z", "y"), "tp")
    return jax.shard_map(
        per_device,
        mesh=split,
        in_specs=(
            rows,
            rows,
            P(),
            P("tp", None),
            P("tp", None),
            P("tp", None),
            P("tp", None),
            P(),
            P(),
        ),
        out_specs=rows,
        check_vma=False,
    )
```

```python
import math

import jax
import jax.numpy as jnp
import numpy as np
from jax import lax
from jax.sharding import Mesh
from jax.sharding import PartitionSpec as P

PIECE = 128

scale_base = 1.4426950408889634
masked_score = -1e30
norm_eps = 1e-06


def column_scale(query_scale, head_count):
    head_width = query_scale.shape[0]
    factor = scale_base / math.sqrt(head_width) * jax.nn.softplus(query_scale)
    return jnp.tile(factor, head_count)


def block_positions(offsets, rows):
    return (offsets[:, None] * PIECE + lax.iota(jnp.int32, PIECE)[None, :]).reshape(rows)


def ring_steps(size):
    return size // 2, (size - 1) // 2


def shift(data, axis, size, step):
    return lax.ppermute(data, axis, [(i, (i + step) % size) for i in range(size)])


def ring_gather(data, axis, size):
    forward, backward = ring_steps(size)
    pieces = [None] * size
    pieces[0] = data
    ahead = behind = data
    for step in range(max(forward, backward)):
        if step < forward:
            ahead = shift(ahead, axis, size, 1)
            pieces[size - 1 - step] = ahead
        if step < backward:
            behind = shift(behind, axis, size, -1)
            pieces[1 + step] = behind
    return pieces


def ring4_first(data, axis):
    return shift(data, axis, 4, 1), shift(data, axis, 4, -1)


def ring4_last(data, ahead, behind, axis):
    half = data.shape[0] // 2
    far = jnp.concatenate(
        [shift(ahead[:half], axis, 4, 1), shift(behind[half:], axis, 4, -1)], axis=0
    )
    return [data, behind, far, ahead]


def per_device(
    inputs, out_grads, norm_gain, w_query, w_key, w_value, w_output, query_scale, offsets
):
    row_count, width_here = inputs.shape
    head_width = query_scale.shape[0]
    heads_here = w_query.shape[0] // head_width
    cols = heads_here * head_width
    tp_size = lax.axis_size("tp")
    y_size = lax.axis_size("y")
    shards = offsets.shape[0]
    all_rows = shards * row_count
    contract = (((1,), (1,)), ((), ()))

    with jax.named_scope("gather_features"):
        both = jnp.concatenate([inputs, out_grads], axis=1)
        gathered = lax.all_gather(both, "tp", axis=1, tiled=True)
        gathered = gathered.reshape(row_count, tp_size, 2, width_here)
        full_inputs = gathered[:, :, 0, :].reshape(row_count, tp_size * width_here)
        full_grads = gathered[:, :, 1, :].reshape(row_count, tp_size * width_here)
    full_width = full_inputs.shape[1]

    with jax.named_scope("projections"):
        widened = full_inputs.astype(jnp.float32)
        inverse = lax.rsqrt(jnp.mean(widened * widened, axis=1, keepdims=True) + norm_eps)
        normed = (widened * inverse * norm_gain[None, :]).astype(jnp.bfloat16)
        factor = column_scale(query_scale, heads_here)
        queries = (
            lax.dot_general(normed, w_query, contract, preferred_element_type=jnp.float32)
            * factor[None, :]
        ).astype(jnp.bfloat16)
        keys = lax.dot_general(normed, w_key, contract, preferred_element_type=jnp.float32).astype(
            jnp.bfloat16
        )
        values = lax.dot_general(
            normed, w_value, contract, preferred_element_type=jnp.float32
        ).astype(jnp.bfloat16)
        head_grads = lax.dot_general(
            full_grads, w_output, contract, preferred_element_type=jnp.float32
        ).astype(jnp.bfloat16)

    z_size = lax.axis_size("z")
    z_index = lax.axis_index("z")
    y_index = lax.axis_index("y")

    with jax.named_scope("gather_sequence"):
        kv = jnp.concatenate([keys, values], axis=1)
        qg = jnp.concatenate([queries, head_grads], axis=1)
        kv_all = lax.all_gather(kv, "y", axis=0, tiled=True)
        kv_all = lax.all_gather(kv_all, "z", axis=0, tiled=True)
        qg_z = jnp.concatenate(ring_gather(qg, "z", z_size), axis=0)
        qg_ahead, qg_behind = ring4_first(qg_z, "y")
        key_all = kv_all[:, :cols].reshape(all_rows, heads_here, head_width)
        value_all = kv_all[:, cols:].reshape(all_rows, heads_here, head_width)

    rel_z = lax.iota(jnp.int32, z_size)
    rel_y = lax.iota(jnp.int32, y_size)
    abs_z = (z_index + rel_z) % z_size
    abs_y = (y_index + rel_y) % y_size
    qg_source = (abs_z[None, :] * y_size + abs_y[:, None]).reshape(shards)
    key_positions = block_positions(offsets, all_rows)
    seq_index = z_index * y_size + y_index
    own_positions = offsets[seq_index] * PIECE + lax.iota(jnp.int32, row_count)

    query_heads = queries.reshape(row_count, heads_here, head_width)
    grad_heads = head_grads.reshape(row_count, heads_here, head_width)
    key_heads = keys.reshape(row_count, heads_here, head_width)
    value_heads = values.reshape(row_count, heads_here, head_width)

    with jax.named_scope("query_pass"):
        scores = jnp.einsum(
            "qhd,khd->hqk", query_heads, key_all, preferred_element_type=jnp.float32
        )
        visible = key_positions[None, None, :] <= own_positions[None, :, None]
        masked = jnp.where(visible, scores, masked_score)
        row_peak = jnp.max(masked, axis=2)
        summed = jnp.sum(jnp.where(visible, jnp.exp(masked - row_peak[:, :, None]), 0.0), axis=2)
        log_total = row_peak + jnp.log(summed)
        attend = jnp.exp(jnp.where(visible, scores - log_total[:, :, None], masked_score))
        grad_probs = jnp.einsum(
            "qhd,khd->hqk", grad_heads, value_all, preferred_element_type=jnp.float32
        )
        weighted = attend * grad_probs
        row_delta = jnp.sum(weighted, axis=2)
        first_sum = jnp.einsum(
            "hqk,khd->hqd",
            weighted.astype(jnp.bfloat16),
            key_all,
            preferred_element_type=jnp.float32,
        )
        second_sum = jnp.einsum(
            "hqk,khd->hqd", attend.astype(jnp.bfloat16), key_all, preferred_element_type=jnp.float32
        )
        query_grad = first_sum - row_delta[:, :, None] * second_sum
        query_grad = jnp.transpose(query_grad, (1, 0, 2)).reshape(row_count, cols)
        query_done = (query_grad * factor[None, :]).astype(jnp.bfloat16)

    with jax.named_scope("gather_row_stats"):
        stats = jnp.stack([log_total, row_delta], axis=0)
        stats, qg_ahead, qg_behind = lax.optimization_barrier((stats, qg_ahead, qg_behind))
        qg_pieces = ring4_last(qg_z, qg_ahead, qg_behind, "y")
        sent = jnp.broadcast_to(stats[None], (shards,) + stats.shape)
        stats_all = lax.all_to_all(sent, ("z", "y"), 0, 0, tiled=False)

    with jax.named_scope("key_pass"):
        piece_rows = qg_pieces[0].shape[0]
        key_grad = jnp.zeros((row_count, heads_here, head_width), jnp.float32)
        value_grad = jnp.zeros((row_count, heads_here, head_width), jnp.float32)
        for ry, piece in enumerate(qg_pieces):
            source = qg_source[ry * z_size : (ry + 1) * z_size]
            query_part = piece[:, :cols].reshape(piece_rows, heads_here, head_width)
            grad_part = piece[:, cols:].reshape(piece_rows, heads_here, head_width)
            place = block_positions(offsets[source], piece_rows)
            part_stats = stats_all[source]
            log_part = jnp.transpose(part_stats[:, 0], (1, 0, 2)).reshape(heads_here, piece_rows)
            delta_part = jnp.transpose(part_stats[:, 1], (1, 0, 2)).reshape(
                heads_here, piece_rows
            )
            scores_t = jnp.einsum(
                "khd,qhd->hkq", key_heads, query_part, preferred_element_type=jnp.float32
            )
            visible_t = own_positions[None, :, None] <= place[None, None, :]
            attend_t = jnp.exp(
                jnp.where(visible_t, scores_t - log_part[:, None, :], masked_score)
            )
            grad_probs_t = jnp.einsum(
                "khd,qhd->hkq", value_heads, grad_part, preferred_element_type=jnp.float32
            )
            score_grad = (attend_t * (grad_probs_t - delta_part[:, None, :])).astype(
                jnp.bfloat16
            )
            key_grad = key_grad + jnp.einsum(
                "hkq,qhd->khd", score_grad, query_part, preferred_element_type=jnp.float32
            )
            value_grad = value_grad + jnp.einsum(
                "hkq,qhd->khd",
                attend_t.astype(jnp.bfloat16),
                grad_part,
                preferred_element_type=jnp.float32,
            )
        key_done = key_grad.reshape(row_count, cols).astype(jnp.bfloat16)
        value_done = value_grad.reshape(row_count, cols).astype(jnp.bfloat16)

    with jax.named_scope("back_projection"):
        back_sum = jnp.dot(query_done, w_query, preferred_element_type=jnp.float32)
        back_sum = back_sum + jnp.dot(key_done, w_key, preferred_element_type=jnp.float32)
        back_sum = back_sum + jnp.dot(value_done, w_value, preferred_element_type=jnp.float32)
        scaled = back_sum * norm_gain[None, :]
        row_part = jnp.sum(widened * scaled, axis=1)
        chunks = scaled.reshape(row_count, tp_size, width_here).transpose(1, 0, 2)
        extra = jnp.zeros((tp_size, 1, width_here), jnp.float32)
        extra = extra.at[:, 0, :row_count].set(jnp.broadcast_to(row_part, (tp_size, row_count)))
        payload = jnp.concatenate([chunks, extra], axis=1)
        received = lax.all_to_all(payload, "tp", 0, 0, tiled=False)
        total = jnp.sum(received, axis=0)
        scaled_own = total[:row_count]
        row_dot = total[row_count, :row_count][:, None]

    with jax.named_scope("input_grads"):
        start_col = lax.axis_index("tp") * width_here
        own_inputs = inputs.astype(jnp.float32)
        branch = (
            inverse * scaled_own
            - own_inputs * inverse * inverse * inverse * row_dot / full_width
        )
        result = out_grads.astype(jnp.float32) + branch
    return result.astype(jnp.bfloat16)


def solution(mesh):
    seq_size = mesh.shape["seq"]
    devices = mesh.devices
    y_size = 4 if seq_size % 4 == 0 else 1
    split = Mesh(
        devices.reshape((seq_size // y_size, y_size) + devices.shape[1:]),
        ("z", "y", "tp", "dp"),
    )
    rows = P(("dp", "z", "y"), "tp")
    return jax.shard_map(
        per_device,
        mesh=split,
        in_specs=(
            rows,
            rows,
            P(),
            P("tp", None),
            P("tp", None),
            P("tp", None),
            P("tp", None),
            P(),
            P(),
        ),
        out_specs=rows,
        check_vma=False,
    )
```

```python
import functools
import math

import jax
import jax.numpy as jnp
import numpy as np
from jax import lax
from jax.experimental import pallas as pl
from jax.sharding import Mesh
from jax.sharding import PartitionSpec as P

PIECE = 128

scale_base = 1.4426950408889634
masked_score = -1e30
norm_eps = 1e-06


def column_scale(query_scale, head_count):
    head_width = query_scale.shape[0]
    factor = scale_base / math.sqrt(head_width) * jax.nn.softplus(query_scale)
    return jnp.tile(factor, head_count)


def block_positions(offsets, rows):
    return (offsets[:, None] * PIECE + lax.iota(jnp.int32, PIECE)[None, :]).reshape(rows)


def ring_steps(size):
    return size // 2, (size - 1) // 2


def shift(data, axis, size, step):
    return lax.ppermute(data, axis, [(i, (i + step) % size) for i in range(size)])


def ring_gather(data, axis, size):
    forward, backward = ring_steps(size)
    pieces = [None] * size
    pieces[0] = data
    ahead = behind = data
    for step in range(max(forward, backward)):
        if step < forward:
            ahead = shift(ahead, axis, size, 1)
            pieces[size - 1 - step] = ahead
        if step < backward:
            behind = shift(behind, axis, size, -1)
            pieces[1 + step] = behind
    return pieces


def ring4_first(data, axis):
    return shift(data, axis, 4, 1), shift(data, axis, 4, -1)


def ring4_last(data, ahead, behind, axis):
    half = data.shape[0] // 2
    far = jnp.concatenate(
        [shift(ahead[:half], axis, 4, 1), shift(behind[half:], axis, 4, -1)], axis=0
    )
    return [data, behind, far, ahead]


def key_pass_kernel(own_ref, key_ref, value_ref, qg_ref, place_ref, stats_ref, dk_ref, dv_ref, *, heads, head_width):
    step = pl.program_id(0)

    @pl.when(step == 0)
    def _():
        dk_ref[...] = jnp.zeros_like(dk_ref)
        dv_ref[...] = jnp.zeros_like(dv_ref)

    cols = heads * head_width
    query = qg_ref[:, :cols]
    grad = qg_ref[:, cols:]
    keys = key_ref[...]
    values = value_ref[...]
    visible = own_ref[...] <= place_ref[...]
    column = lax.broadcasted_iota(jnp.int32, (1, cols), 1) // head_width
    nt = (((1,), (1,)), ((), ()))
    dk = dk_ref[...]
    dv = dv_ref[...]
    for h in range(heads):
        mine = column == h
        key_h = jnp.where(mine, keys, jnp.zeros_like(keys))
        value_h = jnp.where(mine, values, jnp.zeros_like(values))
        scores = lax.dot_general(key_h, query, nt, preferred_element_type=jnp.float32)
        grad_probs = lax.dot_general(value_h, grad, nt, preferred_element_type=jnp.float32)
        log_h = stats_ref[h : h + 1, :]
        delta_h = stats_ref[heads + h : heads + h + 1, :]
        attend = jnp.exp(jnp.where(visible, scores - log_h, masked_score))
        score_grad = (attend * (grad_probs - delta_h)).astype(jnp.bfloat16)
        part_k = jnp.dot(score_grad, query, preferred_element_type=jnp.float32)
        part_v = jnp.dot(attend.astype(jnp.bfloat16), grad, preferred_element_type=jnp.float32)
        dk = dk + jnp.where(mine, part_k, 0.0)
        dv = dv + jnp.where(mine, part_v, 0.0)
    dk_ref[...] = dk
    dv_ref[...] = dv


def key_pass(own_positions, keys, values, qg, place, stats, heads, head_width, block=512):
    rows = keys.shape[0]
    cols = keys.shape[1]
    total = qg.shape[0]
    steps = total // block
    kernel = functools.partial(key_pass_kernel, heads=heads, head_width=head_width)
    flops = steps * heads * 4 * 2 * rows * block * cols
    return pl.pallas_call(
        kernel,
        grid=(steps,),
        in_specs=[
            pl.BlockSpec((rows, 1), lambda i: (0, 0)),
            pl.BlockSpec((rows, cols), lambda i: (0, 0)),
            pl.BlockSpec((rows, cols), lambda i: (0, 0)),
            pl.BlockSpec((block, 2 * cols), lambda i: (i, 0)),
            pl.BlockSpec((1, block), lambda i: (0, i)),
            pl.BlockSpec((2 * heads, block), lambda i: (0, i)),
        ],
        out_specs=[
            pl.BlockSpec((rows, cols), lambda i: (0, 0)),
            pl.BlockSpec((rows, cols), lambda i: (0, 0)),
        ],
        out_shape=[
            jax.ShapeDtypeStruct((rows, cols), jnp.float32),
            jax.ShapeDtypeStruct((rows, cols), jnp.float32),
        ],
        cost_estimate=pl.CostEstimate(
            flops=flops, transcendentals=steps * heads * rows * block,
            bytes_accessed=total * 2 * cols * 2 + total * 4 * (2 * heads + 1) + rows * cols * 12,
        ),
    )(own_positions.reshape(rows, 1), keys, values, qg, place.reshape(1, total), stats)


def per_device(
    inputs, out_grads, norm_gain, w_query, w_key, w_value, w_output, query_scale, offsets
):
    row_count, width_here = inputs.shape
    head_width = query_scale.shape[0]
    heads_here = w_query.shape[0] // head_width
    cols = heads_here * head_width
    tp_size = lax.axis_size("tp")
    y_size = lax.axis_size("y")
    shards = offsets.shape[0]
    all_rows = shards * row_count
    contract = (((1,), (1,)), ((), ()))

    with jax.named_scope("gather_features"):
        both = jnp.concatenate([inputs, out_grads], axis=1)
        gathered = lax.all_gather(both, "tp", axis=1, tiled=True)
        gathered = gathered.reshape(row_count, tp_size, 2, width_here)
        full_inputs = gathered[:, :, 0, :].reshape(row_count, tp_size * width_here)
        full_grads = gathered[:, :, 1, :].reshape(row_count, tp_size * width_here)
    full_width = full_inputs.shape[1]

    with jax.named_scope("projections"):
        widened = full_inputs.astype(jnp.float32)
        inverse = lax.rsqrt(jnp.mean(widened * widened, axis=1, keepdims=True) + norm_eps)
        normed = (widened * inverse * norm_gain[None, :]).astype(jnp.bfloat16)
        factor = column_scale(query_scale, heads_here)
        queries = (
            lax.dot_general(normed, w_query, contract, preferred_element_type=jnp.float32)
            * factor[None, :]
        ).astype(jnp.bfloat16)
        keys = lax.dot_general(normed, w_key, contract, preferred_element_type=jnp.float32).astype(
            jnp.bfloat16
        )
        values = lax.dot_general(
            normed, w_value, contract, preferred_element_type=jnp.float32
        ).astype(jnp.bfloat16)
        head_grads = lax.dot_general(
            full_grads, w_output, contract, preferred_element_type=jnp.float32
        ).astype(jnp.bfloat16)

    z_size = lax.axis_size("z")
    z_index = lax.axis_index("z")
    y_index = lax.axis_index("y")

    with jax.named_scope("gather_sequence"):
        kv = jnp.concatenate([keys, values], axis=1)
        qg = jnp.concatenate([queries, head_grads], axis=1)
        kv_all = lax.all_gather(kv, "y", axis=0, tiled=True)
        kv_all = lax.all_gather(kv_all, "z", axis=0, tiled=True)
        qg_z = jnp.concatenate(ring_gather(qg, "z", z_size), axis=0)
        qg_ahead, qg_behind = ring4_first(qg_z, "y")
        key_all = kv_all[:, :cols].reshape(all_rows, heads_here, head_width)
        value_all = kv_all[:, cols:].reshape(all_rows, heads_here, head_width)

    rel_z = lax.iota(jnp.int32, z_size)
    rel_y = lax.iota(jnp.int32, y_size)
    abs_z = (z_index + rel_z) % z_size
    abs_y = (y_index + rel_y) % y_size
    qg_source = (abs_z[None, :] * y_size + abs_y[:, None]).reshape(shards)
    key_positions = block_positions(offsets, all_rows)
    seq_index = z_index * y_size + y_index
    own_positions = offsets[seq_index] * PIECE + lax.iota(jnp.int32, row_count)

    query_heads = queries.reshape(row_count, heads_here, head_width)
    grad_heads = head_grads.reshape(row_count, heads_here, head_width)
    key_heads = keys.reshape(row_count, heads_here, head_width)
    value_heads = values.reshape(row_count, heads_here, head_width)

    with jax.named_scope("query_pass"):
        scores = jnp.einsum(
            "qhd,khd->hqk", query_heads, key_all, preferred_element_type=jnp.float32
        )
        visible = key_positions[None, None, :] <= own_positions[None, :, None]
        masked = jnp.where(visible, scores, masked_score)
        row_peak = jnp.max(masked, axis=2)
        summed = jnp.sum(jnp.where(visible, jnp.exp(masked - row_peak[:, :, None]), 0.0), axis=2)
        log_total = row_peak + jnp.log(summed)
        attend = jnp.exp(jnp.where(visible, scores - log_total[:, :, None], masked_score))
        grad_probs = jnp.einsum(
            "qhd,khd->hqk", grad_heads, value_all, preferred_element_type=jnp.float32
        )
        weighted = attend * grad_probs
        row_delta = jnp.sum(weighted, axis=2)
        first_sum = jnp.einsum(
            "hqk,khd->hqd",
            weighted.astype(jnp.bfloat16),
            key_all,
            preferred_element_type=jnp.float32,
        )
        second_sum = jnp.einsum(
            "hqk,khd->hqd", attend.astype(jnp.bfloat16), key_all, preferred_element_type=jnp.float32
        )
        query_grad = first_sum - row_delta[:, :, None] * second_sum
        query_grad = jnp.transpose(query_grad, (1, 0, 2)).reshape(row_count, cols)
        query_done = (query_grad * factor[None, :]).astype(jnp.bfloat16)

    with jax.named_scope("gather_row_stats"):
        stats = jnp.stack([log_total, row_delta], axis=0)
        stats, qg_ahead, qg_behind = lax.optimization_barrier((stats, qg_ahead, qg_behind))
        qg_pieces = ring4_last(qg_z, qg_ahead, qg_behind, "y")
        sent = jnp.broadcast_to(stats[None], (shards,) + stats.shape)
        stats_all = lax.all_to_all(sent, ("z", "y"), 0, 0, tiled=False)

    with jax.named_scope("key_pass"):
        piece_rows = qg_pieces[0].shape[0]
        key_grad = jnp.zeros((row_count, cols), jnp.float32)
        value_grad = jnp.zeros((row_count, cols), jnp.float32)
        for ry, piece in enumerate(qg_pieces):
            source = qg_source[ry * z_size : (ry + 1) * z_size]
            place = block_positions(offsets[source], piece_rows)
            part_stats = stats_all[source]
            part_stats = jnp.transpose(part_stats, (1, 2, 0, 3)).reshape(
                2 * heads_here, piece_rows
            )
            part_k, part_v = key_pass(
                own_positions, keys, values, piece, place, part_stats, heads_here, head_width
            )
            key_grad = key_grad + part_k
            value_grad = value_grad + part_v
        key_done = key_grad.reshape(row_count, cols).astype(jnp.bfloat16)
        value_done = value_grad.reshape(row_count, cols).astype(jnp.bfloat16)

    with jax.named_scope("back_projection"):
        back_sum = jnp.dot(query_done, w_query, preferred_element_type=jnp.float32)
        back_sum = back_sum + jnp.dot(key_done, w_key, preferred_element_type=jnp.float32)
        back_sum = back_sum + jnp.dot(value_done, w_value, preferred_element_type=jnp.float32)
        scaled = back_sum * norm_gain[None, :]
        row_part = jnp.sum(widened * scaled, axis=1)
        chunks = scaled.reshape(row_count, tp_size, width_here).transpose(1, 0, 2)
        extra = jnp.zeros((tp_size, 1, width_here), jnp.float32)
        extra = extra.at[:, 0, :row_count].set(jnp.broadcast_to(row_part, (tp_size, row_count)))
        payload = jnp.concatenate([chunks, extra], axis=1)
        received = lax.all_to_all(payload, "tp", 0, 0, tiled=False)
        total = jnp.sum(received, axis=0)
        scaled_own = total[:row_count]
        row_dot = total[row_count, :row_count][:, None]

    with jax.named_scope("input_grads"):
        start_col = lax.axis_index("tp") * width_here
        own_inputs = inputs.astype(jnp.float32)
        branch = (
            inverse * scaled_own
            - own_inputs * inverse * inverse * inverse * row_dot / full_width
        )
        result = out_grads.astype(jnp.float32) + branch
    return result.astype(jnp.bfloat16)


def solution(mesh):
    seq_size = mesh.shape["seq"]
    devices = mesh.devices
    y_size = 4 if seq_size % 4 == 0 else 1
    split = Mesh(
        devices.reshape((seq_size // y_size, y_size) + devices.shape[1:]),
        ("z", "y", "tp", "dp"),
    )
    rows = P(("dp", "z", "y"), "tp")
    return jax.shard_map(
        per_device,
        mesh=split,
        in_specs=(
            rows,
            rows,
            P(),
            P("tp", None),
            P("tp", None),
            P("tp", None),
            P("tp", None),
            P(),
            P(),
        ),
        out_specs=rows,
        check_vma=False,
    )
```

```python
import math

import jax
import jax.numpy as jnp
import numpy as np
from jax import lax
from jax.sharding import Mesh
from jax.sharding import PartitionSpec as P

PIECE = 128

scale_base = 1.4426950408889634
masked_score = -1e30
norm_eps = 1e-06


def column_scale(query_scale, head_count):
    head_width = query_scale.shape[0]
    factor = scale_base / math.sqrt(head_width) * jax.nn.softplus(query_scale)
    return jnp.tile(factor, head_count)


def block_positions(offsets, rows):
    return (offsets[:, None] * PIECE + lax.iota(jnp.int32, PIECE)[None, :]).reshape(rows)


def ring_steps(size):
    return size // 2, (size - 1) // 2


def shift(data, axis, size, step):
    return lax.ppermute(data, axis, [(i, (i + step) % size) for i in range(size)])


def ring_gather(data, axis, size):
    forward, backward = ring_steps(size)
    pieces = [None] * size
    pieces[0] = data
    ahead = behind = data
    for step in range(max(forward, backward)):
        if step < forward:
            ahead = shift(ahead, axis, size, 1)
            pieces[size - 1 - step] = ahead
        if step < backward:
            behind = shift(behind, axis, size, -1)
            pieces[1 + step] = behind
    return pieces


def ring4_first(data, axis):
    return shift(data, axis, 4, 1), shift(data, axis, 4, -1)


def ring4_last(data, ahead, behind, axis):
    half = data.shape[0] // 2
    far = jnp.concatenate(
        [shift(ahead[:half], axis, 4, 1), shift(behind[half:], axis, 4, -1)], axis=0
    )
    return [data, behind, far, ahead]


def per_device(
    inputs, out_grads, norm_gain, w_query, w_key, w_value, w_output, query_scale, offsets
):
    row_count, width_here = inputs.shape
    head_width = query_scale.shape[0]
    heads_here = w_query.shape[0] // head_width
    cols = heads_here * head_width
    tp_size = lax.axis_size("tp")
    y_size = lax.axis_size("y")
    shards = offsets.shape[0]
    all_rows = shards * row_count
    contract = (((1,), (1,)), ((), ()))

    with jax.named_scope("gather_features"):
        both = jnp.concatenate([inputs, out_grads], axis=1)
        gathered = lax.all_gather(both, "tp", axis=1, tiled=True)
        gathered = gathered.reshape(row_count, tp_size, 2, width_here)
        full_inputs = gathered[:, :, 0, :].reshape(row_count, tp_size * width_here)
        full_grads = gathered[:, :, 1, :].reshape(row_count, tp_size * width_here)
    full_width = full_inputs.shape[1]

    with jax.named_scope("projections"):
        widened = full_inputs.astype(jnp.float32)
        inverse = lax.rsqrt(jnp.mean(widened * widened, axis=1, keepdims=True) + norm_eps)
        normed = (widened * inverse * norm_gain[None, :]).astype(jnp.bfloat16)
        factor = column_scale(query_scale, heads_here)
        queries = (
            lax.dot_general(normed, w_query, contract, preferred_element_type=jnp.float32)
            * factor[None, :]
        ).astype(jnp.bfloat16)
        keys = lax.dot_general(normed, w_key, contract, preferred_element_type=jnp.float32).astype(
            jnp.bfloat16
        )
        values = lax.dot_general(
            normed, w_value, contract, preferred_element_type=jnp.float32
        ).astype(jnp.bfloat16)
        head_grads = lax.dot_general(
            full_grads, w_output, contract, preferred_element_type=jnp.float32
        ).astype(jnp.bfloat16)

    z_size = lax.axis_size("z")
    z_index = lax.axis_index("z")
    y_index = lax.axis_index("y")

    with jax.named_scope("gather_sequence"):
        kv = jnp.concatenate([keys, values], axis=1)
        qg = jnp.concatenate([queries, head_grads], axis=1)
        kv_ahead, kv_behind = ring4_first(kv, "y")
        kv_all = jnp.concatenate(ring4_last(kv, kv_ahead, kv_behind, "y"), axis=0)
        kv_all = lax.all_gather(kv_all, "z", axis=0, tiled=True)
        qg_z = jnp.concatenate(ring_gather(qg, "z", z_size), axis=0)
        qg_ahead, qg_behind = ring4_first(qg_z, "y")
        key_all = kv_all[:, :cols].reshape(all_rows, heads_here, head_width)
        value_all = kv_all[:, cols:].reshape(all_rows, heads_here, head_width)

    rel_z = lax.iota(jnp.int32, z_size)
    rel_y = lax.iota(jnp.int32, y_size)
    abs_z = (z_index + rel_z) % z_size
    abs_y = (y_index + rel_y) % y_size
    qg_source = (abs_z[None, :] * y_size + abs_y[:, None]).reshape(shards)
    kv_source = (lax.iota(jnp.int32, z_size)[:, None] * y_size + abs_y[None, :]).reshape(shards)
    key_positions = block_positions(offsets[kv_source], all_rows)
    seq_index = z_index * y_size + y_index
    own_positions = offsets[seq_index] * PIECE + lax.iota(jnp.int32, row_count)

    query_heads = queries.reshape(row_count, heads_here, head_width)
    grad_heads = head_grads.reshape(row_count, heads_here, head_width)
    key_heads = keys.reshape(row_count, heads_here, head_width)
    value_heads = values.reshape(row_count, heads_here, head_width)

    with jax.named_scope("query_pass"):
        scores = jnp.einsum(
            "qhd,khd->hqk", query_heads, key_all, preferred_element_type=jnp.float32
        )
        visible = key_positions[None, None, :] <= own_positions[None, :, None]
        masked = jnp.where(visible, scores, masked_score)
        row_peak = jnp.max(masked, axis=2)
        summed = jnp.sum(jnp.where(visible, jnp.exp(masked - row_peak[:, :, None]), 0.0), axis=2)
        log_total = row_peak + jnp.log(summed)
        attend = jnp.exp(jnp.where(visible, scores - log_total[:, :, None], masked_score))
        grad_probs = jnp.einsum(
            "qhd,khd->hqk", grad_heads, value_all, preferred_element_type=jnp.float32
        )
        weighted = attend * grad_probs
        row_delta = jnp.sum(weighted, axis=2)
        first_sum = jnp.einsum(
            "hqk,khd->hqd",
            weighted.astype(jnp.bfloat16),
            key_all,
            preferred_element_type=jnp.float32,
        )
        second_sum = jnp.einsum(
            "hqk,khd->hqd", attend.astype(jnp.bfloat16), key_all, preferred_element_type=jnp.float32
        )
        query_grad = first_sum - row_delta[:, :, None] * second_sum
        query_grad = jnp.transpose(query_grad, (1, 0, 2)).reshape(row_count, cols)
        query_done = (query_grad * factor[None, :]).astype(jnp.bfloat16)

    with jax.named_scope("gather_row_stats"):
        stats = jnp.stack([log_total, row_delta], axis=0)
        stats, qg_ahead, qg_behind = lax.optimization_barrier((stats, qg_ahead, qg_behind))
        qg_pieces = ring4_last(qg_z, qg_ahead, qg_behind, "y")
        sent = jnp.broadcast_to(stats[None], (shards,) + stats.shape)
        stats_all = lax.all_to_all(sent, ("z", "y"), 0, 0, tiled=False)

    with jax.named_scope("key_pass"):
        piece_rows = qg_pieces[0].shape[0]
        key_grad = jnp.zeros((row_count, heads_here, head_width), jnp.float32)
        value_grad = jnp.zeros((row_count, heads_here, head_width), jnp.float32)
        for ry, piece in enumerate(qg_pieces):
            source = qg_source[ry * z_size : (ry + 1) * z_size]
            query_part = piece[:, :cols].reshape(piece_rows, heads_here, head_width)
            grad_part = piece[:, cols:].reshape(piece_rows, heads_here, head_width)
            place = block_positions(offsets[source], piece_rows)
            part_stats = stats_all[source]
            log_part = jnp.transpose(part_stats[:, 0], (1, 0, 2)).reshape(heads_here, piece_rows)
            delta_part = jnp.transpose(part_stats[:, 1], (1, 0, 2)).reshape(
                heads_here, piece_rows
            )
            scores_t = jnp.einsum(
                "khd,qhd->hkq", key_heads, query_part, preferred_element_type=jnp.float32
            )
            visible_t = own_positions[None, :, None] <= place[None, None, :]
            attend_t = jnp.exp(
                jnp.where(visible_t, scores_t - log_part[:, None, :], masked_score)
            )
            grad_probs_t = jnp.einsum(
                "khd,qhd->hkq", value_heads, grad_part, preferred_element_type=jnp.float32
            )
            score_grad = (attend_t * (grad_probs_t - delta_part[:, None, :])).astype(
                jnp.bfloat16
            )
            key_grad = key_grad + jnp.einsum(
                "hkq,qhd->khd", score_grad, query_part, preferred_element_type=jnp.float32
            )
            value_grad = value_grad + jnp.einsum(
                "hkq,qhd->khd",
                attend_t.astype(jnp.bfloat16),
                grad_part,
                preferred_element_type=jnp.float32,
            )
        key_done = key_grad.reshape(row_count, cols).astype(jnp.bfloat16)
        value_done = value_grad.reshape(row_count, cols).astype(jnp.bfloat16)

    with jax.named_scope("back_projection"):
        back_sum = jnp.dot(query_done, w_query, preferred_element_type=jnp.float32)
        back_sum = back_sum + jnp.dot(key_done, w_key, preferred_element_type=jnp.float32)
        back_sum = back_sum + jnp.dot(value_done, w_value, preferred_element_type=jnp.float32)
        scaled = back_sum * norm_gain[None, :]
        row_part = jnp.sum(widened * scaled, axis=1)
        chunks = scaled.reshape(row_count, tp_size, width_here).transpose(1, 0, 2)
        extra = jnp.zeros((tp_size, 1, width_here), jnp.float32)
        extra = extra.at[:, 0, :row_count].set(jnp.broadcast_to(row_part, (tp_size, row_count)))
        payload = jnp.concatenate([chunks, extra], axis=1)
        received = lax.all_to_all(payload, "tp", 0, 0, tiled=False)
        total = jnp.sum(received, axis=0)
        scaled_own = total[:row_count]
        row_dot = total[row_count, :row_count][:, None]

    with jax.named_scope("input_grads"):
        start_col = lax.axis_index("tp") * width_here
        own_inputs = inputs.astype(jnp.float32)
        branch = (
            inverse * scaled_own
            - own_inputs * inverse * inverse * inverse * row_dot / full_width
        )
        result = out_grads.astype(jnp.float32) + branch
    return result.astype(jnp.bfloat16)


def solution(mesh):
    seq_size = mesh.shape["seq"]
    devices = mesh.devices
    y_size = 4 if seq_size % 4 == 0 else 1
    split = Mesh(
        devices.reshape((seq_size // y_size, y_size) + devices.shape[1:]),
        ("z", "y", "tp", "dp"),
    )
    rows = P(("dp", "z", "y"), "tp")
    return jax.shard_map(
        per_device,
        mesh=split,
        in_specs=(
            rows,
            rows,
            P(),
            P("tp", None),
            P("tp", None),
            P("tp", None),
            P("tp", None),
            P(),
            P(),
        ),
        out_specs=rows,
        check_vma=False,
    )
```

```python
import math

import jax
import jax.numpy as jnp
import numpy as np
from jax import lax
from jax.sharding import Mesh
from jax.sharding import PartitionSpec as P

PIECE = 128

scale_base = 1.4426950408889634
masked_score = -1e30
norm_eps = 1e-06


def column_scale(query_scale, head_count):
    head_width = query_scale.shape[0]
    factor = scale_base / math.sqrt(head_width) * jax.nn.softplus(query_scale)
    return jnp.tile(factor, head_count)


def block_positions(offsets, rows):
    return (offsets[:, None] * PIECE + lax.iota(jnp.int32, PIECE)[None, :]).reshape(rows)


def ring_steps(size):
    return size // 2, (size - 1) // 2


def shift(data, axis, size, step):
    return lax.ppermute(data, axis, [(i, (i + step) % size) for i in range(size)])


def ring_gather(data, axis, size):
    forward, backward = ring_steps(size)
    pieces = [None] * size
    pieces[0] = data
    ahead = behind = data
    for step in range(max(forward, backward)):
        if step < forward:
            ahead = shift(ahead, axis, size, 1)
            pieces[size - 1 - step] = ahead
        if step < backward:
            behind = shift(behind, axis, size, -1)
            pieces[1 + step] = behind
    return pieces


def ring4_first(data, axis):
    return shift(data, axis, 4, 1), shift(data, axis, 4, -1)


def ring4_last(data, ahead, behind, axis):
    half = data.shape[0] // 2
    far = jnp.concatenate(
        [shift(ahead[:half], axis, 4, 1), shift(behind[half:], axis, 4, -1)], axis=0
    )
    return [data, behind, far, ahead]


def per_device(
    inputs, out_grads, norm_gain, w_query, w_key, w_value, w_output, query_scale, offsets
):
    row_count, width_here = inputs.shape
    head_width = query_scale.shape[0]
    heads_here = w_query.shape[0] // head_width
    cols = heads_here * head_width
    tp_size = lax.axis_size("tp")
    y_size = lax.axis_size("y")
    shards = offsets.shape[0]
    all_rows = shards * row_count
    contract = (((1,), (1,)), ((), ()))

    with jax.named_scope("gather_features"):
        both = jnp.concatenate([inputs, out_grads], axis=1)
        gathered = lax.all_gather(both, "tp", axis=1, tiled=True)
        gathered = gathered.reshape(row_count, tp_size, 2, width_here)
        full_inputs = gathered[:, :, 0, :].reshape(row_count, tp_size * width_here)
        full_grads = gathered[:, :, 1, :].reshape(row_count, tp_size * width_here)
    full_width = full_inputs.shape[1]

    with jax.named_scope("projections"):
        widened = full_inputs.astype(jnp.float32)
        inverse = lax.rsqrt(jnp.mean(widened * widened, axis=1, keepdims=True) + norm_eps)
        normed = (widened * inverse * norm_gain[None, :]).astype(jnp.bfloat16)
        factor = column_scale(query_scale, heads_here)
        queries = (
            lax.dot_general(normed, w_query, contract, preferred_element_type=jnp.float32)
            * factor[None, :]
        ).astype(jnp.bfloat16)
        keys = lax.dot_general(normed, w_key, contract, preferred_element_type=jnp.float32).astype(
            jnp.bfloat16
        )
        values = lax.dot_general(
            normed, w_value, contract, preferred_element_type=jnp.float32
        ).astype(jnp.bfloat16)
        head_grads = lax.dot_general(
            full_grads, w_output, contract, preferred_element_type=jnp.float32
        ).astype(jnp.bfloat16)

    z_size = lax.axis_size("z")
    z_index = lax.axis_index("z")
    y_index = lax.axis_index("y")

    with jax.named_scope("gather_sequence"):
        kv = jnp.concatenate([keys, values], axis=1)
        qg = jnp.concatenate([queries, head_grads], axis=1)
        kv_all = lax.all_gather(kv, "y", axis=0, tiled=True)
        kv_all = lax.all_gather(kv_all, "z", axis=0, tiled=True)
        qg_z = jnp.concatenate(ring_gather(qg, "z", z_size), axis=0)
        qg_ahead, qg_behind = ring4_first(qg_z, "y")
        key_all = kv_all[:, :cols].reshape(all_rows, heads_here, head_width)
        value_all = kv_all[:, cols:].reshape(all_rows, heads_here, head_width)

    rel_z = lax.iota(jnp.int32, z_size)
    rel_y = lax.iota(jnp.int32, y_size)
    abs_z = (z_index + rel_z) % z_size
    abs_y = (y_index + rel_y) % y_size
    qg_source = (abs_z[None, :] * y_size + abs_y[:, None]).reshape(shards)
    key_positions = block_positions(offsets, all_rows)
    seq_index = z_index * y_size + y_index
    own_positions = offsets[seq_index] * PIECE + lax.iota(jnp.int32, row_count)

    query_heads = queries.reshape(row_count, heads_here, head_width)
    grad_heads = head_grads.reshape(row_count, heads_here, head_width)
    key_heads = keys.reshape(row_count, heads_here, head_width)
    value_heads = values.reshape(row_count, heads_here, head_width)

    with jax.named_scope("query_pass"):
        scores = jnp.einsum(
            "qhd,khd->hqk", query_heads, key_all, preferred_element_type=jnp.float32
        )
        visible = key_positions[None, None, :] <= own_positions[None, :, None]
        masked = jnp.where(visible, scores, masked_score)
        row_peak = jnp.max(masked, axis=2)
        summed = jnp.sum(jnp.where(visible, jnp.exp(masked - row_peak[:, :, None]), 0.0), axis=2)
        log_total = row_peak + jnp.log(summed)
        attend = jnp.exp(jnp.where(visible, scores - log_total[:, :, None], masked_score))
        grad_probs = jnp.einsum(
            "qhd,khd->hqk", grad_heads, value_all, preferred_element_type=jnp.float32
        )
        weighted = attend * grad_probs
        row_delta = jnp.sum(weighted, axis=2)
        first_sum = jnp.einsum(
            "hqk,khd->hqd",
            weighted.astype(jnp.bfloat16),
            key_all,
            preferred_element_type=jnp.float32,
        )
        second_sum = jnp.einsum(
            "hqk,khd->hqd", attend.astype(jnp.bfloat16), key_all, preferred_element_type=jnp.float32
        )
        query_grad = first_sum - row_delta[:, :, None] * second_sum
        query_grad = jnp.transpose(query_grad, (1, 0, 2)).reshape(row_count, cols)
        query_done = (query_grad * factor[None, :]).astype(jnp.bfloat16)

    with jax.named_scope("gather_row_stats"):
        stats = jnp.stack([log_total, row_delta], axis=0)
        stats, qg_ahead, qg_behind = lax.optimization_barrier((stats, qg_ahead, qg_behind))
        qg_pieces = ring4_last(qg_z, qg_ahead, qg_behind, "y")
        sent = jnp.broadcast_to(stats[None], (shards,) + stats.shape)
        stats_all = lax.all_to_all(sent, ("z", "y"), 0, 0, tiled=False)

    with jax.named_scope("key_pass"):
        piece_rows = qg_pieces[0].shape[0]
        key_grad = jnp.zeros((row_count, heads_here, head_width), jnp.float32)
        value_grad = jnp.zeros((row_count, heads_here, head_width), jnp.float32)
        for ry, piece in enumerate(qg_pieces):
            source = qg_source[ry * z_size : (ry + 1) * z_size]
            query_part = piece[:, :cols].reshape(piece_rows, heads_here, head_width)
            grad_part = piece[:, cols:].reshape(piece_rows, heads_here, head_width)
            place = block_positions(offsets[source], piece_rows)
            part_stats = stats_all[source]
            log_part = jnp.transpose(part_stats[:, 0], (1, 0, 2)).reshape(heads_here, piece_rows)
            delta_part = jnp.transpose(part_stats[:, 1], (1, 0, 2)).reshape(
                heads_here, piece_rows
            )
            scores_t = jnp.einsum(
                "qhd,khd->hqk", query_part, key_heads, preferred_element_type=jnp.float32
            )
            visible_t = own_positions[None, None, :] <= place[None, :, None]
            attend_t = jnp.exp(
                jnp.where(visible_t, scores_t - log_part[:, :, None], masked_score)
            )
            grad_probs_t = jnp.einsum(
                "qhd,khd->hqk", grad_part, value_heads, preferred_element_type=jnp.float32
            )
            score_grad = (attend_t * (grad_probs_t - delta_part[:, :, None])).astype(
                jnp.bfloat16
            )
            key_grad = key_grad + jnp.einsum(
                "hqk,qhd->khd", score_grad, query_part, preferred_element_type=jnp.float32
            )
            value_grad = value_grad + jnp.einsum(
                "hqk,qhd->khd",
                attend_t.astype(jnp.bfloat16),
                grad_part,
                preferred_element_type=jnp.float32,
            )
        key_done = key_grad.reshape(row_count, cols).astype(jnp.bfloat16)
        value_done = value_grad.reshape(row_count, cols).astype(jnp.bfloat16)

    with jax.named_scope("back_projection"):
        back_sum = jnp.dot(query_done, w_query, preferred_element_type=jnp.float32)
        back_sum = back_sum + jnp.dot(key_done, w_key, preferred_element_type=jnp.float32)
        back_sum = back_sum + jnp.dot(value_done, w_value, preferred_element_type=jnp.float32)
        scaled = back_sum * norm_gain[None, :]
        row_part = jnp.sum(widened * scaled, axis=1)
        chunks = scaled.reshape(row_count, tp_size, width_here).transpose(1, 0, 2)
        extra = jnp.zeros((tp_size, 1, width_here), jnp.float32)
        extra = extra.at[:, 0, :row_count].set(jnp.broadcast_to(row_part, (tp_size, row_count)))
        payload = jnp.concatenate([chunks, extra], axis=1)
        received = lax.all_to_all(payload, "tp", 0, 0, tiled=False)
        total = jnp.sum(received, axis=0)
        scaled_own = total[:row_count]
        row_dot = total[row_count, :row_count][:, None]

    with jax.named_scope("input_grads"):
        start_col = lax.axis_index("tp") * width_here
        own_inputs = inputs.astype(jnp.float32)
        branch = (
            inverse * scaled_own
            - own_inputs * inverse * inverse * inverse * row_dot / full_width
        )
        result = out_grads.astype(jnp.float32) + branch
    return result.astype(jnp.bfloat16)


def solution(mesh):
    seq_size = mesh.shape["seq"]
    devices = mesh.devices
    y_size = 4 if seq_size % 4 == 0 else 1
    split = Mesh(
        devices.reshape((seq_size // y_size, y_size) + devices.shape[1:]),
        ("z", "y", "tp", "dp"),
    )
    rows = P(("dp", "z", "y"), "tp")
    return jax.shard_map(
        per_device,
        mesh=split,
        in_specs=(
            rows,
            rows,
            P(),
            P("tp", None),
            P("tp", None),
            P("tp", None),
            P("tp", None),
            P(),
            P(),
        ),
        out_specs=rows,
        check_vma=False,
    )
```

```python
import math

import jax
import jax.numpy as jnp
import numpy as np
from jax import lax
from jax.sharding import Mesh
from jax.sharding import PartitionSpec as P

PIECE = 128

scale_base = 1.4426950408889634
masked_score = -1e30
norm_eps = 1e-06


def column_scale(query_scale, head_count):
    head_width = query_scale.shape[0]
    factor = scale_base / math.sqrt(head_width) * jax.nn.softplus(query_scale)
    return jnp.tile(factor, head_count)


def block_positions(offsets, rows):
    return (offsets[:, None] * PIECE + lax.iota(jnp.int32, PIECE)[None, :]).reshape(rows)


def ring_steps(size):
    return size // 2, (size - 1) // 2


def shift(data, axis, size, step):
    return lax.ppermute(data, axis, [(i, (i + step) % size) for i in range(size)])


def ring_gather(data, axis, size):
    forward, backward = ring_steps(size)
    pieces = [None] * size
    pieces[0] = data
    ahead = behind = data
    for step in range(max(forward, backward)):
        if step < forward:
            ahead = shift(ahead, axis, size, 1)
            pieces[size - 1 - step] = ahead
        if step < backward:
            behind = shift(behind, axis, size, -1)
            pieces[1 + step] = behind
    return pieces


def ring4_first(data, axis):
    return shift(data, axis, 4, 1), shift(data, axis, 4, -1)


def ring4_last(data, ahead, behind, axis):
    half = data.shape[0] // 2
    far = jnp.concatenate(
        [shift(ahead[:half], axis, 4, 1), shift(behind[half:], axis, 4, -1)], axis=0
    )
    return [data, behind, far, ahead]


def per_device(
    inputs, out_grads, norm_gain, w_query, w_key, w_value, w_output, query_scale, offsets
):
    row_count, width_here = inputs.shape
    head_width = query_scale.shape[0]
    heads_here = w_query.shape[0] // head_width
    cols = heads_here * head_width
    tp_size = lax.axis_size("tp")
    y_size = lax.axis_size("y")
    shards = offsets.shape[0]
    all_rows = shards * row_count
    contract = (((1,), (1,)), ((), ()))

    with jax.named_scope("gather_features"):
        both = jnp.concatenate([inputs, out_grads], axis=1)
        gathered = lax.all_gather(both, "tp", axis=1, tiled=True)
        gathered = gathered.reshape(row_count, tp_size, 2, width_here)
        full_inputs = gathered[:, :, 0, :].reshape(row_count, tp_size * width_here)
        full_grads = gathered[:, :, 1, :].reshape(row_count, tp_size * width_here)
    full_width = full_inputs.shape[1]

    with jax.named_scope("projections"):
        widened = full_inputs.astype(jnp.float32)
        inverse = lax.rsqrt(jnp.mean(widened * widened, axis=1, keepdims=True) + norm_eps)
        normed = (widened * inverse * norm_gain[None, :]).astype(jnp.bfloat16)
        factor = column_scale(query_scale, heads_here)
        queries = (
            lax.dot_general(normed, w_query, contract, preferred_element_type=jnp.float32)
            * factor[None, :]
        ).astype(jnp.bfloat16)
        keys = lax.dot_general(normed, w_key, contract, preferred_element_type=jnp.float32).astype(
            jnp.bfloat16
        )
        values = lax.dot_general(
            normed, w_value, contract, preferred_element_type=jnp.float32
        ).astype(jnp.bfloat16)
        head_grads = lax.dot_general(
            full_grads, w_output, contract, preferred_element_type=jnp.float32
        ).astype(jnp.bfloat16)

    z_size = lax.axis_size("z")
    z_index = lax.axis_index("z")
    y_index = lax.axis_index("y")

    with jax.named_scope("gather_sequence"):
        kv = jnp.concatenate([keys, values], axis=1)
        qg = jnp.concatenate([queries, head_grads], axis=1)
        kv_all = lax.all_gather(kv, "y", axis=0, tiled=True)
        kv_all = lax.all_gather(kv_all, "z", axis=0, tiled=True)
        qg_z = jnp.concatenate(ring_gather(qg, "z", z_size), axis=0)
        qg_ahead, qg_behind = ring4_first(qg_z, "y")
        key_all = kv_all[:, :cols].reshape(all_rows, heads_here, head_width)
        value_all = kv_all[:, cols:].reshape(all_rows, heads_here, head_width)

    rel_z = lax.iota(jnp.int32, z_size)
    rel_y = lax.iota(jnp.int32, y_size)
    abs_z = (z_index + rel_z) % z_size
    abs_y = (y_index + rel_y) % y_size
    qg_source = (abs_z[None, :] * y_size + abs_y[:, None]).reshape(shards)
    key_positions = block_positions(offsets, all_rows)
    seq_index = z_index * y_size + y_index
    own_positions = offsets[seq_index] * PIECE + lax.iota(jnp.int32, row_count)

    query_heads = queries.reshape(row_count, heads_here, head_width)
    grad_heads = head_grads.reshape(row_count, heads_here, head_width)
    key_heads = keys.reshape(row_count, heads_here, head_width)
    value_heads = values.reshape(row_count, heads_here, head_width)

    with jax.named_scope("query_pass"):
        scores = jnp.einsum(
            "qhd,khd->hqk", query_heads, key_all, preferred_element_type=jnp.float32
        )
        visible = key_positions[None, None, :] <= own_positions[None, :, None]
        masked = jnp.where(visible, scores, masked_score)
        row_peak = jnp.max(masked, axis=2)
        summed = jnp.sum(jnp.where(visible, jnp.exp(masked - row_peak[:, :, None]), 0.0), axis=2)
        log_total = row_peak + jnp.log(summed)
        attend = jnp.exp(jnp.where(visible, scores - log_total[:, :, None], masked_score))
        grad_probs = jnp.einsum(
            "qhd,khd->hqk", grad_heads, value_all, preferred_element_type=jnp.float32
        )
        weighted = attend * grad_probs
        row_delta = jnp.sum(weighted, axis=2)
        first_sum = jnp.einsum(
            "hqk,khd->hqd",
            weighted.astype(jnp.bfloat16),
            key_all,
            preferred_element_type=jnp.float32,
        )
        second_sum = jnp.einsum(
            "hqk,khd->hqd", attend.astype(jnp.bfloat16), key_all, preferred_element_type=jnp.float32
        )
        query_grad = first_sum - row_delta[:, :, None] * second_sum
        query_grad = jnp.transpose(query_grad, (1, 0, 2)).reshape(row_count, cols)
        query_done = (query_grad * factor[None, :]).astype(jnp.bfloat16)

    with jax.named_scope("gather_row_stats"):
        stats = jnp.stack([log_total, row_delta], axis=0)
        qg_pieces = ring4_last(qg_z, qg_ahead, qg_behind, "y")
        sent = jnp.broadcast_to(stats[None], (shards,) + stats.shape)
        stats_all = lax.all_to_all(sent, ("z", "y"), 0, 0, tiled=False)

    with jax.named_scope("key_pass"):
        piece_rows = qg_pieces[0].shape[0]
        key_grad = jnp.zeros((row_count, heads_here, head_width), jnp.float32)
        value_grad = jnp.zeros((row_count, heads_here, head_width), jnp.float32)
        for ry, piece in enumerate(qg_pieces):
            source = qg_source[ry * z_size : (ry + 1) * z_size]
            query_part = piece[:, :cols].reshape(piece_rows, heads_here, head_width)
            grad_part = piece[:, cols:].reshape(piece_rows, heads_here, head_width)
            place = block_positions(offsets[source], piece_rows)
            part_stats = stats_all[source]
            log_part = jnp.transpose(part_stats[:, 0], (1, 0, 2)).reshape(heads_here, piece_rows)
            delta_part = jnp.transpose(part_stats[:, 1], (1, 0, 2)).reshape(
                heads_here, piece_rows
            )
            scores_t = jnp.einsum(
                "khd,qhd->hkq", key_heads, query_part, preferred_element_type=jnp.float32
            )
            visible_t = own_positions[None, :, None] <= place[None, None, :]
            attend_t = jnp.exp(
                jnp.where(visible_t, scores_t - log_part[:, None, :], masked_score)
            )
            grad_probs_t = jnp.einsum(
                "khd,qhd->hkq", value_heads, grad_part, preferred_element_type=jnp.float32
            )
            score_grad = (attend_t * (grad_probs_t - delta_part[:, None, :])).astype(
                jnp.bfloat16
            )
            key_grad = key_grad + jnp.einsum(
                "hkq,qhd->khd", score_grad, query_part, preferred_element_type=jnp.float32
            )
            value_grad = value_grad + jnp.einsum(
                "hkq,qhd->khd",
                attend_t.astype(jnp.bfloat16),
                grad_part,
                preferred_element_type=jnp.float32,
            )
        key_done = key_grad.reshape(row_count, cols).astype(jnp.bfloat16)
        value_done = value_grad.reshape(row_count, cols).astype(jnp.bfloat16)

    with jax.named_scope("back_projection"):
        back_sum = jnp.dot(query_done, w_query, preferred_element_type=jnp.float32)
        back_sum = back_sum + jnp.dot(key_done, w_key, preferred_element_type=jnp.float32)
        back_sum = back_sum + jnp.dot(value_done, w_value, preferred_element_type=jnp.float32)
        scaled = back_sum * norm_gain[None, :]
        row_part = jnp.sum(widened * scaled, axis=1)
        chunks = scaled.reshape(row_count, tp_size, width_here).transpose(1, 0, 2)
        extra = jnp.zeros((tp_size, 1, width_here), jnp.float32)
        extra = extra.at[:, 0, :row_count].set(jnp.broadcast_to(row_part, (tp_size, row_count)))
        payload = jnp.concatenate([chunks, extra], axis=1)
        received = lax.all_to_all(payload, "tp", 0, 0, tiled=False)
        total = jnp.sum(received, axis=0)
        scaled_own = total[:row_count]
        row_dot = total[row_count, :row_count][:, None]

    with jax.named_scope("input_grads"):
        start_col = lax.axis_index("tp") * width_here
        own_inputs = inputs.astype(jnp.float32)
        branch = (
            inverse * scaled_own
            - own_inputs * inverse * inverse * inverse * row_dot / full_width
        )
        result = out_grads.astype(jnp.float32) + branch
    return result.astype(jnp.bfloat16)


def solution(mesh):
    seq_size = mesh.shape["seq"]
    devices = mesh.devices
    y_size = 4 if seq_size % 4 == 0 else 1
    split = Mesh(
        devices.reshape((seq_size // y_size, y_size) + devices.shape[1:]),
        ("z", "y", "tp", "dp"),
    )
    rows = P(("dp", "z", "y"), "tp")
    return jax.shard_map(
        per_device,
        mesh=split,
        in_specs=(
            rows,
            rows,
            P(),
            P("tp", None),
            P("tp", None),
            P("tp", None),
            P("tp", None),
            P(),
            P(),
        ),
        out_specs=rows,
        check_vma=False,
    )
```

```python
import math

import jax
import jax.numpy as jnp
import numpy as np
from jax import lax
from jax.sharding import Mesh
from jax.sharding import PartitionSpec as P

PIECE = 128

scale_base = 1.4426950408889634
masked_score = -1e30
norm_eps = 1e-06


def column_scale(query_scale, head_count):
    head_width = query_scale.shape[0]
    factor = scale_base / math.sqrt(head_width) * jax.nn.softplus(query_scale)
    return jnp.tile(factor, head_count)


def block_positions(offsets, rows):
    return (offsets[:, None] * PIECE + lax.iota(jnp.int32, PIECE)[None, :]).reshape(rows)


def ring_steps(size):
    return size // 2, (size - 1) // 2


def shift(data, axis, size, step):
    return lax.ppermute(data, axis, [(i, (i + step) % size) for i in range(size)])


def ring_gather(data, axis, size):
    forward, backward = ring_steps(size)
    pieces = [None] * size
    pieces[0] = data
    ahead = behind = data
    for step in range(max(forward, backward)):
        if step < forward:
            ahead = shift(ahead, axis, size, 1)
            pieces[size - 1 - step] = ahead
        if step < backward:
            behind = shift(behind, axis, size, -1)
            pieces[1 + step] = behind
    return pieces


def ring4_first(data, axis):
    return shift(data, axis, 4, 1), shift(data, axis, 4, -1)


def ring4_last(data, ahead, behind, axis):
    half = data.shape[0] // 2
    far = jnp.concatenate(
        [shift(ahead[:half], axis, 4, 1), shift(behind[half:], axis, 4, -1)], axis=0
    )
    return [data, behind, far, ahead]


def per_device(
    inputs, out_grads, norm_gain, w_query, w_key, w_value, w_output, query_scale, offsets
):
    row_count, width_here = inputs.shape
    head_width = query_scale.shape[0]
    heads_here = w_query.shape[0] // head_width
    cols = heads_here * head_width
    tp_size = lax.axis_size("tp")
    y_size = lax.axis_size("y")
    shards = offsets.shape[0]
    all_rows = shards * row_count
    contract = (((1,), (1,)), ((), ()))

    with jax.named_scope("gather_features"):
        both = jnp.concatenate([inputs, out_grads], axis=1)
        gathered = lax.all_gather(both, "tp", axis=1, tiled=True)
        gathered = gathered.reshape(row_count, tp_size, 2, width_here)
        full_inputs = gathered[:, :, 0, :].reshape(row_count, tp_size * width_here)
        full_grads = gathered[:, :, 1, :].reshape(row_count, tp_size * width_here)
    full_width = full_inputs.shape[1]

    with jax.named_scope("projections"):
        widened = full_inputs.astype(jnp.float32)
        inverse = lax.rsqrt(jnp.mean(widened * widened, axis=1, keepdims=True) + norm_eps)
        normed = (widened * inverse * norm_gain[None, :]).astype(jnp.bfloat16)
        factor = column_scale(query_scale, heads_here)
        queries = (
            lax.dot_general(normed, w_query, contract, preferred_element_type=jnp.float32)
            * factor[None, :]
        ).astype(jnp.bfloat16)
        keys = lax.dot_general(normed, w_key, contract, preferred_element_type=jnp.float32).astype(
            jnp.bfloat16
        )
        values = lax.dot_general(
            normed, w_value, contract, preferred_element_type=jnp.float32
        ).astype(jnp.bfloat16)
        head_grads = lax.dot_general(
            full_grads, w_output, contract, preferred_element_type=jnp.float32
        ).astype(jnp.bfloat16)

    z_size = lax.axis_size("z")
    z_index = lax.axis_index("z")
    y_index = lax.axis_index("y")

    with jax.named_scope("gather_sequence"):
        kv = jnp.concatenate([keys, values], axis=1)
        qg = jnp.concatenate([queries, head_grads], axis=1)
        kv_all = lax.all_gather(kv, "y", axis=0, tiled=True)
        kv_all = lax.all_gather(kv_all, "z", axis=0, tiled=True)
        qg_z = jnp.concatenate(ring_gather(qg, "z", z_size), axis=0)
        qg_ahead, qg_behind = ring4_first(qg_z, "y")
        key_all = kv_all[:, :cols].reshape(all_rows, heads_here, head_width)
        value_all = kv_all[:, cols:].reshape(all_rows, heads_here, head_width)

    rel_z = lax.iota(jnp.int32, z_size)
    rel_y = lax.iota(jnp.int32, y_size)
    abs_z = (z_index + rel_z) % z_size
    abs_y = (y_index + rel_y) % y_size
    qg_source = (abs_z[None, :] * y_size + abs_y[:, None]).reshape(shards)
    key_positions = block_positions(offsets, all_rows)
    seq_index = z_index * y_size + y_index
    own_positions = offsets[seq_index] * PIECE + lax.iota(jnp.int32, row_count)

    query_heads = queries.reshape(row_count, heads_here, head_width)
    grad_heads = head_grads.reshape(row_count, heads_here, head_width)
    key_heads = keys.reshape(row_count, heads_here, head_width)
    value_heads = values.reshape(row_count, heads_here, head_width)

    with jax.named_scope("query_pass"):
        scores = jnp.einsum(
            "qhd,khd->hqk", query_heads, key_all, preferred_element_type=jnp.float32
        )
        visible = key_positions[None, None, :] <= own_positions[None, :, None]
        masked = jnp.where(visible, scores, masked_score)
        row_peak = jnp.max(masked, axis=2)
        summed = jnp.sum(jnp.where(visible, jnp.exp(masked - row_peak[:, :, None]), 0.0), axis=2)
        log_total = row_peak + jnp.log(summed)
        attend = jnp.exp(jnp.where(visible, scores - log_total[:, :, None], masked_score))
        grad_probs = jnp.einsum(
            "qhd,khd->hqk", grad_heads, value_all, preferred_element_type=jnp.float32
        )
        weighted = attend * grad_probs
        row_delta = jnp.sum(weighted, axis=2)
        first_sum = jnp.einsum(
            "hqk,khd->hqd",
            weighted.astype(jnp.bfloat16),
            key_all,
            preferred_element_type=jnp.float32,
        )
        second_sum = jnp.einsum(
            "hqk,khd->hqd", attend.astype(jnp.bfloat16), key_all, preferred_element_type=jnp.float32
        )
        query_grad = first_sum - row_delta[:, :, None] * second_sum
        query_grad = jnp.transpose(query_grad, (1, 0, 2)).reshape(row_count, cols)
        query_done = (query_grad * factor[None, :]).astype(jnp.bfloat16)

    with jax.named_scope("gather_row_stats"):
        stats = jnp.stack([log_total, row_delta], axis=0)
        stats, qg_ahead, qg_behind = lax.optimization_barrier((stats, qg_ahead, qg_behind))
        qg_pieces = ring4_last(qg_z, qg_ahead, qg_behind, "y")
        sent = jnp.broadcast_to(stats[None], (shards,) + stats.shape)
        stats_all = lax.all_to_all(sent, ("z", "y"), 0, 0, tiled=False)

    with jax.named_scope("key_pass"):
        piece_rows = qg_pieces[0].shape[0]
        key_grad = jnp.zeros((row_count, heads_here, head_width), jnp.float32)
        value_grad = jnp.zeros((row_count, heads_here, head_width), jnp.float32)
        for ry, piece in enumerate(qg_pieces):
            source = qg_source[ry * z_size : (ry + 1) * z_size]
            query_part = piece[:, :cols].reshape(piece_rows, heads_here, head_width)
            grad_part = piece[:, cols:].reshape(piece_rows, heads_here, head_width)
            place = block_positions(offsets[source], piece_rows)
            part_stats = stats_all[source]
            log_part = jnp.transpose(part_stats[:, 0], (1, 0, 2)).reshape(heads_here, piece_rows)
            delta_part = jnp.transpose(part_stats[:, 1], (1, 0, 2)).reshape(
                heads_here, piece_rows
            )
            scores_t = jnp.einsum(
                "khd,qhd->hkq", key_heads, query_part, preferred_element_type=jnp.float32
            )
            visible_t = own_positions[None, :, None] <= place[None, None, :]
            attend_t = jnp.exp(
                jnp.where(visible_t, scores_t - log_part[:, None, :], masked_score)
            )
            grad_probs_t = jnp.einsum(
                "khd,qhd->hkq", value_heads, grad_part, preferred_element_type=jnp.float32
            )
            score_grad = (attend_t * (grad_probs_t - delta_part[:, None, :])).astype(
                jnp.bfloat16
            )
            plain_t = attend_t.astype(jnp.bfloat16)
            score_grad, plain_t = lax.optimization_barrier((score_grad, plain_t))
            key_grad = key_grad + jnp.einsum(
                "hkq,qhd->khd", score_grad, query_part, preferred_element_type=jnp.float32
            )
            value_grad = value_grad + jnp.einsum(
                "hkq,qhd->khd",
                plain_t,
                grad_part,
                preferred_element_type=jnp.float32,
            )
        key_done = key_grad.reshape(row_count, cols).astype(jnp.bfloat16)
        value_done = value_grad.reshape(row_count, cols).astype(jnp.bfloat16)

    with jax.named_scope("back_projection"):
        back_sum = jnp.dot(query_done, w_query, preferred_element_type=jnp.float32)
        back_sum = back_sum + jnp.dot(key_done, w_key, preferred_element_type=jnp.float32)
        back_sum = back_sum + jnp.dot(value_done, w_value, preferred_element_type=jnp.float32)
        scaled = back_sum * norm_gain[None, :]
        row_part = jnp.sum(widened * scaled, axis=1)
        chunks = scaled.reshape(row_count, tp_size, width_here).transpose(1, 0, 2)
        extra = jnp.zeros((tp_size, 1, width_here), jnp.float32)
        extra = extra.at[:, 0, :row_count].set(jnp.broadcast_to(row_part, (tp_size, row_count)))
        payload = jnp.concatenate([chunks, extra], axis=1)
        received = lax.all_to_all(payload, "tp", 0, 0, tiled=False)
        total = jnp.sum(received, axis=0)
        scaled_own = total[:row_count]
        row_dot = total[row_count, :row_count][:, None]

    with jax.named_scope("input_grads"):
        start_col = lax.axis_index("tp") * width_here
        own_inputs = inputs.astype(jnp.float32)
        branch = (
            inverse * scaled_own
            - own_inputs * inverse * inverse * inverse * row_dot / full_width
        )
        result = out_grads.astype(jnp.float32) + branch
    return result.astype(jnp.bfloat16)


def solution(mesh):
    seq_size = mesh.shape["seq"]
    devices = mesh.devices
    y_size = 4 if seq_size % 4 == 0 else 1
    split = Mesh(
        devices.reshape((seq_size // y_size, y_size) + devices.shape[1:]),
        ("z", "y", "tp", "dp"),
    )
    rows = P(("dp", "z", "y"), "tp")
    return jax.shard_map(
        per_device,
        mesh=split,
        in_specs=(
            rows,
            rows,
            P(),
            P("tp", None),
            P("tp", None),
            P("tp", None),
            P("tp", None),
            P(),
            P(),
        ),
        out_specs=rows,
        check_vma=False,
    )
```

```python
import math

import jax
import jax.numpy as jnp
import numpy as np
from jax import lax
from jax.sharding import Mesh
from jax.sharding import PartitionSpec as P

PIECE = 128

scale_base = 1.4426950408889634
masked_score = -1e30
norm_eps = 1e-06


def column_scale(query_scale, head_count):
    head_width = query_scale.shape[0]
    factor = scale_base / math.sqrt(head_width) * jax.nn.softplus(query_scale)
    return jnp.tile(factor, head_count)


def block_positions(offsets, rows):
    return (offsets[:, None] * PIECE + lax.iota(jnp.int32, PIECE)[None, :]).reshape(rows)


def ring_steps(size):
    return size // 2, (size - 1) // 2


def shift(data, axis, size, step):
    return lax.ppermute(data, axis, [(i, (i + step) % size) for i in range(size)])


def ring_gather(data, axis, size):
    forward, backward = ring_steps(size)
    pieces = [None] * size
    pieces[0] = data
    ahead = behind = data
    for step in range(max(forward, backward)):
        if step < forward:
            ahead = shift(ahead, axis, size, 1)
            pieces[size - 1 - step] = ahead
        if step < backward:
            behind = shift(behind, axis, size, -1)
            pieces[1 + step] = behind
    return pieces


def ring4_first(data, axis):
    return shift(data, axis, 4, 1), shift(data, axis, 4, -1)


def ring4_last(data, ahead, behind, axis):
    half = data.shape[0] // 2
    far = jnp.concatenate(
        [shift(ahead[:half], axis, 4, 1), shift(behind[half:], axis, 4, -1)], axis=0
    )
    return [data, behind, far, ahead]


def per_device(
    inputs, out_grads, norm_gain, w_query, w_key, w_value, w_output, query_scale, offsets
):
    row_count, width_here = inputs.shape
    head_width = query_scale.shape[0]
    heads_here = w_query.shape[0] // head_width
    cols = heads_here * head_width
    tp_size = lax.axis_size("tp")
    y_size = lax.axis_size("y")
    shards = offsets.shape[0]
    all_rows = shards * row_count
    contract = (((1,), (1,)), ((), ()))

    with jax.named_scope("gather_features"):
        both = jnp.concatenate([inputs, out_grads], axis=1)
        gathered = lax.all_gather(both, "tp", axis=1, tiled=True)
        gathered = gathered.reshape(row_count, tp_size, 2, width_here)
        full_inputs = gathered[:, :, 0, :].reshape(row_count, tp_size * width_here)
        full_grads = gathered[:, :, 1, :].reshape(row_count, tp_size * width_here)
    full_width = full_inputs.shape[1]

    with jax.named_scope("projections"):
        widened = full_inputs.astype(jnp.float32)
        inverse = lax.rsqrt(jnp.mean(widened * widened, axis=1, keepdims=True) + norm_eps)
        normed = (widened * inverse * norm_gain[None, :]).astype(jnp.bfloat16)
        factor = column_scale(query_scale, heads_here)
        queries = (
            lax.dot_general(normed, w_query, contract, preferred_element_type=jnp.float32)
            * factor[None, :]
        ).astype(jnp.bfloat16)
        keys = lax.dot_general(normed, w_key, contract, preferred_element_type=jnp.float32).astype(
            jnp.bfloat16
        )
        values = lax.dot_general(
            normed, w_value, contract, preferred_element_type=jnp.float32
        ).astype(jnp.bfloat16)
        head_grads = lax.dot_general(
            full_grads, w_output, contract, preferred_element_type=jnp.float32
        ).astype(jnp.bfloat16)

    z_size = lax.axis_size("z")
    z_index = lax.axis_index("z")
    y_index = lax.axis_index("y")

    with jax.named_scope("gather_sequence"):
        kv = jnp.concatenate([keys, values], axis=1)
        qg = jnp.concatenate([queries, head_grads], axis=1)
        kv_all = lax.all_gather(kv, "y", axis=0, tiled=True)
        kv_all = lax.all_gather(kv_all, "z", axis=0, tiled=True)
        qg_z = jnp.concatenate(ring_gather(qg, "z", z_size), axis=0)
        qg_ahead, qg_behind = ring4_first(qg_z, "y")
        key_all = kv_all[:, :cols].reshape(all_rows, heads_here, head_width)
        value_all = kv_all[:, cols:].reshape(all_rows, heads_here, head_width)

    rel_z = lax.iota(jnp.int32, z_size)
    rel_y = lax.iota(jnp.int32, y_size)
    abs_z = (z_index + rel_z) % z_size
    abs_y = (y_index + rel_y) % y_size
    qg_source = (abs_z[None, :] * y_size + abs_y[:, None]).reshape(shards)
    key_positions = block_positions(offsets, all_rows)
    seq_index = z_index * y_size + y_index
    own_positions = offsets[seq_index] * PIECE + lax.iota(jnp.int32, row_count)

    query_heads = queries.reshape(row_count, heads_here, head_width)
    grad_heads = head_grads.reshape(row_count, heads_here, head_width)
    key_heads = keys.reshape(row_count, heads_here, head_width)
    value_heads = values.reshape(row_count, heads_here, head_width)

    with jax.named_scope("query_pass"):
        scores = jnp.einsum(
            "qhd,khd->hqk", query_heads, key_all, preferred_element_type=jnp.float32
        )
        visible = key_positions[None, None, :] <= own_positions[None, :, None]
        masked = jnp.where(visible, scores, masked_score)
        row_peak = jnp.max(masked, axis=2)
        summed = jnp.sum(jnp.where(visible, jnp.exp(masked - row_peak[:, :, None]), 0.0), axis=2)
        log_total = row_peak + jnp.log(summed)
        attend = jnp.exp(jnp.where(visible, scores - log_total[:, :, None], masked_score))
        grad_probs = jnp.einsum(
            "qhd,khd->hqk", grad_heads, value_all, preferred_element_type=jnp.float32
        )
        weighted = attend * grad_probs
        row_delta = jnp.sum(weighted, axis=2)
        weighted_bf = weighted.astype(jnp.bfloat16)
        plain = attend.astype(jnp.bfloat16)
        weighted_bf, plain, row_delta = lax.optimization_barrier((weighted_bf, plain, row_delta))
        first_sum = jnp.einsum(
            "hqk,khd->hqd", weighted_bf, key_all, preferred_element_type=jnp.float32
        )
        second_sum = jnp.einsum(
            "hqk,khd->hqd", plain, key_all, preferred_element_type=jnp.float32
        )
        query_grad = first_sum - row_delta[:, :, None] * second_sum
        query_grad = jnp.transpose(query_grad, (1, 0, 2)).reshape(row_count, cols)
        query_done = (query_grad * factor[None, :]).astype(jnp.bfloat16)

    with jax.named_scope("gather_row_stats"):
        stats = jnp.stack([log_total, row_delta], axis=0)
        stats, qg_ahead, qg_behind = lax.optimization_barrier((stats, qg_ahead, qg_behind))
        qg_pieces = ring4_last(qg_z, qg_ahead, qg_behind, "y")
        sent = jnp.broadcast_to(stats[None], (shards,) + stats.shape)
        stats_all = lax.all_to_all(sent, ("z", "y"), 0, 0, tiled=False)

    with jax.named_scope("key_pass"):
        piece_rows = qg_pieces[0].shape[0]
        key_grad = jnp.zeros((row_count, heads_here, head_width), jnp.float32)
        value_grad = jnp.zeros((row_count, heads_here, head_width), jnp.float32)
        for ry, piece in enumerate(qg_pieces):
            source = qg_source[ry * z_size : (ry + 1) * z_size]
            query_part = piece[:, :cols].reshape(piece_rows, heads_here, head_width)
            grad_part = piece[:, cols:].reshape(piece_rows, heads_here, head_width)
            place = block_positions(offsets[source], piece_rows)
            part_stats = stats_all[source]
            log_part = jnp.transpose(part_stats[:, 0], (1, 0, 2)).reshape(heads_here, piece_rows)
            delta_part = jnp.transpose(part_stats[:, 1], (1, 0, 2)).reshape(
                heads_here, piece_rows
            )
            scores_t = jnp.einsum(
                "khd,qhd->hkq", key_heads, query_part, preferred_element_type=jnp.float32
            )
            visible_t = own_positions[None, :, None] <= place[None, None, :]
            attend_t = jnp.exp(
                jnp.where(visible_t, scores_t - log_part[:, None, :], masked_score)
            )
            grad_probs_t = jnp.einsum(
                "khd,qhd->hkq", value_heads, grad_part, preferred_element_type=jnp.float32
            )
            score_grad = (attend_t * (grad_probs_t - delta_part[:, None, :])).astype(
                jnp.bfloat16
            )
            plain_t = attend_t.astype(jnp.bfloat16)
            score_grad, plain_t = lax.optimization_barrier((score_grad, plain_t))
            key_grad = key_grad + jnp.einsum(
                "hkq,qhd->khd", score_grad, query_part, preferred_element_type=jnp.float32
            )
            value_grad = value_grad + jnp.einsum(
                "hkq,qhd->khd",
                plain_t,
                grad_part,
                preferred_element_type=jnp.float32,
            )
        key_done = key_grad.reshape(row_count, cols).astype(jnp.bfloat16)
        value_done = value_grad.reshape(row_count, cols).astype(jnp.bfloat16)

    with jax.named_scope("back_projection"):
        back_sum = jnp.dot(query_done, w_query, preferred_element_type=jnp.float32)
        back_sum = back_sum + jnp.dot(key_done, w_key, preferred_element_type=jnp.float32)
        back_sum = back_sum + jnp.dot(value_done, w_value, preferred_element_type=jnp.float32)
        scaled = back_sum * norm_gain[None, :]
        row_part = jnp.sum(widened * scaled, axis=1)
        chunks = scaled.reshape(row_count, tp_size, width_here).transpose(1, 0, 2)
        extra = jnp.zeros((tp_size, 1, width_here), jnp.float32)
        extra = extra.at[:, 0, :row_count].set(jnp.broadcast_to(row_part, (tp_size, row_count)))
        payload = jnp.concatenate([chunks, extra], axis=1)
        received = lax.all_to_all(payload, "tp", 0, 0, tiled=False)
        total = jnp.sum(received, axis=0)
        scaled_own = total[:row_count]
        row_dot = total[row_count, :row_count][:, None]

    with jax.named_scope("input_grads"):
        start_col = lax.axis_index("tp") * width_here
        own_inputs = inputs.astype(jnp.float32)
        branch = (
            inverse * scaled_own
            - own_inputs * inverse * inverse * inverse * row_dot / full_width
        )
        result = out_grads.astype(jnp.float32) + branch
    return result.astype(jnp.bfloat16)


def solution(mesh):
    seq_size = mesh.shape["seq"]
    devices = mesh.devices
    y_size = 4 if seq_size % 4 == 0 else 1
    split = Mesh(
        devices.reshape((seq_size // y_size, y_size) + devices.shape[1:]),
        ("z", "y", "tp", "dp"),
    )
    rows = P(("dp", "z", "y"), "tp")
    return jax.shard_map(
        per_device,
        mesh=split,
        in_specs=(
            rows,
            rows,
            P(),
            P("tp", None),
            P("tp", None),
            P("tp", None),
            P("tp", None),
            P(),
            P(),
        ),
        out_specs=rows,
        check_vma=False,
    )
```

```python
import math

import jax
import jax.numpy as jnp
import numpy as np
from jax import lax
from jax.sharding import Mesh
from jax.sharding import PartitionSpec as P

PIECE = 128

scale_base = 1.4426950408889634
masked_score = -1e30
norm_eps = 1e-06


def column_scale(query_scale, head_count):
    head_width = query_scale.shape[0]
    factor = scale_base / math.sqrt(head_width) * jax.nn.softplus(query_scale)
    return jnp.tile(factor, head_count)


def block_positions(offsets, rows):
    return (offsets[:, None] * PIECE + lax.iota(jnp.int32, PIECE)[None, :]).reshape(rows)


def ring_steps(size):
    return size // 2, (size - 1) // 2


def shift(data, axis, size, step):
    return lax.ppermute(data, axis, [(i, (i + step) % size) for i in range(size)])


def ring_gather(data, axis, size):
    forward, backward = ring_steps(size)
    pieces = [None] * size
    pieces[0] = data
    ahead = behind = data
    for step in range(max(forward, backward)):
        if step < forward:
            ahead = shift(ahead, axis, size, 1)
            pieces[size - 1 - step] = ahead
        if step < backward:
            behind = shift(behind, axis, size, -1)
            pieces[1 + step] = behind
    return pieces


def ring4_first(data, axis):
    return shift(data, axis, 4, 1), shift(data, axis, 4, -1)


def ring4_last(data, ahead, behind, axis):
    half = data.shape[0] // 2
    far = jnp.concatenate(
        [shift(ahead[:half], axis, 4, 1), shift(behind[half:], axis, 4, -1)], axis=0
    )
    return [data, behind, far, ahead]


def per_device(
    inputs, out_grads, norm_gain, w_query, w_key, w_value, w_output, query_scale, offsets
):
    row_count, width_here = inputs.shape
    head_width = query_scale.shape[0]
    heads_here = w_query.shape[0] // head_width
    cols = heads_here * head_width
    tp_size = lax.axis_size("tp")
    y_size = lax.axis_size("y")
    shards = offsets.shape[0]
    all_rows = shards * row_count
    contract = (((1,), (1,)), ((), ()))

    with jax.named_scope("gather_features"):
        both = jnp.concatenate([inputs, out_grads], axis=1)
        gathered = lax.all_gather(both, "tp", axis=1, tiled=True)
        gathered = gathered.reshape(row_count, tp_size, 2, width_here)
        full_inputs = gathered[:, :, 0, :].reshape(row_count, tp_size * width_here)
        full_grads = gathered[:, :, 1, :].reshape(row_count, tp_size * width_here)
    full_width = full_inputs.shape[1]

    with jax.named_scope("projections"):
        widened = full_inputs.astype(jnp.float32)
        inverse = lax.rsqrt(jnp.mean(widened * widened, axis=1, keepdims=True) + norm_eps)
        normed = (widened * inverse * norm_gain[None, :]).astype(jnp.bfloat16)
        factor = column_scale(query_scale, heads_here)
        queries = (
            lax.dot_general(normed, w_query, contract, preferred_element_type=jnp.float32)
            * factor[None, :]
        ).astype(jnp.bfloat16)
        keys = lax.dot_general(normed, w_key, contract, preferred_element_type=jnp.float32).astype(
            jnp.bfloat16
        )
        values = lax.dot_general(
            normed, w_value, contract, preferred_element_type=jnp.float32
        ).astype(jnp.bfloat16)
        head_grads = lax.dot_general(
            full_grads, w_output, contract, preferred_element_type=jnp.float32
        ).astype(jnp.bfloat16)

    z_size = lax.axis_size("z")
    z_index = lax.axis_index("z")
    y_index = lax.axis_index("y")

    with jax.named_scope("gather_sequence"):
        kv = jnp.concatenate([keys, values], axis=1)
        qg = jnp.concatenate([queries, head_grads], axis=1)
        kv_all = lax.all_gather(kv, "y", axis=0, tiled=True)
        kv_all = lax.all_gather(kv_all, "z", axis=0, tiled=True)
        qg_z = jnp.concatenate(ring_gather(qg, "z", z_size), axis=0)
        qg_ahead, qg_behind = ring4_first(qg_z, "y")
        key_all = kv_all[:, :cols].reshape(all_rows, heads_here, head_width)
        value_all = kv_all[:, cols:].reshape(all_rows, heads_here, head_width)

    rel_z = lax.iota(jnp.int32, z_size)
    rel_y = lax.iota(jnp.int32, y_size)
    abs_z = (z_index + rel_z) % z_size
    abs_y = (y_index + rel_y) % y_size
    qg_source = (abs_z[None, :] * y_size + abs_y[:, None]).reshape(shards)
    key_positions = block_positions(offsets, all_rows)
    seq_index = z_index * y_size + y_index
    own_positions = offsets[seq_index] * PIECE + lax.iota(jnp.int32, row_count)

    query_heads = queries.reshape(row_count, heads_here, head_width)
    grad_heads = head_grads.reshape(row_count, heads_here, head_width)
    key_heads = keys.reshape(row_count, heads_here, head_width)
    value_heads = values.reshape(row_count, heads_here, head_width)

    with jax.named_scope("query_pass"):
        scores = jnp.einsum(
            "qhd,khd->hqk", query_heads, key_all, preferred_element_type=jnp.float32
        )
        visible = key_positions[None, None, :] <= own_positions[None, :, None]
        masked = jnp.where(visible, scores, masked_score)
        row_peak = jnp.max(masked, axis=2)
        summed = jnp.sum(jnp.where(visible, jnp.exp(masked - row_peak[:, :, None]), 0.0), axis=2)
        log_total = row_peak + jnp.log(summed)
        attend = jnp.exp(jnp.where(visible, scores - log_total[:, :, None], masked_score))
        grad_probs = jnp.einsum(
            "qhd,khd->hqk", grad_heads, value_all, preferred_element_type=jnp.float32
        )
        weighted = attend * grad_probs
        row_delta = jnp.sum(weighted, axis=2)
        first_sum = jnp.einsum(
            "hqk,khd->hqd",
            weighted.astype(jnp.bfloat16),
            key_all,
            preferred_element_type=jnp.float32,
        )
        second_sum = jnp.einsum(
            "hqk,khd->hqd", attend.astype(jnp.bfloat16), key_all, preferred_element_type=jnp.float32
        )
        query_grad = first_sum - row_delta[:, :, None] * second_sum
        query_grad = jnp.transpose(query_grad, (1, 0, 2)).reshape(row_count, cols)
        query_done = (query_grad * factor[None, :]).astype(jnp.bfloat16)

    with jax.named_scope("gather_row_stats"):
        stats = jnp.stack([log_total, row_delta], axis=0)
        stats, qg_ahead, qg_behind = lax.optimization_barrier((stats, qg_ahead, qg_behind))
        qg_pieces = ring4_last(qg_z, qg_ahead, qg_behind, "y")
        sent = jnp.broadcast_to(stats[None], (shards,) + stats.shape)
        stats_all = lax.all_to_all(sent, ("z", "y"), 0, 0, tiled=False)

    with jax.named_scope("key_pass"):
        piece_rows = qg_pieces[0].shape[0]
        stats_ordered = stats_all[qg_source]
        key_grad = jnp.zeros((row_count, heads_here, head_width), jnp.float32)
        value_grad = jnp.zeros((row_count, heads_here, head_width), jnp.float32)
        for ry, piece in enumerate(qg_pieces):
            source = qg_source[ry * z_size : (ry + 1) * z_size]
            query_part = piece[:, :cols].reshape(piece_rows, heads_here, head_width)
            grad_part = piece[:, cols:].reshape(piece_rows, heads_here, head_width)
            place = block_positions(offsets[source], piece_rows)
            part_stats = stats_ordered[ry * z_size : (ry + 1) * z_size]
            log_part = jnp.transpose(part_stats[:, 0], (1, 0, 2)).reshape(heads_here, piece_rows)
            delta_part = jnp.transpose(part_stats[:, 1], (1, 0, 2)).reshape(
                heads_here, piece_rows
            )
            scores_t = jnp.einsum(
                "khd,qhd->hkq", key_heads, query_part, preferred_element_type=jnp.float32
            )
            visible_t = own_positions[None, :, None] <= place[None, None, :]
            attend_t = jnp.exp(
                jnp.where(visible_t, scores_t - log_part[:, None, :], masked_score)
            )
            grad_probs_t = jnp.einsum(
                "khd,qhd->hkq", value_heads, grad_part, preferred_element_type=jnp.float32
            )
            score_grad = (attend_t * (grad_probs_t - delta_part[:, None, :])).astype(
                jnp.bfloat16
            )
            plain_t = attend_t.astype(jnp.bfloat16)
            score_grad, plain_t = lax.optimization_barrier((score_grad, plain_t))
            key_grad = key_grad + jnp.einsum(
                "hkq,qhd->khd", score_grad, query_part, preferred_element_type=jnp.float32
            )
            value_grad = value_grad + jnp.einsum(
                "hkq,qhd->khd",
                plain_t,
                grad_part,
                preferred_element_type=jnp.float32,
            )
        key_done = key_grad.reshape(row_count, cols).astype(jnp.bfloat16)
        value_done = value_grad.reshape(row_count, cols).astype(jnp.bfloat16)

    with jax.named_scope("back_projection"):
        back_sum = jnp.dot(query_done, w_query, preferred_element_type=jnp.float32)
        back_sum = back_sum + jnp.dot(key_done, w_key, preferred_element_type=jnp.float32)
        back_sum = back_sum + jnp.dot(value_done, w_value, preferred_element_type=jnp.float32)
        scaled = back_sum * norm_gain[None, :]
        row_part = jnp.sum(widened * scaled, axis=1)
        chunks = scaled.reshape(row_count, tp_size, width_here).transpose(1, 0, 2)
        extra = jnp.zeros((tp_size, 1, width_here), jnp.float32)
        extra = extra.at[:, 0, :row_count].set(jnp.broadcast_to(row_part, (tp_size, row_count)))
        payload = jnp.concatenate([chunks, extra], axis=1)
        received = lax.all_to_all(payload, "tp", 0, 0, tiled=False)
        total = jnp.sum(received, axis=0)
        scaled_own = total[:row_count]
        row_dot = total[row_count, :row_count][:, None]

    with jax.named_scope("input_grads"):
        start_col = lax.axis_index("tp") * width_here
        own_inputs = inputs.astype(jnp.float32)
        branch = (
            inverse * scaled_own
            - own_inputs * inverse * inverse * inverse * row_dot / full_width
        )
        result = out_grads.astype(jnp.float32) + branch
    return result.astype(jnp.bfloat16)


def solution(mesh):
    seq_size = mesh.shape["seq"]
    devices = mesh.devices
    y_size = 4 if seq_size % 4 == 0 else 1
    split = Mesh(
        devices.reshape((seq_size // y_size, y_size) + devices.shape[1:]),
        ("z", "y", "tp", "dp"),
    )
    rows = P(("dp", "z", "y"), "tp")
    return jax.shard_map(
        per_device,
        mesh=split,
        in_specs=(
            rows,
            rows,
            P(),
            P("tp", None),
            P("tp", None),
            P("tp", None),
            P("tp", None),
            P(),
            P(),
        ),
        out_specs=rows,
        check_vma=False,
    )
```

```python
import math

import jax
import jax.numpy as jnp
import numpy as np
from jax import lax
from jax.sharding import Mesh
from jax.sharding import PartitionSpec as P

PIECE = 128

scale_base = 1.4426950408889634
masked_score = -1e30
norm_eps = 1e-06


def column_scale(query_scale, head_count):
    head_width = query_scale.shape[0]
    factor = scale_base / math.sqrt(head_width) * jax.nn.softplus(query_scale)
    return jnp.tile(factor, head_count)


def block_positions(offsets, rows):
    return (offsets[:, None] * PIECE + lax.iota(jnp.int32, PIECE)[None, :]).reshape(rows)


def ring_steps(size):
    return size // 2, (size - 1) // 2


def shift(data, axis, size, step):
    return lax.ppermute(data, axis, [(i, (i + step) % size) for i in range(size)])


def ring_gather(data, axis, size):
    forward, backward = ring_steps(size)
    pieces = [None] * size
    pieces[0] = data
    ahead = behind = data
    for step in range(max(forward, backward)):
        if step < forward:
            ahead = shift(ahead, axis, size, 1)
            pieces[size - 1 - step] = ahead
        if step < backward:
            behind = shift(behind, axis, size, -1)
            pieces[1 + step] = behind
    return pieces


def ring4_first(data, axis):
    return shift(data, axis, 4, 1), shift(data, axis, 4, -1)


def ring4_last(data, ahead, behind, axis):
    far = shift(ahead, axis, 4, 1)
    return [data, behind, far, ahead]


def per_device(
    inputs, out_grads, norm_gain, w_query, w_key, w_value, w_output, query_scale, offsets
):
    row_count, width_here = inputs.shape
    head_width = query_scale.shape[0]
    heads_here = w_query.shape[0] // head_width
    cols = heads_here * head_width
    tp_size = lax.axis_size("tp")
    y_size = lax.axis_size("y")
    shards = offsets.shape[0]
    all_rows = shards * row_count
    contract = (((1,), (1,)), ((), ()))

    with jax.named_scope("gather_features"):
        both = jnp.concatenate([inputs, out_grads], axis=1)
        gathered = lax.all_gather(both, "tp", axis=1, tiled=True)
        gathered = gathered.reshape(row_count, tp_size, 2, width_here)
        full_inputs = gathered[:, :, 0, :].reshape(row_count, tp_size * width_here)
        full_grads = gathered[:, :, 1, :].reshape(row_count, tp_size * width_here)
    full_width = full_inputs.shape[1]

    with jax.named_scope("projections"):
        widened = full_inputs.astype(jnp.float32)
        inverse = lax.rsqrt(jnp.mean(widened * widened, axis=1, keepdims=True) + norm_eps)
        normed = (widened * inverse * norm_gain[None, :]).astype(jnp.bfloat16)
        factor = column_scale(query_scale, heads_here)
        queries = (
            lax.dot_general(normed, w_query, contract, preferred_element_type=jnp.float32)
            * factor[None, :]
        ).astype(jnp.bfloat16)
        keys = lax.dot_general(normed, w_key, contract, preferred_element_type=jnp.float32).astype(
            jnp.bfloat16
        )
        values = lax.dot_general(
            normed, w_value, contract, preferred_element_type=jnp.float32
        ).astype(jnp.bfloat16)
        head_grads = lax.dot_general(
            full_grads, w_output, contract, preferred_element_type=jnp.float32
        ).astype(jnp.bfloat16)

    z_size = lax.axis_size("z")
    z_index = lax.axis_index("z")
    y_index = lax.axis_index("y")

    with jax.named_scope("gather_sequence"):
        kv = jnp.concatenate([keys, values], axis=1)
        qg = jnp.concatenate([queries, head_grads], axis=1)
        kv_all = lax.all_gather(kv, "y", axis=0, tiled=True)
        kv_all = lax.all_gather(kv_all, "z", axis=0, tiled=True)
        qg_z = jnp.concatenate(ring_gather(qg, "z", z_size), axis=0)
        qg_ahead, qg_behind = ring4_first(qg_z, "y")
        key_all = kv_all[:, :cols].reshape(all_rows, heads_here, head_width)
        value_all = kv_all[:, cols:].reshape(all_rows, heads_here, head_width)

    rel_z = lax.iota(jnp.int32, z_size)
    rel_y = lax.iota(jnp.int32, y_size)
    abs_z = (z_index + rel_z) % z_size
    abs_y = (y_index + rel_y) % y_size
    qg_source = (abs_z[None, :] * y_size + abs_y[:, None]).reshape(shards)
    key_positions = block_positions(offsets, all_rows)
    seq_index = z_index * y_size + y_index
    own_positions = offsets[seq_index] * PIECE + lax.iota(jnp.int32, row_count)

    query_heads = queries.reshape(row_count, heads_here, head_width)
    grad_heads = head_grads.reshape(row_count, heads_here, head_width)
    key_heads = keys.reshape(row_count, heads_here, head_width)
    value_heads = values.reshape(row_count, heads_here, head_width)

    with jax.named_scope("query_pass"):
        scores = jnp.einsum(
            "qhd,khd->hqk", query_heads, key_all, preferred_element_type=jnp.float32
        )
        visible = key_positions[None, None, :] <= own_positions[None, :, None]
        masked = jnp.where(visible, scores, masked_score)
        row_peak = jnp.max(masked, axis=2)
        summed = jnp.sum(jnp.where(visible, jnp.exp(masked - row_peak[:, :, None]), 0.0), axis=2)
        log_total = row_peak + jnp.log(summed)
        attend = jnp.exp(jnp.where(visible, scores - log_total[:, :, None], masked_score))
        grad_probs = jnp.einsum(
            "qhd,khd->hqk", grad_heads, value_all, preferred_element_type=jnp.float32
        )
        weighted = attend * grad_probs
        row_delta = jnp.sum(weighted, axis=2)
        first_sum = jnp.einsum(
            "hqk,khd->hqd",
            weighted.astype(jnp.bfloat16),
            key_all,
            preferred_element_type=jnp.float32,
        )
        second_sum = jnp.einsum(
            "hqk,khd->hqd", attend.astype(jnp.bfloat16), key_all, preferred_element_type=jnp.float32
        )
        query_grad = first_sum - row_delta[:, :, None] * second_sum
        query_grad = jnp.transpose(query_grad, (1, 0, 2)).reshape(row_count, cols)
        query_done = (query_grad * factor[None, :]).astype(jnp.bfloat16)

    with jax.named_scope("gather_row_stats"):
        stats = jnp.stack([log_total, row_delta], axis=0)
        stats, qg_ahead, qg_behind = lax.optimization_barrier((stats, qg_ahead, qg_behind))
        qg_pieces = ring4_last(qg_z, qg_ahead, qg_behind, "y")
        sent = jnp.broadcast_to(stats[None], (shards,) + stats.shape)
        stats_all = lax.all_to_all(sent, ("z", "y"), 0, 0, tiled=False)

    with jax.named_scope("key_pass"):
        piece_rows = qg_pieces[0].shape[0]
        stats_ordered = stats_all[qg_source]
        key_grad = jnp.zeros((row_count, heads_here, head_width), jnp.float32)
        value_grad = jnp.zeros((row_count, heads_here, head_width), jnp.float32)
        for ry, piece in enumerate(qg_pieces):
            source = qg_source[ry * z_size : (ry + 1) * z_size]
            query_part = piece[:, :cols].reshape(piece_rows, heads_here, head_width)
            grad_part = piece[:, cols:].reshape(piece_rows, heads_here, head_width)
            place = block_positions(offsets[source], piece_rows)
            part_stats = stats_ordered[ry * z_size : (ry + 1) * z_size]
            log_part = jnp.transpose(part_stats[:, 0], (1, 0, 2)).reshape(heads_here, piece_rows)
            delta_part = jnp.transpose(part_stats[:, 1], (1, 0, 2)).reshape(
                heads_here, piece_rows
            )
            scores_t = jnp.einsum(
                "khd,qhd->hkq", key_heads, query_part, preferred_element_type=jnp.float32
            )
            visible_t = own_positions[None, :, None] <= place[None, None, :]
            attend_t = jnp.exp(
                jnp.where(visible_t, scores_t - log_part[:, None, :], masked_score)
            )
            grad_probs_t = jnp.einsum(
                "khd,qhd->hkq", value_heads, grad_part, preferred_element_type=jnp.float32
            )
            score_grad = (attend_t * (grad_probs_t - delta_part[:, None, :])).astype(
                jnp.bfloat16
            )
            plain_t = attend_t.astype(jnp.bfloat16)
            score_grad, plain_t = lax.optimization_barrier((score_grad, plain_t))
            key_grad = key_grad + jnp.einsum(
                "hkq,qhd->khd", score_grad, query_part, preferred_element_type=jnp.float32
            )
            value_grad = value_grad + jnp.einsum(
                "hkq,qhd->khd",
                plain_t,
                grad_part,
                preferred_element_type=jnp.float32,
            )
        key_done = key_grad.reshape(row_count, cols).astype(jnp.bfloat16)
        value_done = value_grad.reshape(row_count, cols).astype(jnp.bfloat16)

    with jax.named_scope("back_projection"):
        back_sum = jnp.dot(query_done, w_query, preferred_element_type=jnp.float32)
        back_sum = back_sum + jnp.dot(key_done, w_key, preferred_element_type=jnp.float32)
        back_sum = back_sum + jnp.dot(value_done, w_value, preferred_element_type=jnp.float32)
        scaled = back_sum * norm_gain[None, :]
        row_part = jnp.sum(widened * scaled, axis=1)
        chunks = scaled.reshape(row_count, tp_size, width_here).transpose(1, 0, 2)
        extra = jnp.zeros((tp_size, 1, width_here), jnp.float32)
        extra = extra.at[:, 0, :row_count].set(jnp.broadcast_to(row_part, (tp_size, row_count)))
        payload = jnp.concatenate([chunks, extra], axis=1)
        received = lax.all_to_all(payload, "tp", 0, 0, tiled=False)
        total = jnp.sum(received, axis=0)
        scaled_own = total[:row_count]
        row_dot = total[row_count, :row_count][:, None]

    with jax.named_scope("input_grads"):
        start_col = lax.axis_index("tp") * width_here
        own_inputs = inputs.astype(jnp.float32)
        branch = (
            inverse * scaled_own
            - own_inputs * inverse * inverse * inverse * row_dot / full_width
        )
        result = out_grads.astype(jnp.float32) + branch
    return result.astype(jnp.bfloat16)


def solution(mesh):
    seq_size = mesh.shape["seq"]
    devices = mesh.devices
    y_size = 4 if seq_size % 4 == 0 else 1
    split = Mesh(
        devices.reshape((seq_size // y_size, y_size) + devices.shape[1:]),
        ("z", "y", "tp", "dp"),
    )
    rows = P(("dp", "z", "y"), "tp")
    return jax.shard_map(
        per_device,
        mesh=split,
        in_specs=(
            rows,
            rows,
            P(),
            P("tp", None),
            P("tp", None),
            P("tp", None),
            P("tp", None),
            P(),
            P(),
        ),
        out_specs=rows,
        check_vma=False,
    )
```

```python
import math

import jax
import jax.numpy as jnp
import numpy as np
from jax import lax
from jax.sharding import Mesh
from jax.sharding import PartitionSpec as P

PIECE = 128

scale_base = 1.4426950408889634
masked_score = -1e30
norm_eps = 1e-06


def column_scale(query_scale, head_count):
    head_width = query_scale.shape[0]
    factor = scale_base / math.sqrt(head_width) * jax.nn.softplus(query_scale)
    return jnp.tile(factor, head_count)


def block_positions(offsets, rows):
    return (offsets[:, None] * PIECE + lax.iota(jnp.int32, PIECE)[None, :]).reshape(rows)


def ring_steps(size):
    return size // 2, (size - 1) // 2


def shift(data, axis, size, step):
    return lax.ppermute(data, axis, [(i, (i + step) % size) for i in range(size)])


def ring_gather(data, axis, size):
    forward, backward = ring_steps(size)
    pieces = [None] * size
    pieces[0] = data
    ahead = behind = data
    for step in range(max(forward, backward)):
        if step < forward:
            ahead = shift(ahead, axis, size, 1)
            pieces[size - 1 - step] = ahead
        if step < backward:
            behind = shift(behind, axis, size, -1)
            pieces[1 + step] = behind
    return pieces


def ring4_first(data, axis):
    return shift(data, axis, 4, 1), shift(data, axis, 4, -1)


def ring4_last(data, ahead, behind, axis):
    half = data.shape[0] // 2
    far = jnp.concatenate(
        [shift(ahead[:half], axis, 4, 1), shift(behind[half:], axis, 4, -1)], axis=0
    )
    return [data, behind, far, ahead]


def per_device(
    inputs, out_grads, norm_gain, w_query, w_key, w_value, w_output, query_scale, offsets
):
    row_count, width_here = inputs.shape
    head_width = query_scale.shape[0]
    heads_here = w_query.shape[0] // head_width
    cols = heads_here * head_width
    tp_size = lax.axis_size("tp")
    y_size = lax.axis_size("y")
    shards = offsets.shape[0]
    all_rows = shards * row_count
    contract = (((1,), (1,)), ((), ()))

    with jax.named_scope("gather_features"):
        both = jnp.concatenate([inputs, out_grads], axis=1)
        gathered = lax.all_gather(both, "tp", axis=1, tiled=True)
        gathered = gathered.reshape(row_count, tp_size, 2, width_here)
        full_inputs = gathered[:, :, 0, :].reshape(row_count, tp_size * width_here)
        full_grads = gathered[:, :, 1, :].reshape(row_count, tp_size * width_here)
    full_width = full_inputs.shape[1]

    with jax.named_scope("projections"):
        widened = full_inputs.astype(jnp.float32)
        inverse = lax.rsqrt(jnp.mean(widened * widened, axis=1, keepdims=True) + norm_eps)
        normed = (widened * inverse * norm_gain[None, :]).astype(jnp.bfloat16)
        factor = column_scale(query_scale, heads_here)
        queries = (
            lax.dot_general(normed, w_query, contract, preferred_element_type=jnp.float32)
            * factor[None, :]
        ).astype(jnp.bfloat16)
        keys = lax.dot_general(normed, w_key, contract, preferred_element_type=jnp.float32).astype(
            jnp.bfloat16
        )
        values = lax.dot_general(
            normed, w_value, contract, preferred_element_type=jnp.float32
        ).astype(jnp.bfloat16)
        head_grads = lax.dot_general(
            full_grads, w_output, contract, preferred_element_type=jnp.float32
        ).astype(jnp.bfloat16)

    z_size = lax.axis_size("z")
    z_index = lax.axis_index("z")
    y_index = lax.axis_index("y")

    with jax.named_scope("gather_sequence"):
        kv = jnp.concatenate([keys, values], axis=1)
        qg = jnp.concatenate([queries, head_grads], axis=1)
        kv_all = lax.all_gather(kv, "y", axis=0, tiled=True)
        kv_all = lax.all_gather(kv_all, "z", axis=0, tiled=True)
        qg_z = jnp.concatenate(ring_gather(qg, "z", z_size), axis=0)
        qg_ahead, qg_behind = ring4_first(qg_z, "y")
        key_all = kv_all[:, :cols].reshape(all_rows, heads_here, head_width)
        value_all = kv_all[:, cols:].reshape(all_rows, heads_here, head_width)

    rel_z = lax.iota(jnp.int32, z_size)
    rel_y = lax.iota(jnp.int32, y_size)
    abs_z = (z_index + rel_z) % z_size
    abs_y = (y_index + rel_y) % y_size
    qg_source = (abs_z[None, :] * y_size + abs_y[:, None]).reshape(shards)
    key_positions = block_positions(offsets, all_rows)
    seq_index = z_index * y_size + y_index
    own_positions = offsets[seq_index] * PIECE + lax.iota(jnp.int32, row_count)

    query_heads = queries.reshape(row_count, heads_here, head_width)
    grad_heads = head_grads.reshape(row_count, heads_here, head_width)
    key_heads = keys.reshape(row_count, heads_here, head_width)
    value_heads = values.reshape(row_count, heads_here, head_width)

    with jax.named_scope("query_pass"):
        scores = jnp.einsum(
            "qhd,khd->hqk", query_heads, key_all, preferred_element_type=jnp.float32
        )
        visible = key_positions[None, None, :] <= own_positions[None, :, None]
        masked = jnp.where(visible, scores, masked_score)
        row_peak = jnp.max(masked, axis=2)
        summed = jnp.sum(jnp.where(visible, jnp.exp(masked - row_peak[:, :, None]), 0.0), axis=2)
        log_total = row_peak + jnp.log(summed)
        attend = jnp.exp(jnp.where(visible, scores - log_total[:, :, None], masked_score))
        grad_probs = jnp.einsum(
            "qhd,khd->hqk", grad_heads, value_all, preferred_element_type=jnp.float32
        )
        weighted = attend * grad_probs
        row_delta = jnp.sum(weighted, axis=2)
        first_sum = jnp.einsum(
            "hqk,khd->hqd",
            weighted.astype(jnp.bfloat16),
            key_all,
            preferred_element_type=jnp.float32,
        )
        second_sum = jnp.einsum(
            "hqk,khd->hqd", attend.astype(jnp.bfloat16), key_all, preferred_element_type=jnp.float32
        )
        query_grad = first_sum - row_delta[:, :, None] * second_sum
        query_grad = jnp.transpose(query_grad, (1, 0, 2)).reshape(row_count, cols)
        query_done = (query_grad * factor[None, :]).astype(jnp.bfloat16)

    with jax.named_scope("gather_row_stats"):
        stats = jnp.stack([log_total, row_delta], axis=0)
        stats, qg_ahead, qg_behind = lax.optimization_barrier((stats, qg_ahead, qg_behind))
        qg_pieces = ring4_last(qg_z, qg_ahead, qg_behind, "y")
        sent = jnp.broadcast_to(stats[None], (shards,) + stats.shape)
        stats_all = lax.all_to_all(sent, ("z", "y"), 0, 0, tiled=False)

    with jax.named_scope("key_pass"):
        piece_rows = qg_pieces[0].shape[0]
        stats_ordered = stats_all[qg_source]
        query_places = block_positions(offsets[qg_source], all_rows)
        key_grad = jnp.zeros((row_count, heads_here, head_width), jnp.float32)
        value_grad = jnp.zeros((row_count, heads_here, head_width), jnp.float32)
        for ry, piece in enumerate(qg_pieces):
            source = qg_source[ry * z_size : (ry + 1) * z_size]
            query_part = piece[:, :cols].reshape(piece_rows, heads_here, head_width)
            grad_part = piece[:, cols:].reshape(piece_rows, heads_here, head_width)
            place = query_places[ry * piece_rows : (ry + 1) * piece_rows]
            part_stats = stats_ordered[ry * z_size : (ry + 1) * z_size]
            log_part = jnp.transpose(part_stats[:, 0], (1, 0, 2)).reshape(heads_here, piece_rows)
            delta_part = jnp.transpose(part_stats[:, 1], (1, 0, 2)).reshape(
                heads_here, piece_rows
            )
            scores_t = jnp.einsum(
                "khd,qhd->hkq", key_heads, query_part, preferred_element_type=jnp.float32
            )
            visible_t = own_positions[None, :, None] <= place[None, None, :]
            attend_t = jnp.exp(
                jnp.where(visible_t, scores_t - log_part[:, None, :], masked_score)
            )
            grad_probs_t = jnp.einsum(
                "khd,qhd->hkq", value_heads, grad_part, preferred_element_type=jnp.float32
            )
            score_grad = (attend_t * (grad_probs_t - delta_part[:, None, :])).astype(
                jnp.bfloat16
            )
            plain_t = attend_t.astype(jnp.bfloat16)
            score_grad, plain_t = lax.optimization_barrier((score_grad, plain_t))
            key_grad = key_grad + jnp.einsum(
                "hkq,qhd->khd", score_grad, query_part, preferred_element_type=jnp.float32
            )
            value_grad = value_grad + jnp.einsum(
                "hkq,qhd->khd",
                plain_t,
                grad_part,
                preferred_element_type=jnp.float32,
            )
        key_done = key_grad.reshape(row_count, cols).astype(jnp.bfloat16)
        value_done = value_grad.reshape(row_count, cols).astype(jnp.bfloat16)

    with jax.named_scope("back_projection"):
        back_sum = jnp.dot(query_done, w_query, preferred_element_type=jnp.float32)
        back_sum = back_sum + jnp.dot(key_done, w_key, preferred_element_type=jnp.float32)
        back_sum = back_sum + jnp.dot(value_done, w_value, preferred_element_type=jnp.float32)
        scaled = back_sum * norm_gain[None, :]
        row_part = jnp.sum(widened * scaled, axis=1)
        chunks = scaled.reshape(row_count, tp_size, width_here).transpose(1, 0, 2)
        extra = jnp.zeros((tp_size, 1, width_here), jnp.float32)
        extra = extra.at[:, 0, :row_count].set(jnp.broadcast_to(row_part, (tp_size, row_count)))
        payload = jnp.concatenate([chunks, extra], axis=1)
        received = lax.all_to_all(payload, "tp", 0, 0, tiled=False)
        total = jnp.sum(received, axis=0)
        scaled_own = total[:row_count]
        row_dot = total[row_count, :row_count][:, None]

    with jax.named_scope("input_grads"):
        start_col = lax.axis_index("tp") * width_here
        own_inputs = inputs.astype(jnp.float32)
        branch = (
            inverse * scaled_own
            - own_inputs * inverse * inverse * inverse * row_dot / full_width
        )
        result = out_grads.astype(jnp.float32) + branch
    return result.astype(jnp.bfloat16)


def solution(mesh):
    seq_size = mesh.shape["seq"]
    devices = mesh.devices
    y_size = 4 if seq_size % 4 == 0 else 1
    split = Mesh(
        devices.reshape((seq_size // y_size, y_size) + devices.shape[1:]),
        ("z", "y", "tp", "dp"),
    )
    rows = P(("dp", "z", "y"), "tp")
    return jax.shard_map(
        per_device,
        mesh=split,
        in_specs=(
            rows,
            rows,
            P(),
            P("tp", None),
            P("tp", None),
            P("tp", None),
            P("tp", None),
            P(),
            P(),
        ),
        out_specs=rows,
        check_vma=False,
    )
```

```python
import math

import jax
import jax.numpy as jnp
import numpy as np
from jax import lax
from jax.sharding import Mesh
from jax.sharding import PartitionSpec as P

PIECE = 128

scale_base = 1.4426950408889634
masked_score = -1e30
norm_eps = 1e-06


def column_scale(query_scale, head_count):
    head_width = query_scale.shape[0]
    factor = scale_base / math.sqrt(head_width) * jax.nn.softplus(query_scale)
    return jnp.tile(factor, head_count)


def block_positions(offsets, rows):
    return (offsets[:, None] * PIECE + lax.iota(jnp.int32, PIECE)[None, :]).reshape(rows)


def ring_steps(size):
    return size // 2, (size - 1) // 2


def shift(data, axis, size, step):
    return lax.ppermute(data, axis, [(i, (i + step) % size) for i in range(size)])


def ring_gather(data, axis, size):
    forward, backward = ring_steps(size)
    pieces = [None] * size
    pieces[0] = data
    ahead = behind = data
    for step in range(max(forward, backward)):
        if step < forward:
            ahead = shift(ahead, axis, size, 1)
            pieces[size - 1 - step] = ahead
        if step < backward:
            behind = shift(behind, axis, size, -1)
            pieces[1 + step] = behind
    return pieces


def ring4_first(data, axis):
    return shift(data, axis, 4, 1), shift(data, axis, 4, -1)


def ring4_last(data, ahead, behind, axis):
    half = data.shape[0] // 2
    far = jnp.concatenate(
        [shift(ahead[:half], axis, 4, 1), shift(behind[half:], axis, 4, -1)], axis=0
    )
    return [data, behind, far, ahead]


def per_device(
    inputs, out_grads, norm_gain, w_query, w_key, w_value, w_output, query_scale, offsets
):
    row_count, width_here = inputs.shape
    head_width = query_scale.shape[0]
    heads_here = w_query.shape[0] // head_width
    cols = heads_here * head_width
    tp_size = lax.axis_size("tp")
    y_size = lax.axis_size("y")
    shards = offsets.shape[0]
    all_rows = shards * row_count
    contract = (((1,), (1,)), ((), ()))

    with jax.named_scope("gather_features"):
        both = jnp.concatenate([inputs, out_grads], axis=1)
        gathered = lax.all_gather(both, "tp", axis=1, tiled=True)
        gathered = gathered.reshape(row_count, tp_size, 2, width_here)
        full_inputs = gathered[:, :, 0, :].reshape(row_count, tp_size * width_here)
        full_grads = gathered[:, :, 1, :].reshape(row_count, tp_size * width_here)
    full_width = full_inputs.shape[1]

    with jax.named_scope("projections"):
        widened = full_inputs.astype(jnp.float32)
        inverse = lax.rsqrt(jnp.mean(widened * widened, axis=1, keepdims=True) + norm_eps)
        normed = (widened * inverse * norm_gain[None, :]).astype(jnp.bfloat16)
        factor = column_scale(query_scale, heads_here)
        queries = (
            lax.dot_general(normed, w_query, contract, preferred_element_type=jnp.float32)
            * factor[None, :]
        ).astype(jnp.bfloat16)
        keys = lax.dot_general(normed, w_key, contract, preferred_element_type=jnp.float32).astype(
            jnp.bfloat16
        )
        values = lax.dot_general(
            normed, w_value, contract, preferred_element_type=jnp.float32
        ).astype(jnp.bfloat16)
        head_grads = lax.dot_general(
            full_grads, w_output, contract, preferred_element_type=jnp.float32
        ).astype(jnp.bfloat16)

    z_size = lax.axis_size("z")
    z_index = lax.axis_index("z")
    y_index = lax.axis_index("y")

    with jax.named_scope("gather_sequence"):
        kv = jnp.concatenate([keys, values], axis=1)
        qg = jnp.concatenate([queries, head_grads], axis=1)
        kv_all = lax.all_gather(kv, "y", axis=0, tiled=True)
        kv_all = lax.all_gather(kv_all, "z", axis=0, tiled=True)
        qg_z = jnp.concatenate(ring_gather(qg, "z", z_size), axis=0)
        qg_ahead, qg_behind = ring4_first(qg_z, "y")
        key_all = kv_all[:, :cols].reshape(all_rows, heads_here, head_width)
        value_all = kv_all[:, cols:].reshape(all_rows, heads_here, head_width)

    rel_z = lax.iota(jnp.int32, z_size)
    rel_y = lax.iota(jnp.int32, y_size)
    abs_z = (z_index + rel_z) % z_size
    abs_y = (y_index + rel_y) % y_size
    qg_source = (abs_z[None, :] * y_size + abs_y[:, None]).reshape(shards)
    key_positions = block_positions(offsets, all_rows)
    seq_index = z_index * y_size + y_index
    own_positions = offsets[seq_index] * PIECE + lax.iota(jnp.int32, row_count)

    query_heads = queries.reshape(row_count, heads_here, head_width)
    grad_heads = head_grads.reshape(row_count, heads_here, head_width)
    key_heads = keys.reshape(row_count, heads_here, head_width)
    value_heads = values.reshape(row_count, heads_here, head_width)

    with jax.named_scope("query_pass"):
        scores = jnp.einsum(
            "qhd,khd->hqk", query_heads, key_all, preferred_element_type=jnp.float32
        )
        visible = key_positions[None, None, :] <= own_positions[None, :, None]
        masked = jnp.where(visible, scores, masked_score)
        row_peak = jnp.max(masked, axis=2)
        summed = jnp.sum(jnp.where(visible, jnp.exp(masked - row_peak[:, :, None]), 0.0), axis=2)
        log_total = row_peak + jnp.log(summed)
        attend = jnp.exp(jnp.where(visible, scores - log_total[:, :, None], masked_score))
        grad_probs = jnp.einsum(
            "qhd,khd->hqk", grad_heads, value_all, preferred_element_type=jnp.float32
        )
        weighted = attend * grad_probs
        row_delta = jnp.sum(weighted, axis=2)
        first_sum = jnp.einsum(
            "hqk,khd->hqd",
            weighted.astype(jnp.bfloat16),
            key_all,
            preferred_element_type=jnp.float32,
        )
        second_sum = jnp.einsum(
            "hqk,khd->hqd", attend.astype(jnp.bfloat16), key_all, preferred_element_type=jnp.float32
        )
        query_grad = first_sum - row_delta[:, :, None] * second_sum
        query_grad = jnp.transpose(query_grad, (1, 0, 2)).reshape(row_count, cols)
        query_done = (query_grad * factor[None, :]).astype(jnp.bfloat16)

    with jax.named_scope("gather_row_stats"):
        stats = jnp.stack([log_total, row_delta], axis=0)
        stats, qg_ahead, qg_behind = lax.optimization_barrier((stats, qg_ahead, qg_behind))
        qg_pieces = ring4_last(qg_z, qg_ahead, qg_behind, "y")
        sent = jnp.broadcast_to(stats[None], (shards,) + stats.shape)
        stats_all = lax.all_to_all(sent, ("z", "y"), 0, 0, tiled=False)

    with jax.named_scope("key_pass"):
        piece_rows = qg_pieces[0].shape[0]
        stats_ordered = stats_all[qg_source]
        query_places = block_positions(offsets[qg_source], all_rows)
        stats_rows = jnp.transpose(stats_ordered, (1, 2, 0, 3)).reshape(2, heads_here, all_rows)
        key_grad = jnp.zeros((row_count, heads_here, head_width), jnp.float32)
        value_grad = jnp.zeros((row_count, heads_here, head_width), jnp.float32)
        for ry, piece in enumerate(qg_pieces):
            source = qg_source[ry * z_size : (ry + 1) * z_size]
            query_part = piece[:, :cols].reshape(piece_rows, heads_here, head_width)
            grad_part = piece[:, cols:].reshape(piece_rows, heads_here, head_width)
            place = query_places[ry * piece_rows : (ry + 1) * piece_rows]
            rows_here = slice(ry * piece_rows, (ry + 1) * piece_rows)
            log_part = stats_rows[0, :, rows_here]
            delta_part = stats_rows[1, :, rows_here]
            scores_t = jnp.einsum(
                "khd,qhd->hkq", key_heads, query_part, preferred_element_type=jnp.float32
            )
            visible_t = own_positions[None, :, None] <= place[None, None, :]
            attend_t = jnp.exp(
                jnp.where(visible_t, scores_t - log_part[:, None, :], masked_score)
            )
            grad_probs_t = jnp.einsum(
                "khd,qhd->hkq", value_heads, grad_part, preferred_element_type=jnp.float32
            )
            score_grad = (attend_t * (grad_probs_t - delta_part[:, None, :])).astype(
                jnp.bfloat16
            )
            plain_t = attend_t.astype(jnp.bfloat16)
            score_grad, plain_t = lax.optimization_barrier((score_grad, plain_t))
            key_grad = key_grad + jnp.einsum(
                "hkq,qhd->khd", score_grad, query_part, preferred_element_type=jnp.float32
            )
            value_grad = value_grad + jnp.einsum(
                "hkq,qhd->khd",
                plain_t,
                grad_part,
                preferred_element_type=jnp.float32,
            )
        key_done = key_grad.reshape(row_count, cols).astype(jnp.bfloat16)
        value_done = value_grad.reshape(row_count, cols).astype(jnp.bfloat16)

    with jax.named_scope("back_projection"):
        back_sum = jnp.dot(query_done, w_query, preferred_element_type=jnp.float32)
        back_sum = back_sum + jnp.dot(key_done, w_key, preferred_element_type=jnp.float32)
        back_sum = back_sum + jnp.dot(value_done, w_value, preferred_element_type=jnp.float32)
        scaled = back_sum * norm_gain[None, :]
        row_part = jnp.sum(widened * scaled, axis=1)
        chunks = scaled.reshape(row_count, tp_size, width_here).transpose(1, 0, 2)
        extra = jnp.zeros((tp_size, 1, width_here), jnp.float32)
        extra = extra.at[:, 0, :row_count].set(jnp.broadcast_to(row_part, (tp_size, row_count)))
        payload = jnp.concatenate([chunks, extra], axis=1)
        received = lax.all_to_all(payload, "tp", 0, 0, tiled=False)
        total = jnp.sum(received, axis=0)
        scaled_own = total[:row_count]
        row_dot = total[row_count, :row_count][:, None]

    with jax.named_scope("input_grads"):
        start_col = lax.axis_index("tp") * width_here
        own_inputs = inputs.astype(jnp.float32)
        branch = (
            inverse * scaled_own
            - own_inputs * inverse * inverse * inverse * row_dot / full_width
        )
        result = out_grads.astype(jnp.float32) + branch
    return result.astype(jnp.bfloat16)


def solution(mesh):
    seq_size = mesh.shape["seq"]
    devices = mesh.devices
    y_size = 4 if seq_size % 4 == 0 else 1
    split = Mesh(
        devices.reshape((seq_size // y_size, y_size) + devices.shape[1:]),
        ("z", "y", "tp", "dp"),
    )
    rows = P(("dp", "z", "y"), "tp")
    return jax.shard_map(
        per_device,
        mesh=split,
        in_specs=(
            rows,
            rows,
            P(),
            P("tp", None),
            P("tp", None),
            P("tp", None),
            P("tp", None),
            P(),
            P(),
        ),
        out_specs=rows,
        check_vma=False,
    )
```

```python
import math

import jax
import jax.numpy as jnp
import numpy as np
from jax import lax
from jax.sharding import Mesh
from jax.sharding import PartitionSpec as P

PIECE = 128

scale_base = 1.4426950408889634
masked_score = -1e30
norm_eps = 1e-06


def column_scale(query_scale, head_count):
    head_width = query_scale.shape[0]
    factor = scale_base / math.sqrt(head_width) * jax.nn.softplus(query_scale)
    return jnp.tile(factor, head_count)


def block_positions(offsets, rows):
    return (offsets[:, None] * PIECE + lax.iota(jnp.int32, PIECE)[None, :]).reshape(rows)


def ring_steps(size):
    return size // 2, (size - 1) // 2


def shift(data, axis, size, step):
    return lax.ppermute(data, axis, [(i, (i + step) % size) for i in range(size)])


def ring_gather(data, axis, size):
    forward, backward = ring_steps(size)
    pieces = [None] * size
    pieces[0] = data
    ahead = behind = data
    for step in range(max(forward, backward)):
        if step < forward:
            ahead = shift(ahead, axis, size, 1)
            pieces[size - 1 - step] = ahead
        if step < backward:
            behind = shift(behind, axis, size, -1)
            pieces[1 + step] = behind
    return pieces


def ring4_first(data, axis):
    return shift(data, axis, 4, 1), shift(data, axis, 4, -1)


def ring4_last(data, ahead, behind, axis):
    half = data.shape[0] // 2
    far = jnp.concatenate(
        [shift(ahead[:half], axis, 4, 1), shift(behind[half:], axis, 4, -1)], axis=0
    )
    return [data, behind, far, ahead]


def per_device(
    inputs, out_grads, norm_gain, w_query, w_key, w_value, w_output, query_scale, offsets
):
    row_count, width_here = inputs.shape
    head_width = query_scale.shape[0]
    heads_here = w_query.shape[0] // head_width
    cols = heads_here * head_width
    tp_size = lax.axis_size("tp")
    y_size = lax.axis_size("y")
    shards = offsets.shape[0]
    all_rows = shards * row_count
    contract = (((1,), (1,)), ((), ()))

    with jax.named_scope("gather_features"):
        both = jnp.concatenate([inputs, out_grads], axis=1)
        gathered = lax.all_gather(both, "tp", axis=1, tiled=True)
        gathered = gathered.reshape(row_count, tp_size, 2, width_here)
        full_inputs = gathered[:, :, 0, :].reshape(row_count, tp_size * width_here)
        full_grads = gathered[:, :, 1, :].reshape(row_count, tp_size * width_here)
    full_width = full_inputs.shape[1]

    with jax.named_scope("projections"):
        widened = full_inputs.astype(jnp.float32)
        inverse = lax.rsqrt(jnp.mean(widened * widened, axis=1, keepdims=True) + norm_eps)
        normed = (widened * inverse * norm_gain[None, :]).astype(jnp.bfloat16)
        factor = column_scale(query_scale, heads_here)
        queries = (
            lax.dot_general(normed, w_query, contract, preferred_element_type=jnp.float32)
            * factor[None, :]
        ).astype(jnp.bfloat16)
        keys = lax.dot_general(normed, w_key, contract, preferred_element_type=jnp.float32).astype(
            jnp.bfloat16
        )
        values = lax.dot_general(
            normed, w_value, contract, preferred_element_type=jnp.float32
        ).astype(jnp.bfloat16)
        head_grads = lax.dot_general(
            full_grads, w_output, contract, preferred_element_type=jnp.float32
        ).astype(jnp.bfloat16)

    z_size = lax.axis_size("z")
    z_index = lax.axis_index("z")
    y_index = lax.axis_index("y")

    with jax.named_scope("gather_sequence"):
        kv = jnp.concatenate([keys, values], axis=1)
        qg = jnp.concatenate([queries, head_grads], axis=1)
        kv_all = lax.all_gather(kv, "y", axis=0, tiled=True)
        kv_all = lax.all_gather(kv_all, "z", axis=0, tiled=True)
        qg_z = jnp.concatenate(ring_gather(qg, "z", z_size), axis=0)
        qg_ahead, qg_behind = ring4_first(qg_z, "y")
        key_all = kv_all[:, :cols].reshape(all_rows, heads_here, head_width)
        value_all = kv_all[:, cols:].reshape(all_rows, heads_here, head_width)

    rel_z = lax.iota(jnp.int32, z_size)
    rel_y = lax.iota(jnp.int32, y_size)
    abs_z = (z_index + rel_z) % z_size
    abs_y = (y_index + rel_y) % y_size
    qg_source = (abs_z[None, :] * y_size + abs_y[:, None]).reshape(shards)
    key_positions = block_positions(offsets, all_rows)
    seq_index = z_index * y_size + y_index
    own_positions = offsets[seq_index] * PIECE + lax.iota(jnp.int32, row_count)

    query_heads = queries.reshape(row_count, heads_here, head_width)
    grad_heads = head_grads.reshape(row_count, heads_here, head_width)
    key_heads = keys.reshape(row_count, heads_here, head_width)
    value_heads = values.reshape(row_count, heads_here, head_width)

    with jax.named_scope("query_pass"):
        scores = jnp.einsum(
            "qhd,khd->hqk", query_heads, key_all, preferred_element_type=jnp.float32
        )
        visible = key_positions[None, None, :] <= own_positions[None, :, None]
        masked = jnp.where(visible, scores, masked_score)
        row_peak = jnp.max(masked, axis=2)
        summed = jnp.sum(jnp.where(visible, jnp.exp(masked - row_peak[:, :, None]), 0.0), axis=2)
        log_total = row_peak + jnp.log(summed)
        attend = jnp.exp(jnp.where(visible, scores - log_total[:, :, None], masked_score))
        grad_probs = jnp.einsum(
            "qhd,khd->hqk", grad_heads, value_all, preferred_element_type=jnp.float32
        )
        weighted = attend * grad_probs
        row_delta = jnp.sum(weighted, axis=2)
        first_sum = jnp.einsum(
            "hqk,khd->hqd",
            weighted.astype(jnp.bfloat16),
            key_all,
            preferred_element_type=jnp.float32,
        )
        second_sum = jnp.einsum(
            "hqk,khd->hqd", attend.astype(jnp.bfloat16), key_all, preferred_element_type=jnp.float32
        )
        query_grad = first_sum - row_delta[:, :, None] * second_sum
        query_grad = jnp.transpose(query_grad, (1, 0, 2)).reshape(row_count, cols)
        query_done = (query_grad * factor[None, :]).astype(jnp.bfloat16)

    with jax.named_scope("gather_row_stats"):
        stats = jnp.stack([log_total, row_delta], axis=0)
        stats, qg_ahead, qg_behind = lax.optimization_barrier((stats, qg_ahead, qg_behind))
        qg_pieces = ring4_last(qg_z, qg_ahead, qg_behind, "y")
        sent = jnp.broadcast_to(stats[None], (shards,) + stats.shape)
        stats_all = lax.all_to_all(sent, ("z", "y"), 0, 0, tiled=False)

    with jax.named_scope("key_pass"):
        piece_rows = qg_pieces[0].shape[0]
        stats_ordered = stats_all[qg_source]
        query_places = block_positions(offsets[qg_source], all_rows)
        key_grad = jnp.zeros((row_count, heads_here, head_width), jnp.float32)
        value_grad = jnp.zeros((row_count, heads_here, head_width), jnp.float32)
        for ry in (0, 1, 3, 2):
            piece = qg_pieces[ry]
            source = qg_source[ry * z_size : (ry + 1) * z_size]
            query_part = piece[:, :cols].reshape(piece_rows, heads_here, head_width)
            grad_part = piece[:, cols:].reshape(piece_rows, heads_here, head_width)
            place = query_places[ry * piece_rows : (ry + 1) * piece_rows]
            part_stats = stats_ordered[ry * z_size : (ry + 1) * z_size]
            log_part = jnp.transpose(part_stats[:, 0], (1, 0, 2)).reshape(heads_here, piece_rows)
            delta_part = jnp.transpose(part_stats[:, 1], (1, 0, 2)).reshape(
                heads_here, piece_rows
            )
            scores_t = jnp.einsum(
                "khd,qhd->hkq", key_heads, query_part, preferred_element_type=jnp.float32
            )
            visible_t = own_positions[None, :, None] <= place[None, None, :]
            attend_t = jnp.exp(
                jnp.where(visible_t, scores_t - log_part[:, None, :], masked_score)
            )
            grad_probs_t = jnp.einsum(
                "khd,qhd->hkq", value_heads, grad_part, preferred_element_type=jnp.float32
            )
            score_grad = (attend_t * (grad_probs_t - delta_part[:, None, :])).astype(
                jnp.bfloat16
            )
            plain_t = attend_t.astype(jnp.bfloat16)
            score_grad, plain_t = lax.optimization_barrier((score_grad, plain_t))
            key_grad = key_grad + jnp.einsum(
                "hkq,qhd->khd", score_grad, query_part, preferred_element_type=jnp.float32
            )
            value_grad = value_grad + jnp.einsum(
                "hkq,qhd->khd",
                plain_t,
                grad_part,
                preferred_element_type=jnp.float32,
            )
        key_done = key_grad.reshape(row_count, cols).astype(jnp.bfloat16)
        value_done = value_grad.reshape(row_count, cols).astype(jnp.bfloat16)

    with jax.named_scope("back_projection"):
        back_sum = jnp.dot(query_done, w_query, preferred_element_type=jnp.float32)
        back_sum = back_sum + jnp.dot(key_done, w_key, preferred_element_type=jnp.float32)
        back_sum = back_sum + jnp.dot(value_done, w_value, preferred_element_type=jnp.float32)
        scaled = back_sum * norm_gain[None, :]
        row_part = jnp.sum(widened * scaled, axis=1)
        chunks = scaled.reshape(row_count, tp_size, width_here).transpose(1, 0, 2)
        extra = jnp.zeros((tp_size, 1, width_here), jnp.float32)
        extra = extra.at[:, 0, :row_count].set(jnp.broadcast_to(row_part, (tp_size, row_count)))
        payload = jnp.concatenate([chunks, extra], axis=1)
        received = lax.all_to_all(payload, "tp", 0, 0, tiled=False)
        total = jnp.sum(received, axis=0)
        scaled_own = total[:row_count]
        row_dot = total[row_count, :row_count][:, None]

    with jax.named_scope("input_grads"):
        start_col = lax.axis_index("tp") * width_here
        own_inputs = inputs.astype(jnp.float32)
        branch = (
            inverse * scaled_own
            - own_inputs * inverse * inverse * inverse * row_dot / full_width
        )
        result = out_grads.astype(jnp.float32) + branch
    return result.astype(jnp.bfloat16)


def solution(mesh):
    seq_size = mesh.shape["seq"]
    devices = mesh.devices
    y_size = 4 if seq_size % 4 == 0 else 1
    split = Mesh(
        devices.reshape((seq_size // y_size, y_size) + devices.shape[1:]),
        ("z", "y", "tp", "dp"),
    )
    rows = P(("dp", "z", "y"), "tp")
    return jax.shard_map(
        per_device,
        mesh=split,
        in_specs=(
            rows,
            rows,
            P(),
            P("tp", None),
            P("tp", None),
            P("tp", None),
            P("tp", None),
            P(),
            P(),
        ),
        out_specs=rows,
        check_vma=False,
    )
```
